32 devices in a mesh: grp: 2 (over y), wide: 4 (over z), col: 2 (over x), inc: 2 (over core).
Axes of the slice: x: 2, y: 2, z: 4, core: 2. Of those that a mesh axis runs over, the one named last changes fastest.
Arguments:
- values_in: bfloat16 [32, 64, 256, 512], P(('grp', 'col'), 'inc', 'wide'), parts along dimension 0, may hold values from -6 to 6
- shock_load: float32 [32], P(('grp', 'col')), parts along dimension 0, may hold values from -4 to 4
- price_field: float32 [128, 256, 512], P(('grp', 'inc'), 'wide'), parts along dimension 0, may hold values from -6 to 6
- rate_liquid: float32 [128, 256, 512], P(('grp', 'inc'), 'wide'), parts along dimension 0, may hold values from 0.05 to 0.5
- rate_illiquid: float32 [128, 256, 512], P(('grp', 'inc'), 'wide'), parts along dimension 0, may hold values from 0.05 to 0.5
- mask_liquid: int32 [128, 256, 512], P(('grp', 'inc'), 'wide'), parts along dimension 0, may hold values 0 or 1
- mask_illiquid: int32 [128, 256, 512], P(('grp', 'inc'), 'wide'), parts along dimension 0, may hold values 0 or 1
- jump_inverse: float32 [128, 64], P('grp'), parts along dimension 0, may hold values from -0.07 to 0.87
- coef_liquid: int32 [4096], replicated, may hold values from 0 to 127, as said below
- coef_illiquid: int32 [4096], replicated, may hold values from 0 to 255
- coef_income: int32 [4096], replicated, may hold values from 0 to 63
- owner: int32 [4096], replicated, may hold values from 0 to 7, as said below
Outputs:
- reduced: float32 [32, 8192], P(('grp', 'col'), ('wide', 'inc')), parts along dimension 0
The draws below stay inside these ranges and needn't reach their ends.
There are 2 independent parts, one for each index of `grp`. The reference program is written for one: setup_inputs(seed, part) draws one part's arguments, and reference() takes and returns one part's arrays. A program takes and returns all parts, laid end to end along the dimension named above; an argument that names none is the same for every part. Nothing has to cross between parts.
Inputs may be any that keep to these rules, and one draw needn't show every extreme that they name: `coef_liquid`: every retained coefficient has liquid frequency below 128. No owner has more than 1024 rows, and some owner has exactly 1024.
All inputs are finite; a program needn't handle non-finite values. No bound on the sum of `mask_liquid` or of `mask_illiquid` on one device may be relied on, other than what follows from the above.
Results may differ from the reference program's by a relative error of at most 0.0003.
Values may be sent and summed in bfloat16 or wider, within the bound.
No kernel may reach another device: no remote copies, remote signals or barrier semaphores. Data moves between devices by JAX's collectives and lax.ppermute only.
A program may use at most 256 MiB of HBM per device.

```python
import math
import jax
import jax.numpy as jnp
from jax import lax

NB = 512
NA = 256
NZ = 64
KBLOW = 128
K = 4096
COLS = 16
NOWN = 8
CAP = 1024
N_WIDE = 4
N_INC = 2


def draw_jump_inverse(key, part):
    eye = (jnp.arange(NZ)[:, None] == jnp.arange(NZ)[None, :]).astype(jnp.float32)
    half = 0.065
    noise = jax.random.uniform(key, (NZ, NZ), jnp.float32, -half, half)
    return 0.8 * eye + noise


def bounded_list(key, upper):
    picks = jax.random.randint(key, (K,), 0, upper)
    return picks.at[0].set(upper - 1).at[1].set(0)


def draw_coef_liquid(key, part):
    return bounded_list(jax.random.fold_in(key, 11), KBLOW)


def draw_coef_illiquid(key, part):
    return bounded_list(jax.random.fold_in(key, 12), NA)


def draw_coef_income(key, part):
    return bounded_list(jax.random.fold_in(key, 13), NZ)


def draw_owner(key, part):
    order = jax.random.permutation(jax.random.fold_in(key, 21), K)
    busy = jax.random.randint(jax.random.fold_in(key, 22), (), 0, NOWN)
    spread = (order - CAP) % (NOWN - 1)
    return jnp.where(order < CAP, busy, (busy + 1 + spread) % NOWN).astype(jnp.int32)


def place_ends(array, rng, smallest, high):
    shape = array.shape
    place = [jax.random.randint(jax.random.fold_in(rng, axis), (), 0, shape[axis]) for axis in range(len(shape))]
    array = array.at[tuple(place)].set(smallest)
    longest = shape.index(max(shape))
    place[longest] = (place[longest] + 1) % shape[longest]
    return array.at[tuple(place)].set(high)


def block_levels(own_key, dims, cuts, least, top_value):
    factor_of = 1.0
    for dim, blocks in cuts:
        heights = jax.random.uniform(jax.random.fold_in(jax.random.fold_in(own_key, 6), dim), (blocks,), jnp.float32, least / len(cuts), top_value / len(cuts))
        factor_of = factor_of * jnp.repeat(jnp.exp(heights), dims[dim] // blocks).reshape((-1,) + (1,) * (len(dims) - 1 - dim))
    return factor_of


def centred(own_key, dims, width, bound, split=(), held_as=jnp.bfloat16):
    result = jax.random.normal(own_key, dims, jnp.float32) * width
    if len(split) > 0:
        result = block_levels(own_key, dims, split, -0.22, 0.18) * result
    return jnp.clip(result, min=-bound, max=bound).astype(held_as)


def setup_inputs(seed: int = 0, part: int = 0) -> dict:
    keys = jax.random.split(jax.random.key(seed), 13)
    own_keys = jax.random.split(jax.random.fold_in(keys[12], part), 13)
    return {
        "values_in": centred(own_keys[0], (COLS, NZ, NA, NB), 1.0, 6.0, ((0, 2), (1, 2), (2, 4))),
        "shock_load": centred(own_keys[1], (COLS,), 1.0, 4.0, ((0, 2),), jnp.float32),
        "price_field": centred(own_keys[2], (NZ, NA, NB), 1.0, 6.0, ((0, 2), (1, 4)), jnp.float32),
        "rate_liquid": jnp.clip(jnp.exp(math.log(0.5) - 2.3025851 * jax.random.uniform(own_keys[3], (NZ, NA, NB), jnp.float32) ** block_levels(own_keys[3], (NZ, NA, NB), ((0, 2), (1, 4)), -0.2, 0.2)), 0.05, 0.5),
        "rate_illiquid": jnp.clip(jnp.exp(math.log(0.5) - 2.3025851 * jax.random.uniform(own_keys[4], (NZ, NA, NB), jnp.float32) ** block_levels(own_keys[4], (NZ, NA, NB), ((0, 2), (1, 4)), -0.2, 0.2)), 0.05, 0.5),
        "mask_liquid": place_ends((jax.random.randint(own_keys[5], (NZ, NA, NB), 0, 2) < 1).astype(jnp.int32), jax.random.fold_in(own_keys[5], 1), 0, 1),
        "mask_illiquid": place_ends((jax.random.randint(own_keys[6], (NZ, NA, NB), 0, 2) < 1).astype(jnp.int32), jax.random.fold_in(own_keys[6], 1), 0, 1),
        "jump_inverse": draw_jump_inverse(jax.random.fold_in(jax.random.fold_in(keys[12], part), 71), part),
        "coef_liquid": draw_coef_liquid(jax.random.fold_in(keys[12], 71), part),
        "coef_illiquid": draw_coef_illiquid(jax.random.fold_in(keys[12], 71), part),
        "coef_income": draw_coef_income(jax.random.fold_in(keys[12], 71), part),
        "owner": draw_owner(jax.random.fold_in(keys[12], 71), part),
    }


def cosine_table(count):
    freq = jnp.arange(count, dtype=jnp.int32)[:, None]
    cell = jnp.arange(count, dtype=jnp.int32)[None, :]
    phase = (2 * cell + 1) * freq % (4 * count)
    angle = jnp.pi * phase.astype(jnp.float32) / (2.0 * count)
    first = jnp.where(freq == 0, jnp.sqrt(jnp.float32(0.5)), jnp.float32(1.0))
    return jnp.cos(angle) * jnp.sqrt(jnp.float32(2.0 / count)) * first

def slot_targets(owner, owners, capacity):
    onehot = (owner[:, None] == jnp.arange(owners, dtype=jnp.int32)[None, :]).astype(jnp.int32)
    before = jnp.cumsum(onehot, axis=0) - onehot
    slot = lax.optimization_barrier(jnp.sum(before * onehot, axis=1))
    return (owner * capacity + slot).astype(jnp.int32)

def differences(field, axis):
    step = jnp.diff(field, axis=axis)
    shape = list(field.shape)
    shape[axis] = 1
    zero = jnp.zeros(shape, field.dtype)
    return (jnp.concatenate([step, zero], axis=axis), jnp.concatenate([zero, step], axis=axis))

def reference(values_in, shock_load, price_field, rate_liquid, rate_illiquid, mask_liquid, mask_illiquid, jump_inverse, coef_liquid, coef_illiquid, coef_income, owner):
    high = lax.Precision.HIGHEST
    table_b = cosine_table(NB)[:KBLOW]
    table_a = cosine_table(NA)
    table_z = cosine_table(NZ)
    mask_b = mask_liquid.astype(jnp.float32)
    mask_a = mask_illiquid.astype(jnp.float32)
    owners = N_WIDE * N_INC
    capacity = 2 * K // owners
    targets = slot_targets(owner, owners, capacity)

    def one_column(pair):
        field, load = pair
        v = field.astype(jnp.float32)
        fwd_b, bwd_b = differences(v, 2)
        fwd_a, bwd_a = differences(v, 1)
        explicit = v + rate_liquid * (mask_b * fwd_b - (1.0 - mask_b) * bwd_b) + rate_illiquid * (mask_a * fwd_a - (1.0 - mask_a) * bwd_a) + load * price_field
        updated = jnp.einsum('yz,zab->yab', jump_inverse, explicit, precision=high)
        segment_b = jnp.einsum('zab,kb->zak', updated, table_b, precision=high)
        segment_a = jnp.einsum('zak,ja->zjk', segment_b, table_a, precision=high)
        spectrum = jnp.einsum('zjk,yz->yjk', segment_a, table_z, precision=high)
        return spectrum[coef_income, coef_illiquid, coef_liquid]
    kept = lax.map(one_column, (values_in, shock_load))
    reduced = jnp.zeros((kept.shape[0], owners * capacity), jnp.float32)
    return reduced.at[:, targets].set(kept)
```

```python
import jax
import jax.numpy as jnp
from jax import lax
from jax.sharding import PartitionSpec as P

NB = 512
NA = 256
NZ = 64
KBLOW = 128


def padded_2(cells, sides, width):
    for axis, dim in sides:
        count = lax.axis_size(axis)
        ends = count - 1
        head = lax.slice_in_dim(cells, 0, width, axis=dim)
        tail = lax.slice_in_dim(cells, cells.shape[dim] - width, cells.shape[dim], axis=dim)
        cells = jnp.concatenate(
            [
                lax.ppermute(tail, axis, [(i, (i + 1) % count) for i in range(ends)]),
                cells,
                lax.ppermute(head, axis, [((i + 1) % count, i) for i in range(ends)]),
            ],
            axis=dim,
        )
    return cells


def cosine_table(count):
    freq = jnp.arange(count, dtype=jnp.int32)[:, None]
    cell = jnp.arange(count, dtype=jnp.int32)[None, :]
    phase = (2 * cell + 1) * freq % (4 * count)
    angle = jnp.pi * phase.astype(jnp.float32) / (2.0 * count)
    first = jnp.where(freq == 0, jnp.sqrt(jnp.float32(0.5)), jnp.float32(1.0))
    return jnp.cos(angle) * jnp.sqrt(jnp.float32(2.0 / count)) * first


def slot_targets(owner, owners, capacity):
    onehot = (owner[:, None] == jnp.arange(owners, dtype=jnp.int32)[None, :]).astype(jnp.int32)
    before = jnp.cumsum(onehot, axis=0) - onehot
    slot = jnp.sum(before * onehot, axis=1)
    return owner * capacity + slot


def body(
    values_in,
    shock_load,
    price_field,
    rate_liquid,
    rate_illiquid,
    mask_liquid,
    mask_illiquid,
    jump_inverse,
    coef_liquid,
    coef_illiquid,
    coef_income,
    owner,
):
    high = lax.Precision.HIGH
    columns, nz_loc, na_loc, _ = values_in.shape
    wide_pos = lax.axis_index("wide")
    inc_pos = lax.axis_index("inc")
    wide_count = lax.axis_size("wide")
    padded = padded_2(values_in, (("wide", 2),), 1).astype(jnp.float32)
    center = padded[:, :, 1:-1]
    lower = jnp.where(wide_pos == 0, center[:, :, 0:1], padded[:, :, 0:1])
    upper = jnp.where(wide_pos == wide_count - 1, center[:, :, -1:], padded[:, :, -1:])
    fwd_a = jnp.concatenate([center[:, :, 1:], upper], axis=2) - center
    bwd_a = center - jnp.concatenate([lower, center[:, :, :-1]], axis=2)
    step_b = center[:, :, :, 1:] - center[:, :, :, :-1]
    zero_b = jnp.zeros(center.shape[:3] + (1,), jnp.float32)
    fwd_b = jnp.concatenate([step_b, zero_b], axis=3)
    bwd_b = jnp.concatenate([zero_b, step_b], axis=3)
    mask_b = mask_liquid.astype(jnp.float32)
    mask_a = mask_illiquid.astype(jnp.float32)
    load = shock_load[:, None, None, None]
    explicit = (
        center
        + rate_liquid * (mask_b * fwd_b - (1.0 - mask_b) * bwd_b)
        + rate_illiquid * (mask_a * fwd_a - (1.0 - mask_a) * bwd_a)
        + load * price_field
    )
    table_b = cosine_table(NB)[:KBLOW]
    liquid_part = jnp.einsum("kb,czab->czak", table_b, explicit, precision=high)
    table_a = lax.dynamic_slice_in_dim(cosine_table(NA), wide_pos * na_loc, na_loc, axis=1)
    illiquid_part = jnp.einsum("ja,czak->jkcz", table_a, liquid_part, precision=high)
    rows = illiquid_part.reshape(NA * KBLOW, columns * nz_loc)
    picked = jnp.take(rows, coef_illiquid * KBLOW + coef_liquid, axis=0)
    folded = jnp.dot(cosine_table(NZ), jump_inverse, precision=lax.Precision.HIGHEST)
    folded = lax.dynamic_slice_in_dim(folded, inc_pos * nz_loc, nz_loc, axis=1)
    weight = jnp.take(folded, coef_income, axis=0)
    partial = jnp.sum(picked.reshape(-1, columns, nz_loc) * weight[:, None, :], axis=2)
    kept = lax.psum(partial, ("wide", "inc"))
    owners = lax.axis_size(("wide", "inc"))
    count = owner.shape[0]
    capacity = 2 * count // owners
    targets = slot_targets(owner, owners, capacity)
    source = jnp.full((owners * capacity,), count, jnp.int32).at[targets].set(jnp.arange(count, dtype=jnp.int32))
    mine = lax.dynamic_slice_in_dim(source, lax.axis_index(("wide", "inc")) * capacity, capacity)
    gathered = jnp.take(kept, jnp.minimum(mine, count - 1), axis=0)
    return jnp.where((mine < count)[None, :], gathered.T, jnp.float32(0.0))


def solution(mesh):
    placed = (
        P(("grp", "col"), "inc", "wide", None),
        P(("grp", "col")),
        P(("grp", "inc"), "wide", None),
        P(("grp", "inc"), "wide", None),
        P(("grp", "inc"), "wide", None),
        P(("grp", "inc"), "wide", None),
        P(("grp", "inc"), "wide", None),
        P("grp", None),
        P(),
        P(),
        P(),
        P(),
    )
    return jax.shard_map(
        body,
        mesh=mesh,
        in_specs=placed,
        out_specs=P(("grp", "col"), ("wide", "inc")),
        check_vma=False,
    )
```

```python
import functools
import jax
import jax.numpy as jnp
from jax import lax
from jax.experimental import pallas as pl
from jax.experimental.pallas import tpu as pltpu
from jax.sharding import PartitionSpec as P

NB = 512
NA = 256
NZ = 64
KBLOW = 128
Z_BLOCK = 8


def cosine_table(count):
    freq = jnp.arange(count, dtype=jnp.int32)[:, None]
    cell = jnp.arange(count, dtype=jnp.int32)[None, :]
    phase = (2 * cell + 1) * freq % (4 * count)
    angle = jnp.pi * phase.astype(jnp.float32) / (2.0 * count)
    first = jnp.where(freq == 0, jnp.sqrt(jnp.float32(0.5)), jnp.float32(1.0))
    return jnp.cos(angle) * jnp.sqrt(jnp.float32(2.0 / count)) * first


def slot_targets(owner, owners, capacity):
    onehot = (owner[:, None] == jnp.arange(owners, dtype=jnp.int32)[None, :]).astype(jnp.int32)
    before = jnp.cumsum(onehot, axis=0) - onehot
    slot = jnp.sum(before * onehot, axis=1)
    return owner * capacity + slot


def split_bf16(x):
    hi = x.astype(jnp.bfloat16)
    return hi, (x - hi.astype(jnp.float32)).astype(jnp.bfloat16)


def step_kernel(load_ref, vals_ref, lo_ref, up_ref, rl_ref, ri_ref, pf_ref, ml_ref, mi_ref, tb_ref, out_ref):
    columns = vals_ref.shape[0]
    zb, na, nb = rl_ref.shape
    kb = tb_ref.shape[1]
    rows = zb * na
    rl = rl_ref[...].reshape(rows, nb)
    ri = ri_ref[...].reshape(rows, nb)
    pf = pf_ref[...].reshape(rows, nb)
    mb = ml_ref[...].reshape(rows, nb) != 0
    ma = mi_ref[...].reshape(rows, nb) != 0
    col = lax.broadcasted_iota(jnp.int32, (rows, nb), 1)
    arow = lax.broadcasted_iota(jnp.int32, (zb, na, nb), 1).reshape(rows, nb)
    th, tl = split_bf16(tb_ref[...])

    def per_column(c, carry):
        v = vals_ref[c].reshape(rows, nb).astype(jnp.float32)
        lo = jnp.broadcast_to(lo_ref[c][:, None, :], (zb, na, nb)).reshape(rows, nb)
        up = jnp.broadcast_to(up_ref[c][:, None, :], (zb, na, nb)).reshape(rows, nb)
        fwd_b = jnp.where(col == nb - 1, 0.0, pltpu.roll(v, nb - 1, 1) - v)
        bwd_b = jnp.where(col == 0, 0.0, v - pltpu.roll(v, 1, 1))
        fwd_a = jnp.where(arow == na - 1, up, pltpu.roll(v, rows - 1, 0)) - v
        bwd_a = v - jnp.where(arow == 0, lo, pltpu.roll(v, 1, 0))
        sel_b = jnp.where(mb, fwd_b, -bwd_b)
        sel_a = jnp.where(ma, fwd_a, -bwd_a)
        explicit = v + rl * sel_b + ri * sel_a + load_ref[c] * pf
        hi, low = split_bf16(explicit)
        acc = jnp.dot(low, th, preferred_element_type=jnp.float32)
        acc = acc + jnp.dot(hi, tl, preferred_element_type=jnp.float32)
        acc = acc + jnp.dot(hi, th, preferred_element_type=jnp.float32)
        out_ref[c] = acc.reshape(zb, na, kb)
        return carry

    lax.fori_loop(0, columns, per_column, 0)


def liquid_step(load, vals, lower, upper, rl, ri, pf, ml, mi, tb):
    columns, nz, na, nb = vals.shape
    kb = tb.shape[1]
    zb = min(Z_BLOCK, nz)
    field = pl.BlockSpec((zb, na, nb), lambda j: (j, 0, 0))
    edge = pl.BlockSpec((columns, zb, nb), lambda j: (0, j, 0))
    table = pl.BlockSpec((nb, kb), lambda j: (0, 0))
    return pl.pallas_call(
        step_kernel,
        grid=(nz // zb,),
        in_specs=[
            pl.BlockSpec(memory_space=pltpu.SMEM),
            pl.BlockSpec((columns, zb, na, nb), lambda j: (0, j, 0, 0)),
            edge,
            edge,
            field,
            field,
            field,
            field,
            field,
            table,
        ],
        out_specs=pl.BlockSpec((columns, zb, na, kb), lambda j: (0, j, 0, 0)),
        out_shape=jax.ShapeDtypeStruct((columns, nz, na, kb), jnp.float32),
        compiler_params=pltpu.CompilerParams(vmem_limit_bytes=56 * 1024 * 1024),
    )(load, vals, lower, upper, rl, ri, pf, ml, mi, tb)


def edges(values, axis, dim):
    count = lax.axis_size(axis)
    pos = lax.axis_index(axis)
    ends = count - 1
    head = lax.index_in_dim(values, 0, axis=dim, keepdims=False)
    tail = lax.index_in_dim(values, values.shape[dim] - 1, axis=dim, keepdims=False)
    below = lax.ppermute(tail, axis, [(i, (i + 1) % count) for i in range(ends)])
    above = lax.ppermute(head, axis, [((i + 1) % count, i) for i in range(ends)])
    lower = jnp.where(pos == 0, head, below).astype(jnp.float32)
    upper = jnp.where(pos == ends, tail, above).astype(jnp.float32)
    return lower, upper


def body(
    values_in,
    shock_load,
    price_field,
    rate_liquid,
    rate_illiquid,
    mask_liquid,
    mask_illiquid,
    jump_inverse,
    coef_liquid,
    coef_illiquid,
    coef_income,
    owner,
):
    high = lax.Precision.HIGH
    columns, nz_loc, na_loc, _ = values_in.shape
    wide_pos = lax.axis_index("wide")
    inc_pos = lax.axis_index("inc")
    lower, upper = edges(values_in, "wide", 2)
    liquid_part = liquid_step(
        shock_load, values_in, lower, upper, rate_liquid, rate_illiquid, price_field,
        mask_liquid, mask_illiquid, cosine_table(NB)[:KBLOW].T,
    )
    liquid_part = jnp.transpose(liquid_part, (2, 3, 0, 1)).reshape(na_loc, KBLOW * columns * nz_loc)
    table_a = lax.dynamic_slice_in_dim(cosine_table(NA), wide_pos * na_loc, na_loc, axis=1)
    illiquid_part = jnp.dot(table_a, liquid_part, precision=high)
    rows = illiquid_part.reshape(NA * KBLOW, columns * nz_loc)
    picked = jnp.take(rows, coef_illiquid * KBLOW + coef_liquid, axis=0)
    folded = jnp.dot(cosine_table(NZ), jump_inverse, precision=lax.Precision.HIGHEST)
    folded = lax.dynamic_slice_in_dim(folded, inc_pos * nz_loc, nz_loc, axis=1)
    weight = jnp.take(folded, coef_income, axis=0)
    partial = jnp.sum(picked.reshape(-1, columns, nz_loc) * weight[:, None, :], axis=2)
    kept = lax.psum(partial.T, ("wide", "inc"))
    owners = lax.axis_size(("wide", "inc"))
    count = owner.shape[0]
    capacity = 2 * count // owners
    targets = slot_targets(owner, owners, capacity)
    source = jnp.full((owners * capacity,), count, jnp.int32).at[targets].set(jnp.arange(count, dtype=jnp.int32))
    mine = lax.dynamic_slice_in_dim(source, lax.axis_index(("wide", "inc")) * capacity, capacity)
    gathered = jnp.take(kept, jnp.minimum(mine, count - 1), axis=1)
    return jnp.where((mine < count)[None, :], gathered, jnp.float32(0.0))


def solution(mesh):
    placed = (
        P(("grp", "col"), "inc", "wide", None),
        P(("grp", "col")),
        P(("grp", "inc"), "wide", None),
        P(("grp", "inc"), "wide", None),
        P(("grp", "inc"), "wide", None),
        P(("grp", "inc"), "wide", None),
        P(("grp", "inc"), "wide", None),
        P("grp", None),
        P(),
        P(),
        P(),
        P(),
    )
    return jax.shard_map(
        body,
        mesh=mesh,
        in_specs=placed,
        out_specs=P(("grp", "col"), ("wide", "inc")),
        check_vma=False,
    )
```

```python
import functools
import jax
import jax.numpy as jnp
from jax import lax
from jax.experimental import pallas as pl
from jax.experimental.pallas import tpu as pltpu
from jax.sharding import PartitionSpec as P

NB = 512
NA = 256
NZ = 64
KBLOW = 128
Z_BLOCK = 8


def cosine_table(count):
    freq = jnp.arange(count, dtype=jnp.int32)[:, None]
    cell = jnp.arange(count, dtype=jnp.int32)[None, :]
    phase = (2 * cell + 1) * freq % (4 * count)
    angle = jnp.pi * phase.astype(jnp.float32) / (2.0 * count)
    first = jnp.where(freq == 0, jnp.sqrt(jnp.float32(0.5)), jnp.float32(1.0))
    return jnp.cos(angle) * jnp.sqrt(jnp.float32(2.0 / count)) * first


def slot_targets(owner, owners, capacity):
    onehot = (owner[:, None] == jnp.arange(owners, dtype=jnp.int32)[None, :]).astype(jnp.int32)
    before = jnp.cumsum(onehot, axis=0) - onehot
    slot = jnp.sum(before * onehot, axis=1)
    return owner * capacity + slot


def split_bf16(x):
    hi = x.astype(jnp.bfloat16)
    return hi, (x - hi.astype(jnp.float32)).astype(jnp.bfloat16)


def step_kernel(load_ref, vals_ref, lo_ref, up_ref, rl_ref, ri_ref, pf_ref, ml_ref, mi_ref, tb_ref, out_ref):
    columns = vals_ref.shape[0]
    zb, na, nb = rl_ref.shape
    kb = tb_ref.shape[1]
    rows = zb * na
    rl = rl_ref[...].reshape(rows, nb)
    ri = ri_ref[...].reshape(rows, nb)
    pf = pf_ref[...].reshape(rows, nb)
    mb = ml_ref[...].reshape(rows, nb) != 0
    ma = mi_ref[...].reshape(rows, nb) != 0
    col = lax.broadcasted_iota(jnp.int32, (rows, nb), 1)
    arow = lax.broadcasted_iota(jnp.int32, (zb, na, nb), 1).reshape(rows, nb)
    th, tl = split_bf16(tb_ref[...])

    def per_column(c, carry):
        v = vals_ref[c].reshape(rows, nb).astype(jnp.float32)
        lo = jnp.broadcast_to(lo_ref[c][:, None, :], (zb, na, nb)).reshape(rows, nb)
        up = jnp.broadcast_to(up_ref[c][:, None, :], (zb, na, nb)).reshape(rows, nb)
        fwd_b = jnp.where(col == nb - 1, 0.0, pltpu.roll(v, nb - 1, 1) - v)
        bwd_b = jnp.where(col == 0, 0.0, v - pltpu.roll(v, 1, 1))
        fwd_a = jnp.where(arow == na - 1, up, pltpu.roll(v, rows - 1, 0)) - v
        bwd_a = v - jnp.where(arow == 0, lo, pltpu.roll(v, 1, 0))
        sel_b = jnp.where(mb, fwd_b, -bwd_b)
        sel_a = jnp.where(ma, fwd_a, -bwd_a)
        explicit = v + rl * sel_b + ri * sel_a + load_ref[c] * pf
        hi, low = split_bf16(explicit)
        acc = jnp.dot(low, th, preferred_element_type=jnp.float32)
        acc = acc + jnp.dot(hi, tl, preferred_element_type=jnp.float32)
        acc = acc + jnp.dot(hi, th, preferred_element_type=jnp.float32)
        out_ref[c] = acc.reshape(zb, na, kb)
        return carry

    lax.fori_loop(0, columns, per_column, 0)


def liquid_step(load, vals, lower, upper, rl, ri, pf, ml, mi, tb):
    columns, nz, na, nb = vals.shape
    kb = tb.shape[1]
    zb = min(Z_BLOCK, nz)
    field = pl.BlockSpec((zb, na, nb), lambda j: (j, 0, 0))
    edge = pl.BlockSpec((columns, zb, nb), lambda j: (0, j, 0))
    table = pl.BlockSpec((nb, kb), lambda j: (0, 0))
    return pl.pallas_call(
        step_kernel,
        grid=(nz // zb,),
        in_specs=[
            pl.BlockSpec(memory_space=pltpu.SMEM),
            pl.BlockSpec((columns, zb, na, nb), lambda j: (0, j, 0, 0)),
            edge,
            edge,
            field,
            field,
            field,
            field,
            field,
            table,
        ],
        out_specs=pl.BlockSpec((columns, zb, na, kb), lambda j: (0, j, 0, 0)),
        out_shape=jax.ShapeDtypeStruct((columns, nz, na, kb), jnp.float32),
        compiler_params=pltpu.CompilerParams(vmem_limit_bytes=56 * 1024 * 1024),
    )(load, vals, lower, upper, rl, ri, pf, ml, mi, tb)


def edges(values, axis, dim):
    count = lax.axis_size(axis)
    pos = lax.axis_index(axis)
    ends = count - 1
    head = lax.index_in_dim(values, 0, axis=dim, keepdims=False)
    tail = lax.index_in_dim(values, values.shape[dim] - 1, axis=dim, keepdims=False)
    below = lax.ppermute(tail, axis, [(i, (i + 1) % count) for i in range(ends)])
    above = lax.ppermute(head, axis, [((i + 1) % count, i) for i in range(ends)])
    lower = jnp.where(pos == 0, head, below).astype(jnp.float32)
    upper = jnp.where(pos == ends, tail, above).astype(jnp.float32)
    return lower, upper


def body(
    values_in,
    shock_load,
    price_field,
    rate_liquid,
    rate_illiquid,
    mask_liquid,
    mask_illiquid,
    jump_inverse,
    coef_liquid,
    coef_illiquid,
    coef_income,
    owner,
):
    high = lax.Precision.HIGH
    columns, nz_loc, na_loc, _ = values_in.shape
    wide_pos = lax.axis_index("wide")
    inc_pos = lax.axis_index("inc")
    lower, upper = edges(values_in, "wide", 2)
    liquid_part = liquid_step(
        shock_load, values_in, lower, upper, rate_liquid, rate_illiquid, price_field,
        mask_liquid, mask_illiquid, cosine_table(NB)[:KBLOW].T,
    )
    liquid_part = jnp.transpose(liquid_part, (3, 2, 0, 1)).reshape(KBLOW, na_loc, columns * nz_loc)
    table_a = lax.dynamic_slice_in_dim(cosine_table(NA), wide_pos * na_loc, na_loc, axis=1)
    illiquid_part = jnp.einsum("ja,kac->kjc", table_a, liquid_part, precision=high)
    rows = illiquid_part.reshape(KBLOW * NA, columns * nz_loc)
    picked = jnp.take(rows, coef_liquid * NA + coef_illiquid, axis=0)
    folded = jnp.dot(cosine_table(NZ), jump_inverse, precision=lax.Precision.HIGHEST)
    folded = lax.dynamic_slice_in_dim(folded, inc_pos * nz_loc, nz_loc, axis=1)
    pick_z = (coef_income[:, None] == jnp.arange(NZ, dtype=jnp.int32)[None, :]).astype(jnp.float32)
    weight = jnp.dot(pick_z, folded, precision=lax.Precision.HIGHEST)
    partial = jnp.sum(picked.reshape(-1, columns, nz_loc) * weight[:, None, :], axis=2)
    kept = all_sum(partial.T, ("inc", "wide"))
    owners = lax.axis_size(("wide", "inc"))
    count = owner.shape[0]
    capacity = 2 * count // owners
    me = lax.axis_index(("wide", "inc"))
    seen = jnp.cumsum((owner == me).astype(jnp.int32))
    slots = jnp.arange(1, capacity + 1, dtype=jnp.int32)
    mine = jnp.sum((seen[None, :] < slots[:, None]).astype(jnp.int32), axis=1)
    gathered = jnp.take(kept, jnp.minimum(mine, count - 1), axis=1)
    return jnp.where((mine < count)[None, :], gathered, jnp.float32(0.0))


def all_sum(x, axes):
    for axis in axes:
        count = lax.axis_size(axis)
        step = 1
        while step < count:
            x = x + lax.ppermute(x, axis, [(i, i ^ step) for i in range(count)])
            step *= 2
    return x


def solution(mesh):
    placed = (
        P(("grp", "col"), "inc", "wide", None),
        P(("grp", "col")),
        P(("grp", "inc"), "wide", None),
        P(("grp", "inc"), "wide", None),
        P(("grp", "inc"), "wide", None),
        P(("grp", "inc"), "wide", None),
        P(("grp", "inc"), "wide", None),
        P("grp", None),
        P(),
        P(),
        P(),
        P(),
    )
    return jax.shard_map(
        body,
        mesh=mesh,
        in_specs=placed,
        out_specs=P(("grp", "col"), ("wide", "inc")),
        check_vma=False,
    )
```

```python
import functools
import jax
import jax.numpy as jnp
from jax import lax
from jax.experimental import pallas as pl
from jax.experimental.pallas import tpu as pltpu
from jax.sharding import PartitionSpec as P

NB = 512
NA = 256
NZ = 64
KBLOW = 128
Z_BLOCK = 8


def cosine_table(count):
    freq = jnp.arange(count, dtype=jnp.int32)[:, None]
    cell = jnp.arange(count, dtype=jnp.int32)[None, :]
    phase = (2 * cell + 1) * freq % (4 * count)
    angle = jnp.pi * phase.astype(jnp.float32) / (2.0 * count)
    first = jnp.where(freq == 0, jnp.sqrt(jnp.float32(0.5)), jnp.float32(1.0))
    return jnp.cos(angle) * jnp.sqrt(jnp.float32(2.0 / count)) * first


def slot_targets(owner, owners, capacity):
    onehot = (owner[:, None] == jnp.arange(owners, dtype=jnp.int32)[None, :]).astype(jnp.int32)
    before = jnp.cumsum(onehot, axis=0) - onehot
    slot = jnp.sum(before * onehot, axis=1)
    return owner * capacity + slot


def split_bf16(x):
    hi = x.astype(jnp.bfloat16)
    return hi, (x - hi.astype(jnp.float32)).astype(jnp.bfloat16)


def step_kernel(load_ref, vals_ref, lo_ref, up_ref, rl_ref, ri_ref, pf_ref, ml_ref, mi_ref, tb_ref, out_ref):
    columns = vals_ref.shape[0]
    zb, na, nb = rl_ref.shape
    kb = tb_ref.shape[1]
    rows = zb * na
    rl = rl_ref[...].reshape(rows, nb)
    ri = ri_ref[...].reshape(rows, nb)
    pf = pf_ref[...].reshape(rows, nb)
    mb = ml_ref[...].reshape(rows, nb) != 0
    ma = mi_ref[...].reshape(rows, nb) != 0
    col = lax.broadcasted_iota(jnp.int32, (rows, nb), 1)
    arow = lax.broadcasted_iota(jnp.int32, (zb, na, nb), 1).reshape(rows, nb)
    th, tl = split_bf16(tb_ref[...])

    def per_column(c, carry):
        v = vals_ref[c].reshape(rows, nb).astype(jnp.float32)
        lo = jnp.broadcast_to(lo_ref[c][:, None, :], (zb, na, nb)).reshape(rows, nb)
        up = jnp.broadcast_to(up_ref[c][:, None, :], (zb, na, nb)).reshape(rows, nb)
        fwd_b = jnp.where(col == nb - 1, 0.0, pltpu.roll(v, nb - 1, 1) - v)
        bwd_b = jnp.where(col == 0, 0.0, v - pltpu.roll(v, 1, 1))
        fwd_a = jnp.where(arow == na - 1, up, pltpu.roll(v, rows - 1, 0)) - v
        bwd_a = v - jnp.where(arow == 0, lo, pltpu.roll(v, 1, 0))
        sel_b = jnp.where(mb, fwd_b, -bwd_b)
        sel_a = jnp.where(ma, fwd_a, -bwd_a)
        explicit = v + rl * sel_b + ri * sel_a + load_ref[c] * pf
        hi, low = split_bf16(explicit)
        acc = jnp.dot(low, th, preferred_element_type=jnp.float32)
        acc = acc + jnp.dot(hi, tl, preferred_element_type=jnp.float32)
        acc = acc + jnp.dot(hi, th, preferred_element_type=jnp.float32)
        out_ref[c] = acc.reshape(zb, na, kb)
        return carry

    lax.fori_loop(0, columns, per_column, 0)


def liquid_step(load, vals, lower, upper, rl, ri, pf, ml, mi, tb):
    columns, nz, na, nb = vals.shape
    kb = tb.shape[1]
    zb = min(Z_BLOCK, nz)
    field = pl.BlockSpec((zb, na, nb), lambda j: (j, 0, 0))
    edge = pl.BlockSpec((columns, zb, nb), lambda j: (0, j, 0))
    table = pl.BlockSpec((nb, kb), lambda j: (0, 0))
    return pl.pallas_call(
        step_kernel,
        grid=(nz // zb,),
        in_specs=[
            pl.BlockSpec(memory_space=pltpu.SMEM),
            pl.BlockSpec((columns, zb, na, nb), lambda j: (0, j, 0, 0)),
            edge,
            edge,
            field,
            field,
            field,
            field,
            field,
            table,
        ],
        out_specs=pl.BlockSpec((columns, zb, na, kb), lambda j: (0, j, 0, 0)),
        out_shape=jax.ShapeDtypeStruct((columns, nz, na, kb), jnp.float32),
        compiler_params=pltpu.CompilerParams(vmem_limit_bytes=56 * 1024 * 1024),
    )(load, vals, lower, upper, rl, ri, pf, ml, mi, tb)


def illiquid_kernel(ca_ref, t_ref, out_ref):
    ch, cl = split_bf16(ca_ref[...])
    for k in range(t_ref.shape[0]):
        th, tl = split_bf16(t_ref[k])
        acc = jnp.dot(cl, th, preferred_element_type=jnp.float32)
        acc = acc + jnp.dot(ch, tl, preferred_element_type=jnp.float32)
        out_ref[k] = acc + jnp.dot(ch, th, preferred_element_type=jnp.float32)


def illiquid_step(ca, t):
    kb, na_loc, lanes = t.shape
    na = ca.shape[0]
    block = 8
    return pl.pallas_call(
        illiquid_kernel,
        grid=(kb // block,),
        in_specs=[
            pl.BlockSpec((na, na_loc), lambda j: (0, 0)),
            pl.BlockSpec((block, na_loc, lanes), lambda j: (j, 0, 0)),
        ],
        out_specs=pl.BlockSpec((block, na, lanes), lambda j: (j, 0, 0)),
        out_shape=jax.ShapeDtypeStruct((kb, na, lanes), jnp.float32),
    )(ca, t)


def edges(values, axis, dim):
    count = lax.axis_size(axis)
    pos = lax.axis_index(axis)
    ends = count - 1
    head = lax.index_in_dim(values, 0, axis=dim, keepdims=False)
    tail = lax.index_in_dim(values, values.shape[dim] - 1, axis=dim, keepdims=False)
    below = lax.ppermute(tail, axis, [(i, (i + 1) % count) for i in range(ends)])
    above = lax.ppermute(head, axis, [((i + 1) % count, i) for i in range(ends)])
    lower = jnp.where(pos == 0, head, below).astype(jnp.float32)
    upper = jnp.where(pos == ends, tail, above).astype(jnp.float32)
    return lower, upper


def body(
    values_in,
    shock_load,
    price_field,
    rate_liquid,
    rate_illiquid,
    mask_liquid,
    mask_illiquid,
    jump_inverse,
    coef_liquid,
    coef_illiquid,
    coef_income,
    owner,
):
    high = lax.Precision.HIGH
    columns, nz_loc, na_loc, _ = values_in.shape
    wide_pos = lax.axis_index("wide")
    inc_pos = lax.axis_index("inc")
    lower, upper = edges(values_in, "wide", 2)
    liquid_part = liquid_step(
        shock_load, values_in, lower, upper, rate_liquid, rate_illiquid, price_field,
        mask_liquid, mask_illiquid, cosine_table(NB)[:KBLOW].T,
    )
    liquid_part = jnp.transpose(liquid_part, (3, 2, 0, 1)).reshape(KBLOW, na_loc, columns * nz_loc)
    table_a = lax.dynamic_slice_in_dim(cosine_table(NA), wide_pos * na_loc, na_loc, axis=1)
    illiquid_part = illiquid_step(table_a, liquid_part)
    rows = illiquid_part.reshape(KBLOW * NA, columns * nz_loc)
    picked = jnp.take(rows, coef_liquid * NA + coef_illiquid, axis=0)
    folded = jnp.dot(cosine_table(NZ), jump_inverse, precision=lax.Precision.HIGHEST)
    folded = lax.dynamic_slice_in_dim(folded, inc_pos * nz_loc, nz_loc, axis=1)
    pick_z = (coef_income[:, None] == jnp.arange(NZ, dtype=jnp.int32)[None, :]).astype(jnp.float32)
    weight = jnp.dot(pick_z, folded, precision=lax.Precision.HIGHEST)
    partial = jnp.sum(picked.reshape(-1, columns, nz_loc) * weight[:, None, :], axis=2)
    kept = all_sum(partial.T, ("inc", "wide"))
    owners = lax.axis_size(("wide", "inc"))
    count = owner.shape[0]
    capacity = 2 * count // owners
    me = lax.axis_index(("wide", "inc"))
    seen = jnp.cumsum((owner == me).astype(jnp.int32))
    slots = jnp.arange(1, capacity + 1, dtype=jnp.int32)
    mine = jnp.sum((seen[None, :] < slots[:, None]).astype(jnp.int32), axis=1)
    gathered = jnp.take(kept, jnp.minimum(mine, count - 1), axis=1)
    return jnp.where((mine < count)[None, :], gathered, jnp.float32(0.0))


def all_sum(x, axes):
    for axis in axes:
        count = lax.axis_size(axis)
        step = 1
        while step < count:
            x = x + lax.ppermute(x, axis, [(i, i ^ step) for i in range(count)])
            step *= 2
    return x


def solution(mesh):
    placed = (
        P(("grp", "col"), "inc", "wide", None),
        P(("grp", "col")),
        P(("grp", "inc"), "wide", None),
        P(("grp", "inc"), "wide", None),
        P(("grp", "inc"), "wide", None),
        P(("grp", "inc"), "wide", None),
        P(("grp", "inc"), "wide", None),
        P("grp", None),
        P(),
        P(),
        P(),
        P(),
    )
    return jax.shard_map(
        body,
        mesh=mesh,
        in_specs=placed,
        out_specs=P(("grp", "col"), ("wide", "inc")),
        check_vma=False,
    )
```

```python
import functools
import jax
import jax.numpy as jnp
from jax import lax
from jax.experimental import pallas as pl
from jax.experimental.pallas import tpu as pltpu
from jax.sharding import PartitionSpec as P

NB = 512
NA = 256
NZ = 64
KBLOW = 128
Z_BLOCK = 8


def cosine_table(count):
    freq = jnp.arange(count, dtype=jnp.int32)[:, None]
    cell = jnp.arange(count, dtype=jnp.int32)[None, :]
    phase = (2 * cell + 1) * freq % (4 * count)
    angle = jnp.pi * phase.astype(jnp.float32) / (2.0 * count)
    first = jnp.where(freq == 0, jnp.sqrt(jnp.float32(0.5)), jnp.float32(1.0))
    return jnp.cos(angle) * jnp.sqrt(jnp.float32(2.0 / count)) * first


def slot_targets(owner, owners, capacity):
    onehot = (owner[:, None] == jnp.arange(owners, dtype=jnp.int32)[None, :]).astype(jnp.int32)
    before = jnp.cumsum(onehot, axis=0) - onehot
    slot = jnp.sum(before * onehot, axis=1)
    return owner * capacity + slot


def split_bf16(x):
    hi = x.astype(jnp.bfloat16)
    return hi, (x - hi.astype(jnp.float32)).astype(jnp.bfloat16)


def step_kernel(load_ref, vals_ref, lo_ref, up_ref, rl_ref, ri_ref, pf_ref, ml_ref, mi_ref, tb_ref, out_ref):
    columns = vals_ref.shape[0]
    zb, na, nb = rl_ref.shape
    kb = tb_ref.shape[1]
    rows = zb * na
    rl = rl_ref[...].reshape(rows, nb)
    ri = ri_ref[...].reshape(rows, nb)
    pf = pf_ref[...].reshape(rows, nb)
    mb = ml_ref[...].reshape(rows, nb) != 0
    ma = mi_ref[...].reshape(rows, nb) != 0
    col = lax.broadcasted_iota(jnp.int32, (rows, nb), 1)
    arow = lax.broadcasted_iota(jnp.int32, (zb, na, nb), 1).reshape(rows, nb)
    th, tl = split_bf16(tb_ref[...])

    def per_column(c, carry):
        v = vals_ref[c].reshape(rows, nb).astype(jnp.float32)
        lo = jnp.broadcast_to(lo_ref[c][:, None, :], (zb, na, nb)).reshape(rows, nb)
        up = jnp.broadcast_to(up_ref[c][:, None, :], (zb, na, nb)).reshape(rows, nb)
        fwd_b = jnp.where(col == nb - 1, 0.0, pltpu.roll(v, nb - 1, 1) - v)
        bwd_b = jnp.where(col == 0, 0.0, v - pltpu.roll(v, 1, 1))
        fwd_a = jnp.where(arow == na - 1, up, pltpu.roll(v, rows - 1, 0)) - v
        bwd_a = v - jnp.where(arow == 0, lo, pltpu.roll(v, 1, 0))
        sel_b = jnp.where(mb, fwd_b, -bwd_b)
        sel_a = jnp.where(ma, fwd_a, -bwd_a)
        explicit = v + rl * sel_b + ri * sel_a + load_ref[c] * pf
        hi, low = split_bf16(explicit)
        acc = jnp.dot(low, th, preferred_element_type=jnp.float32)
        acc = acc + jnp.dot(hi, tl, preferred_element_type=jnp.float32)
        acc = acc + jnp.dot(hi, th, preferred_element_type=jnp.float32)
        out_ref[c] = acc.reshape(zb, na, kb)
        return carry

    lax.fori_loop(0, columns, per_column, 0)


def liquid_step(load, vals, lower, upper, rl, ri, pf, ml, mi, tb):
    columns, nz, na, nb = vals.shape
    kb = tb.shape[1]
    zb = min(Z_BLOCK, nz)
    field = pl.BlockSpec((zb, na, nb), lambda j: (j, 0, 0))
    edge = pl.BlockSpec((columns, zb, nb), lambda j: (0, j, 0))
    table = pl.BlockSpec((nb, kb), lambda j: (0, 0))
    return pl.pallas_call(
        step_kernel,
        grid=(nz // zb,),
        in_specs=[
            pl.BlockSpec(memory_space=pltpu.SMEM),
            pl.BlockSpec((columns, zb, na, nb), lambda j: (0, j, 0, 0)),
            edge,
            edge,
            field,
            field,
            field,
            field,
            field,
            table,
        ],
        out_specs=pl.BlockSpec((columns, zb, na, kb), lambda j: (0, j, 0, 0)),
        out_shape=jax.ShapeDtypeStruct((columns, nz, na, kb), jnp.float32),
        compiler_params=pltpu.CompilerParams(vmem_limit_bytes=56 * 1024 * 1024),
    )(load, vals, lower, upper, rl, ri, pf, ml, mi, tb)


def illiquid_kernel(kb_ref, ka_ref, ca_ref, t_ref, out_ref, spectrum):
    j = pl.program_id(0)
    block = t_ref.shape[0]
    ch, cl = split_bf16(ca_ref[...])
    for k in range(block):
        th, tl = split_bf16(t_ref[k])
        acc = jnp.dot(cl, th, preferred_element_type=jnp.float32)
        acc = acc + jnp.dot(ch, tl, preferred_element_type=jnp.float32)
        spectrum[j * block + k] = acc + jnp.dot(ch, th, preferred_element_type=jnp.float32)

    @pl.when(j == pl.num_programs(0) - 1)
    def _():
        def pick(i, carry):
            out_ref[pl.ds(i, 1), :] = spectrum[kb_ref[i], pl.ds(ka_ref[i], 1), :]
            return carry

        lax.fori_loop(0, out_ref.shape[0], pick, 0, unroll=8)


def illiquid_pick(ca, t, kb_index, ka_index):
    kb, na_loc, lanes = t.shape
    na = ca.shape[0]
    count = kb_index.shape[0]
    block = 8
    return pl.pallas_call(
        illiquid_kernel,
        grid_spec=pltpu.PrefetchScalarGridSpec(
            num_scalar_prefetch=2,
            grid=(kb // block,),
            in_specs=[
                pl.BlockSpec((na, na_loc), lambda j, *_: (0, 0)),
                pl.BlockSpec((block, na_loc, lanes), lambda j, *_: (j, 0, 0)),
            ],
            out_specs=pl.BlockSpec((count, lanes), lambda j, *_: (0, 0)),
            scratch_shapes=[pltpu.VMEM((kb, na, lanes), jnp.float32)],
        ),
        out_shape=jax.ShapeDtypeStruct((count, lanes), jnp.float32),
        compiler_params=pltpu.CompilerParams(vmem_limit_bytes=60 * 1024 * 1024),
    )(kb_index, ka_index, ca, t)


def edges(values, axis, dim):
    count = lax.axis_size(axis)
    pos = lax.axis_index(axis)
    ends = count - 1
    head = lax.index_in_dim(values, 0, axis=dim, keepdims=False)
    tail = lax.index_in_dim(values, values.shape[dim] - 1, axis=dim, keepdims=False)
    below = lax.ppermute(tail, axis, [(i, (i + 1) % count) for i in range(ends)])
    above = lax.ppermute(head, axis, [((i + 1) % count, i) for i in range(ends)])
    lower = jnp.where(pos == 0, head, below).astype(jnp.float32)
    upper = jnp.where(pos == ends, tail, above).astype(jnp.float32)
    return lower, upper


def body(
    values_in,
    shock_load,
    price_field,
    rate_liquid,
    rate_illiquid,
    mask_liquid,
    mask_illiquid,
    jump_inverse,
    coef_liquid,
    coef_illiquid,
    coef_income,
    owner,
):
    high = lax.Precision.HIGH
    columns, nz_loc, na_loc, _ = values_in.shape
    wide_pos = lax.axis_index("wide")
    inc_pos = lax.axis_index("inc")
    lower, upper = edges(values_in, "wide", 2)
    liquid_part = liquid_step(
        shock_load, values_in, lower, upper, rate_liquid, rate_illiquid, price_field,
        mask_liquid, mask_illiquid, cosine_table(NB)[:KBLOW].T,
    )
    liquid_part = jnp.transpose(liquid_part, (3, 2, 0, 1)).reshape(KBLOW, na_loc, columns * nz_loc)
    table_a = lax.dynamic_slice_in_dim(cosine_table(NA), wide_pos * na_loc, na_loc, axis=1)
    picked = illiquid_pick(
        table_a, liquid_part, jnp.clip(coef_liquid, 0, KBLOW - 1), jnp.clip(coef_illiquid, 0, NA - 1)
    )
    folded = jnp.dot(cosine_table(NZ), jump_inverse, precision=lax.Precision.HIGHEST)
    folded = lax.dynamic_slice_in_dim(folded, inc_pos * nz_loc, nz_loc, axis=1)
    pick_z = (coef_income[:, None] == jnp.arange(NZ, dtype=jnp.int32)[None, :]).astype(jnp.float32)
    weight = jnp.dot(pick_z, folded, precision=lax.Precision.HIGHEST)
    partial = jnp.sum(picked.reshape(-1, columns, nz_loc) * weight[:, None, :], axis=2)
    kept = all_sum(partial.T, ("inc", "wide"))
    owners = lax.axis_size(("wide", "inc"))
    count = owner.shape[0]
    capacity = 2 * count // owners
    me = lax.axis_index(("wide", "inc"))
    seen = jnp.cumsum((owner == me).astype(jnp.int32))
    slots = jnp.arange(1, capacity + 1, dtype=jnp.int32)
    mine = jnp.sum((seen[None, :] < slots[:, None]).astype(jnp.int32), axis=1)
    gathered = jnp.take(kept, jnp.minimum(mine, count - 1), axis=1)
    return jnp.where((mine < count)[None, :], gathered, jnp.float32(0.0))


def all_sum(x, axes):
    for axis in axes:
        count = lax.axis_size(axis)
        step = 1
        while step < count:
            x = x + lax.ppermute(x, axis, [(i, i ^ step) for i in range(count)])
            step *= 2
    return x


def solution(mesh):
    placed = (
        P(("grp", "col"), "inc", "wide", None),
        P(("grp", "col")),
        P(("grp", "inc"), "wide", None),
        P(("grp", "inc"), "wide", None),
        P(("grp", "inc"), "wide", None),
        P(("grp", "inc"), "wide", None),
        P(("grp", "inc"), "wide", None),
        P("grp", None),
        P(),
        P(),
        P(),
        P(),
    )
    return jax.shard_map(
        body,
        mesh=mesh,
        in_specs=placed,
        out_specs=P(("grp", "col"), ("wide", "inc")),
        check_vma=False,
    )
```

```python
import functools
import jax
import jax.numpy as jnp
from jax import lax
from jax.experimental import pallas as pl
from jax.experimental.pallas import tpu as pltpu
from jax.sharding import PartitionSpec as P

NB = 512
NA = 256
NZ = 64
KBLOW = 128
Z_BLOCK = 8


def cosine_table(count):
    freq = jnp.arange(count, dtype=jnp.int32)[:, None]
    cell = jnp.arange(count, dtype=jnp.int32)[None, :]
    phase = (2 * cell + 1) * freq % (4 * count)
    angle = jnp.pi * phase.astype(jnp.float32) / (2.0 * count)
    first = jnp.where(freq == 0, jnp.sqrt(jnp.float32(0.5)), jnp.float32(1.0))
    return jnp.cos(angle) * jnp.sqrt(jnp.float32(2.0 / count)) * first


def slot_targets(owner, owners, capacity):
    onehot = (owner[:, None] == jnp.arange(owners, dtype=jnp.int32)[None, :]).astype(jnp.int32)
    before = jnp.cumsum(onehot, axis=0) - onehot
    slot = jnp.sum(before * onehot, axis=1)
    return owner * capacity + slot


def split_bf16(x):
    hi = x.astype(jnp.bfloat16)
    return hi, (x - hi.astype(jnp.float32)).astype(jnp.bfloat16)


def step_kernel(load_ref, vals_ref, lo_ref, up_ref, rl_ref, ri_ref, pf_ref, ml_ref, mi_ref, tb_ref, out_ref):
    columns = vals_ref.shape[0]
    zb, na, nb = rl_ref.shape
    kb = tb_ref.shape[1]
    rows = zb * na
    rl = rl_ref[...].reshape(rows, nb)
    ri = ri_ref[...].reshape(rows, nb)
    pf = pf_ref[...].reshape(rows, nb)
    mb = ml_ref[...].reshape(rows, nb) != 0
    ma = mi_ref[...].reshape(rows, nb) != 0
    col = lax.broadcasted_iota(jnp.int32, (rows, nb), 1)
    arow = lax.broadcasted_iota(jnp.int32, (zb, na, nb), 1).reshape(rows, nb)
    next_b = mb & (col != nb - 1)
    prev_b = jnp.logical_not(mb) & (col != 0)
    top = arow == na - 1
    bottom = arow == 0
    th, tl = split_bf16(tb_ref[...])
    pf_hi, pf_lo = split_bf16(pf)
    price = jnp.dot(pf_lo, th, preferred_element_type=jnp.float32)
    price = price + jnp.dot(pf_hi, tl, preferred_element_type=jnp.float32)
    price = price + jnp.dot(pf_hi, th, preferred_element_type=jnp.float32)

    def per_column(c, carry):
        v = vals_ref[c].reshape(rows, nb).astype(jnp.float32)
        lo = jnp.broadcast_to(lo_ref[c][:, None, :], (zb, na, nb)).reshape(rows, nb)
        up = jnp.broadcast_to(up_ref[c][:, None, :], (zb, na, nb)).reshape(rows, nb)
        side_b = jnp.where(next_b, pltpu.roll(v, nb - 1, 1), jnp.where(prev_b, pltpu.roll(v, 1, 1), v))
        above = jnp.where(top, up, pltpu.roll(v, rows - 1, 0))
        below = jnp.where(bottom, lo, pltpu.roll(v, 1, 0))
        side_a = jnp.where(ma, above, below)
        explicit = v + rl * (side_b - v) + ri * (side_a - v)
        hi, low = split_bf16(explicit)
        acc = jnp.dot(low, th, preferred_element_type=jnp.float32)
        acc = acc + jnp.dot(hi, tl, preferred_element_type=jnp.float32)
        acc = acc + jnp.dot(hi, th, preferred_element_type=jnp.float32)
        out_ref[c] = (acc + load_ref[c] * price).reshape(zb, na, kb)
        return carry

    lax.fori_loop(0, columns, per_column, 0)


def liquid_step(load, vals, lower, upper, rl, ri, pf, ml, mi, tb):
    columns, nz, na, nb = vals.shape
    kb = tb.shape[1]
    zb = min(Z_BLOCK, nz)
    field = pl.BlockSpec((zb, na, nb), lambda j: (j, 0, 0))
    edge = pl.BlockSpec((columns, zb, nb), lambda j: (0, j, 0))
    table = pl.BlockSpec((nb, kb), lambda j: (0, 0))
    return pl.pallas_call(
        step_kernel,
        grid=(nz // zb,),
        in_specs=[
            pl.BlockSpec(memory_space=pltpu.SMEM),
            pl.BlockSpec((columns, zb, na, nb), lambda j: (0, j, 0, 0)),
            edge,
            edge,
            field,
            field,
            field,
            field,
            field,
            table,
        ],
        out_specs=pl.BlockSpec((columns, zb, na, kb), lambda j: (0, j, 0, 0)),
        out_shape=jax.ShapeDtypeStruct((columns, nz, na, kb), jnp.float32),
        compiler_params=pltpu.CompilerParams(vmem_limit_bytes=56 * 1024 * 1024),
    )(load, vals, lower, upper, rl, ri, pf, ml, mi, tb)


def illiquid_kernel(kb_ref, ka_ref, ca_ref, t_ref, out_ref, spectrum):
    j = pl.program_id(0)
    block = t_ref.shape[0]
    ch, cl = split_bf16(ca_ref[...])
    for k in range(block):
        th, tl = split_bf16(t_ref[k])
        acc = jnp.dot(cl, th, preferred_element_type=jnp.float32)
        acc = acc + jnp.dot(ch, tl, preferred_element_type=jnp.float32)
        spectrum[j * block + k] = acc + jnp.dot(ch, th, preferred_element_type=jnp.float32)

    @pl.when(j == pl.num_programs(0) - 1)
    def _():
        def pick(i, carry):
            out_ref[pl.ds(i, 1), :] = spectrum[kb_ref[i], pl.ds(ka_ref[i], 1), :]
            return carry

        lax.fori_loop(0, out_ref.shape[0], pick, 0, unroll=8)


def illiquid_pick(ca, t, kb_index, ka_index):
    kb, na_loc, lanes = t.shape
    na = ca.shape[0]
    count = kb_index.shape[0]
    block = 8
    return pl.pallas_call(
        illiquid_kernel,
        grid_spec=pltpu.PrefetchScalarGridSpec(
            num_scalar_prefetch=2,
            grid=(kb // block,),
            in_specs=[
                pl.BlockSpec((na, na_loc), lambda j, *_: (0, 0)),
                pl.BlockSpec((block, na_loc, lanes), lambda j, *_: (j, 0, 0)),
            ],
            out_specs=pl.BlockSpec((count, lanes), lambda j, *_: (0, 0)),
            scratch_shapes=[pltpu.VMEM((kb, na, lanes), jnp.float32)],
        ),
        out_shape=jax.ShapeDtypeStruct((count, lanes), jnp.float32),
        compiler_params=pltpu.CompilerParams(vmem_limit_bytes=60 * 1024 * 1024),
    )(kb_index, ka_index, ca, t)


def edges(values, axis, dim):
    count = lax.axis_size(axis)
    pos = lax.axis_index(axis)
    ends = count - 1
    head = lax.index_in_dim(values, 0, axis=dim, keepdims=False)
    tail = lax.index_in_dim(values, values.shape[dim] - 1, axis=dim, keepdims=False)
    below = lax.ppermute(tail, axis, [(i, (i + 1) % count) for i in range(ends)])
    above = lax.ppermute(head, axis, [((i + 1) % count, i) for i in range(ends)])
    lower = jnp.where(pos == 0, head, below).astype(jnp.float32)
    upper = jnp.where(pos == ends, tail, above).astype(jnp.float32)
    return lower, upper


def body(
    values_in,
    shock_load,
    price_field,
    rate_liquid,
    rate_illiquid,
    mask_liquid,
    mask_illiquid,
    jump_inverse,
    coef_liquid,
    coef_illiquid,
    coef_income,
    owner,
):
    high = lax.Precision.HIGH
    columns, nz_loc, na_loc, _ = values_in.shape
    wide_pos = lax.axis_index("wide")
    inc_pos = lax.axis_index("inc")
    lower, upper = edges(values_in, "wide", 2)
    liquid_part = liquid_step(
        shock_load, values_in, lower, upper, rate_liquid, rate_illiquid, price_field,
        mask_liquid, mask_illiquid, cosine_table(NB)[:KBLOW].T,
    )
    liquid_part = jnp.transpose(liquid_part, (3, 2, 0, 1)).reshape(KBLOW, na_loc, columns * nz_loc)
    table_a = lax.dynamic_slice_in_dim(cosine_table(NA), wide_pos * na_loc, na_loc, axis=1)
    picked = illiquid_pick(
        table_a, liquid_part, jnp.clip(coef_liquid, 0, KBLOW - 1), jnp.clip(coef_illiquid, 0, NA - 1)
    )
    folded = jnp.dot(cosine_table(NZ), jump_inverse, precision=lax.Precision.HIGHEST)
    folded = lax.dynamic_slice_in_dim(folded, inc_pos * nz_loc, nz_loc, axis=1)
    pick_z = (coef_income[:, None] == jnp.arange(NZ, dtype=jnp.int32)[None, :]).astype(jnp.float32)
    weight = jnp.dot(pick_z, folded, precision=lax.Precision.HIGHEST)
    partial = jnp.sum(picked.reshape(-1, columns, nz_loc) * weight[:, None, :], axis=2)
    kept = all_sum(partial.T, ("inc", "wide"))
    owners = lax.axis_size(("wide", "inc"))
    count = owner.shape[0]
    capacity = 2 * count // owners
    me = lax.axis_index(("wide", "inc"))
    seen = jnp.cumsum((owner == me).astype(jnp.int32))
    slots = jnp.arange(1, capacity + 1, dtype=jnp.int32)
    mine = jnp.sum((seen[None, :] < slots[:, None]).astype(jnp.int32), axis=1)
    gathered = jnp.take(kept, jnp.minimum(mine, count - 1), axis=1)
    return jnp.where((mine < count)[None, :], gathered, jnp.float32(0.0))


def all_sum(x, axes):
    for axis in axes:
        count = lax.axis_size(axis)
        step = 1
        while step < count:
            x = x + lax.ppermute(x, axis, [(i, i ^ step) for i in range(count)])
            step *= 2
    return x


def solution(mesh):
    placed = (
        P(("grp", "col"), "inc", "wide", None),
        P(("grp", "col")),
        P(("grp", "inc"), "wide", None),
        P(("grp", "inc"), "wide", None),
        P(("grp", "inc"), "wide", None),
        P(("grp", "inc"), "wide", None),
        P(("grp", "inc"), "wide", None),
        P("grp", None),
        P(),
        P(),
        P(),
        P(),
    )
    return jax.shard_map(
        body,
        mesh=mesh,
        in_specs=placed,
        out_specs=P(("grp", "col"), ("wide", "inc")),
        check_vma=False,
    )
```

```python
import functools
import jax
import jax.numpy as jnp
from jax import lax
from jax.experimental import pallas as pl
from jax.experimental.pallas import tpu as pltpu
from jax.sharding import PartitionSpec as P

NB = 512
NA = 256
NZ = 64
KBLOW = 128
Z_BLOCK = 8
CHUNK = 16


def cosine_table(count):
    freq = jnp.arange(count, dtype=jnp.int32)[:, None]
    cell = jnp.arange(count, dtype=jnp.int32)[None, :]
    phase = (2 * cell + 1) * freq % (4 * count)
    angle = jnp.pi * phase.astype(jnp.float32) / (2.0 * count)
    first = jnp.where(freq == 0, jnp.sqrt(jnp.float32(0.5)), jnp.float32(1.0))
    return jnp.cos(angle) * jnp.sqrt(jnp.float32(2.0 / count)) * first


def slot_targets(owner, owners, capacity):
    onehot = (owner[:, None] == jnp.arange(owners, dtype=jnp.int32)[None, :]).astype(jnp.int32)
    before = jnp.cumsum(onehot, axis=0) - onehot
    slot = jnp.sum(before * onehot, axis=1)
    return owner * capacity + slot


def split_bf16(x):
    hi = x.astype(jnp.bfloat16)
    return hi, (x - hi.astype(jnp.float32)).astype(jnp.bfloat16)


def step_kernel(load_ref, vals_ref, lo_ref, up_ref, rl_ref, ri_ref, pf_ref, ml_ref, mi_ref, tb_ref, out_ref, ex_hi, ex_lo):
    columns, zb, na, nb = vals_ref.shape
    kb = tb_ref.shape[1]
    rows = zb * na
    depth = CHUNK if na % CHUNK == 0 else na
    chunks = na // depth
    col = lax.broadcasted_iota(jnp.int32, (depth, nb), 1)
    row = lax.broadcasted_iota(jnp.int32, (depth, nb), 0)

    def per_slab(index, carry):
        c = index // zb
        z = index % zb
        lo_row = lo_ref[c, pl.ds(z, 1), :]
        up_row = up_ref[c, pl.ds(z, 1), :]
        parts = [vals_ref[c, z, pl.ds(k * depth, depth), :].astype(jnp.float32) for k in range(chunks)]
        for k in range(chunks):
            v = parts[k]
            nxt = parts[k + 1][0:1] if k + 1 < chunks else up_row
            prv = parts[k - 1][depth - 1:depth] if k > 0 else lo_row
            above = jnp.where(row == depth - 1, nxt, pltpu.roll(v, depth - 1, 0))
            below = jnp.where(row == 0, prv, pltpu.roll(v, 1, 0))
            span = pl.ds(k * depth, depth)
            mb = ml_ref[z, span, :] != 0
            ma = mi_ref[z, span, :] != 0
            side_b = jnp.where(
                mb & (col != nb - 1),
                pltpu.roll(v, nb - 1, 1),
                jnp.where(jnp.logical_not(mb) & (col != 0), pltpu.roll(v, 1, 1), v),
            )
            side_a = jnp.where(ma, above, below)
            explicit = v + rl_ref[z, span, :] * (side_b - v) + ri_ref[z, span, :] * (side_a - v)
            hi, low = split_bf16(explicit)
            start = pl.multiple_of(z * na + k * depth, depth)
            ex_hi[c, pl.ds(start, depth), :] = hi
            ex_lo[c, pl.ds(start, depth), :] = low
        return carry

    lax.fori_loop(0, columns * zb, per_slab, 0)
    th, tl = split_bf16(tb_ref[...])
    pf_hi, pf_lo = split_bf16(pf_ref[...].reshape(rows, nb))
    price = jnp.dot(pf_lo, th, preferred_element_type=jnp.float32)
    price = price + jnp.dot(pf_hi, tl, preferred_element_type=jnp.float32)
    price = price + jnp.dot(pf_hi, th, preferred_element_type=jnp.float32)

    def per_column(c, carry):
        hi = ex_hi[c]
        acc = jnp.dot(ex_lo[c], th, preferred_element_type=jnp.float32)
        acc = acc + jnp.dot(hi, tl, preferred_element_type=jnp.float32)
        acc = acc + jnp.dot(hi, th, preferred_element_type=jnp.float32)
        out_ref[c] = (acc + load_ref[c] * price).reshape(zb, na, kb)
        return carry

    lax.fori_loop(0, columns, per_column, 0)


def liquid_step(load, vals, lower, upper, rl, ri, pf, ml, mi, tb):
    columns, nz, na, nb = vals.shape
    kb = tb.shape[1]
    zb = min(Z_BLOCK, nz)
    field = pl.BlockSpec((zb, na, nb), lambda j: (j, 0, 0))
    edge = pl.BlockSpec((columns, zb, nb), lambda j: (0, j, 0))
    table = pl.BlockSpec((nb, kb), lambda j: (0, 0))
    return pl.pallas_call(
        step_kernel,
        grid=(nz // zb,),
        in_specs=[
            pl.BlockSpec(memory_space=pltpu.SMEM),
            pl.BlockSpec((columns, zb, na, nb), lambda j: (0, j, 0, 0)),
            edge,
            edge,
            field,
            field,
            field,
            field,
            field,
            table,
        ],
        out_specs=pl.BlockSpec((columns, zb, na, kb), lambda j: (0, j, 0, 0)),
        out_shape=jax.ShapeDtypeStruct((columns, nz, na, kb), jnp.float32),
        scratch_shapes=[pltpu.VMEM((columns, zb * na, nb), jnp.bfloat16)] * 2,
        compiler_params=pltpu.CompilerParams(vmem_limit_bytes=56 * 1024 * 1024),
    )(load, vals, lower, upper, rl, ri, pf, ml, mi, tb)


def illiquid_kernel(kb_ref, ka_ref, ca_ref, t_ref, out_ref, spectrum):
    j = pl.program_id(0)
    block = t_ref.shape[0]
    ch, cl = split_bf16(ca_ref[...])
    for k in range(block):
        th, tl = split_bf16(t_ref[k])
        acc = jnp.dot(cl, th, preferred_element_type=jnp.float32)
        acc = acc + jnp.dot(ch, tl, preferred_element_type=jnp.float32)
        spectrum[j * block + k] = acc + jnp.dot(ch, th, preferred_element_type=jnp.float32)

    @pl.when(j == pl.num_programs(0) - 1)
    def _():
        def pick(i, carry):
            out_ref[pl.ds(i, 1), :] = spectrum[kb_ref[i], pl.ds(ka_ref[i], 1), :]
            return carry

        lax.fori_loop(0, out_ref.shape[0], pick, 0, unroll=8)


def illiquid_pick(ca, t, kb_index, ka_index):
    kb, na_loc, lanes = t.shape
    na = ca.shape[0]
    count = kb_index.shape[0]
    block = 8
    return pl.pallas_call(
        illiquid_kernel,
        grid_spec=pltpu.PrefetchScalarGridSpec(
            num_scalar_prefetch=2,
            grid=(kb // block,),
            in_specs=[
                pl.BlockSpec((na, na_loc), lambda j, *_: (0, 0)),
                pl.BlockSpec((block, na_loc, lanes), lambda j, *_: (j, 0, 0)),
            ],
            out_specs=pl.BlockSpec((count, lanes), lambda j, *_: (0, 0)),
            scratch_shapes=[pltpu.VMEM((kb, na, lanes), jnp.float32)],
        ),
        out_shape=jax.ShapeDtypeStruct((count, lanes), jnp.float32),
        compiler_params=pltpu.CompilerParams(vmem_limit_bytes=60 * 1024 * 1024),
    )(kb_index, ka_index, ca, t)


def edges(values, axis, dim):
    count = lax.axis_size(axis)
    pos = lax.axis_index(axis)
    ends = count - 1
    head = lax.index_in_dim(values, 0, axis=dim, keepdims=False)
    tail = lax.index_in_dim(values, values.shape[dim] - 1, axis=dim, keepdims=False)
    below = lax.ppermute(tail, axis, [(i, (i + 1) % count) for i in range(ends)])
    above = lax.ppermute(head, axis, [((i + 1) % count, i) for i in range(ends)])
    lower = jnp.where(pos == 0, head, below).astype(jnp.float32)
    upper = jnp.where(pos == ends, tail, above).astype(jnp.float32)
    return lower, upper


def body(
    values_in,
    shock_load,
    price_field,
    rate_liquid,
    rate_illiquid,
    mask_liquid,
    mask_illiquid,
    jump_inverse,
    coef_liquid,
    coef_illiquid,
    coef_income,
    owner,
):
    high = lax.Precision.HIGH
    columns, nz_loc, na_loc, _ = values_in.shape
    wide_pos = lax.axis_index("wide")
    inc_pos = lax.axis_index("inc")
    lower, upper = edges(values_in, "wide", 2)
    liquid_part = liquid_step(
        shock_load, values_in, lower, upper, rate_liquid, rate_illiquid, price_field,
        mask_liquid, mask_illiquid, cosine_table(NB)[:KBLOW].T,
    )
    liquid_part = jnp.transpose(liquid_part, (3, 2, 0, 1)).reshape(KBLOW, na_loc, columns * nz_loc)
    table_a = lax.dynamic_slice_in_dim(cosine_table(NA), wide_pos * na_loc, na_loc, axis=1)
    picked = illiquid_pick(
        table_a, liquid_part, jnp.clip(coef_liquid, 0, KBLOW - 1), jnp.clip(coef_illiquid, 0, NA - 1)
    )
    folded = jnp.dot(cosine_table(NZ), jump_inverse, precision=lax.Precision.HIGHEST)
    folded = lax.dynamic_slice_in_dim(folded, inc_pos * nz_loc, nz_loc, axis=1)
    pick_z = (coef_income[:, None] == jnp.arange(NZ, dtype=jnp.int32)[None, :]).astype(jnp.float32)
    weight = jnp.dot(pick_z, folded, precision=lax.Precision.HIGHEST)
    partial = jnp.sum(picked.reshape(-1, columns, nz_loc) * weight[:, None, :], axis=2)
    kept = all_sum(partial.T, ("inc", "wide"))
    owners = lax.axis_size(("wide", "inc"))
    count = owner.shape[0]
    capacity = 2 * count // owners
    me = lax.axis_index(("wide", "inc"))
    seen = jnp.cumsum((owner == me).astype(jnp.int32))
    slots = jnp.arange(1, capacity + 1, dtype=jnp.int32)
    mine = jnp.sum((seen[None, :] < slots[:, None]).astype(jnp.int32), axis=1)
    gathered = jnp.take(kept, jnp.minimum(mine, count - 1), axis=1)
    return jnp.where((mine < count)[None, :], gathered, jnp.float32(0.0))


def all_sum(x, axes):
    for axis in axes:
        count = lax.axis_size(axis)
        step = 1
        while step < count:
            x = x + lax.ppermute(x, axis, [(i, i ^ step) for i in range(count)])
            step *= 2
    return x


def solution(mesh):
    placed = (
        P(("grp", "col"), "inc", "wide", None),
        P(("grp", "col")),
        P(("grp", "inc"), "wide", None),
        P(("grp", "inc"), "wide", None),
        P(("grp", "inc"), "wide", None),
        P(("grp", "inc"), "wide", None),
        P(("grp", "inc"), "wide", None),
        P("grp", None),
        P(),
        P(),
        P(),
        P(),
    )
    return jax.shard_map(
        body,
        mesh=mesh,
        in_specs=placed,
        out_specs=P(("grp", "col"), ("wide", "inc")),
        check_vma=False,
    )
```

```python
import functools
import numpy as np
import jax
import jax.numpy as jnp
from jax import lax
from jax.experimental import pallas as pl
from jax.experimental.pallas import tpu as pltpu
from jax.sharding import PartitionSpec as P

NB = 512
NA = 256
NZ = 64
KBLOW = 128
Z_BLOCK = 8


def cosine_table(count):
    freq = jnp.arange(count, dtype=jnp.int32)[:, None]
    cell = jnp.arange(count, dtype=jnp.int32)[None, :]
    phase = (2 * cell + 1) * freq % (4 * count)
    angle = jnp.pi * phase.astype(jnp.float32) / (2.0 * count)
    first = jnp.where(freq == 0, jnp.sqrt(jnp.float32(0.5)), jnp.float32(1.0))
    return jnp.cos(angle) * jnp.sqrt(jnp.float32(2.0 / count)) * first


def cosine_constant(count):
    freq = np.arange(count)[:, None]
    cell = np.arange(count)[None, :]
    table = np.cos(np.pi * ((2 * cell + 1) * freq % (4 * count)) / (2.0 * count)) * np.sqrt(2.0 / count)
    table[0] *= np.sqrt(0.5)
    return table.astype(np.float32)


def slot_targets(owner, owners, capacity):
    onehot = (owner[:, None] == jnp.arange(owners, dtype=jnp.int32)[None, :]).astype(jnp.int32)
    before = jnp.cumsum(onehot, axis=0) - onehot
    slot = jnp.sum(before * onehot, axis=1)
    return owner * capacity + slot


def split_bf16(x):
    hi = x.astype(jnp.bfloat16)
    return hi, (x - hi.astype(jnp.float32)).astype(jnp.bfloat16)


def step_kernel(load_ref, vals_ref, lo_ref, up_ref, rl_ref, ri_ref, pf_ref, ml_ref, mi_ref, tb_ref, out_ref):
    columns = vals_ref.shape[0]
    zb, na, nb = rl_ref.shape
    kb = tb_ref.shape[1]
    rows = zb * na
    rl = rl_ref[...].reshape(rows, nb)
    ri = ri_ref[...].reshape(rows, nb)
    pf = pf_ref[...].reshape(rows, nb)
    mb = ml_ref[...].reshape(rows, nb) != 0
    ma = mi_ref[...].reshape(rows, nb) != 0
    col = lax.broadcasted_iota(jnp.int32, (rows, nb), 1)
    arow = lax.broadcasted_iota(jnp.int32, (zb, na, nb), 1).reshape(rows, nb)
    next_b = mb & (col != nb - 1)
    prev_b = jnp.logical_not(mb) & (col != 0)
    top = arow == na - 1
    bottom = arow == 0
    th, tl = split_bf16(tb_ref[...])
    pf_hi, pf_lo = split_bf16(pf)
    price = jnp.dot(pf_lo, th, preferred_element_type=jnp.float32)
    price = price + jnp.dot(pf_hi, tl, preferred_element_type=jnp.float32)
    price = price + jnp.dot(pf_hi, th, preferred_element_type=jnp.float32)

    def per_column(c, carry):
        v = vals_ref[c].reshape(rows, nb).astype(jnp.float32)
        lo = jnp.broadcast_to(lo_ref[c][:, None, :], (zb, na, nb)).reshape(rows, nb)
        up = jnp.broadcast_to(up_ref[c][:, None, :], (zb, na, nb)).reshape(rows, nb)
        side_b = jnp.where(next_b, pltpu.roll(v, nb - 1, 1), jnp.where(prev_b, pltpu.roll(v, 1, 1), v))
        above = jnp.where(top, up, pltpu.roll(v, rows - 1, 0))
        below = jnp.where(bottom, lo, pltpu.roll(v, 1, 0))
        side_a = jnp.where(ma, above, below)
        explicit = v + rl * (side_b - v) + ri * (side_a - v)
        hi, low = split_bf16(explicit)
        acc = jnp.dot(low, th, preferred_element_type=jnp.float32)
        acc = acc + jnp.dot(hi, tl, preferred_element_type=jnp.float32)
        acc = acc + jnp.dot(hi, th, preferred_element_type=jnp.float32)
        out_ref[c] = (acc + load_ref[c] * price).reshape(zb, na, kb)
        return carry

    lax.fori_loop(0, columns, per_column, 0)


def liquid_step(load, vals, lower, upper, rl, ri, pf, ml, mi, tb):
    columns, nz, na, nb = vals.shape
    kb = tb.shape[1]
    zb = min(Z_BLOCK, nz)
    field = pl.BlockSpec((zb, na, nb), lambda j: (j, 0, 0))
    edge = pl.BlockSpec((columns, zb, nb), lambda j: (0, j, 0))
    table = pl.BlockSpec((nb, kb), lambda j: (0, 0))
    return pl.pallas_call(
        step_kernel,
        grid=(nz // zb,),
        in_specs=[
            pl.BlockSpec(memory_space=pltpu.SMEM),
            pl.BlockSpec((columns, zb, na, nb), lambda j: (0, j, 0, 0)),
            edge,
            edge,
            field,
            field,
            field,
            field,
            field,
            table,
        ],
        out_specs=pl.BlockSpec((columns, zb, na, kb), lambda j: (0, j, 0, 0)),
        out_shape=jax.ShapeDtypeStruct((columns, nz, na, kb), jnp.float32),
        compiler_params=pltpu.CompilerParams(vmem_limit_bytes=56 * 1024 * 1024),
    )(load, vals, lower, upper, rl, ri, pf, ml, mi, tb)


def illiquid_kernel(kb_ref, ka_ref, ca_ref, t_ref, out_ref, spectrum):
    j = pl.program_id(0)
    block = t_ref.shape[0]
    ch, cl = split_bf16(ca_ref[...])
    for k in range(block):
        th, tl = split_bf16(t_ref[k])
        acc = jnp.dot(cl, th, preferred_element_type=jnp.float32)
        acc = acc + jnp.dot(ch, tl, preferred_element_type=jnp.float32)
        spectrum[j * block + k] = acc + jnp.dot(ch, th, preferred_element_type=jnp.float32)

    @pl.when(j == pl.num_programs(0) - 1)
    def _():
        def pick(i, carry):
            out_ref[pl.ds(i, 1), :] = spectrum[kb_ref[i], pl.ds(ka_ref[i], 1), :]
            return carry

        lax.fori_loop(0, out_ref.shape[0], pick, 0, unroll=8)


def illiquid_pick(ca, t, kb_index, ka_index):
    kb, na_loc, lanes = t.shape
    na = ca.shape[0]
    count = kb_index.shape[0]
    block = 8
    return pl.pallas_call(
        illiquid_kernel,
        grid_spec=pltpu.PrefetchScalarGridSpec(
            num_scalar_prefetch=2,
            grid=(kb // block,),
            in_specs=[
                pl.BlockSpec((na, na_loc), lambda j, *_: (0, 0)),
                pl.BlockSpec((block, na_loc, lanes), lambda j, *_: (j, 0, 0)),
            ],
            out_specs=pl.BlockSpec((count, lanes), lambda j, *_: (0, 0)),
            scratch_shapes=[pltpu.VMEM((kb, na, lanes), jnp.float32)],
        ),
        out_shape=jax.ShapeDtypeStruct((count, lanes), jnp.float32),
        compiler_params=pltpu.CompilerParams(vmem_limit_bytes=60 * 1024 * 1024),
    )(kb_index, ka_index, ca, t)


def edges(values, axis, dim):
    count = lax.axis_size(axis)
    pos = lax.axis_index(axis)
    ends = count - 1
    head = lax.index_in_dim(values, 0, axis=dim, keepdims=False)
    tail = lax.index_in_dim(values, values.shape[dim] - 1, axis=dim, keepdims=False)
    below = lax.ppermute(tail, axis, [(i, (i + 1) % count) for i in range(ends)])
    above = lax.ppermute(head, axis, [((i + 1) % count, i) for i in range(ends)])
    lower = jnp.where(pos == 0, head, below).astype(jnp.float32)
    upper = jnp.where(pos == ends, tail, above).astype(jnp.float32)
    return lower, upper


def body(
    values_in,
    shock_load,
    price_field,
    rate_liquid,
    rate_illiquid,
    mask_liquid,
    mask_illiquid,
    jump_inverse,
    coef_liquid,
    coef_illiquid,
    coef_income,
    owner,
):
    high = lax.Precision.HIGH
    columns, nz_loc, na_loc, _ = values_in.shape
    wide_pos = lax.axis_index("wide")
    inc_pos = lax.axis_index("inc")
    head = values_in[:, :, 0, :].astype(jnp.float32)
    tail = values_in[:, :, na_loc - 1, :].astype(jnp.float32)
    lower, upper = edges(values_in, "wide", 2)
    table_b = cosine_constant(NB)[:KBLOW]
    liquid_part = liquid_step(
        shock_load, values_in, head, tail, rate_liquid, rate_illiquid, price_field,
        mask_liquid, mask_illiquid, jnp.asarray(table_b.T),
    )
    rim = jnp.stack(
        [
            jnp.where(mask_illiquid[:, 0, :] == 0, rate_illiquid[:, 0, :] * (lower - head), 0.0),
            jnp.where(mask_illiquid[:, na_loc - 1, :] != 0, rate_illiquid[:, na_loc - 1, :] * (upper - tail), 0.0),
        ],
        axis=2,
    )
    rim = jnp.einsum("kb,czeb->czek", jnp.asarray(table_b), rim, precision=high)
    liquid_part = liquid_part.at[:, :, 0, :].add(rim[:, :, 0]).at[:, :, na_loc - 1, :].add(rim[:, :, 1])
    liquid_part = jnp.transpose(liquid_part, (3, 2, 0, 1)).reshape(KBLOW, na_loc, columns * nz_loc)
    table_a = lax.dynamic_slice_in_dim(jnp.asarray(cosine_constant(NA)), wide_pos * na_loc, na_loc, axis=1)
    picked = illiquid_pick(
        table_a, liquid_part, jnp.clip(coef_liquid, 0, KBLOW - 1), jnp.clip(coef_illiquid, 0, NA - 1)
    )
    folded = jnp.dot(jnp.asarray(cosine_constant(NZ)), jump_inverse, precision=lax.Precision.HIGHEST)
    folded = lax.dynamic_slice_in_dim(folded, inc_pos * nz_loc, nz_loc, axis=1)
    pick_z = (coef_income[:, None] == jnp.arange(NZ, dtype=jnp.int32)[None, :]).astype(jnp.float32)
    weight = jnp.dot(pick_z, folded, precision=lax.Precision.HIGHEST)
    partial = jnp.sum(picked.reshape(-1, columns, nz_loc) * weight[:, None, :], axis=2)
    kept = all_sum(partial.T, ("inc", "wide"))
    owners = lax.axis_size(("wide", "inc"))
    count = owner.shape[0]
    capacity = 2 * count // owners
    me = lax.axis_index(("wide", "inc"))
    seen = jnp.cumsum((owner == me).astype(jnp.int32))
    slots = jnp.arange(1, capacity + 1, dtype=jnp.int32)
    mine = jnp.sum((seen[None, :] < slots[:, None]).astype(jnp.int32), axis=1)
    gathered = jnp.take(kept, jnp.minimum(mine, count - 1), axis=1)
    return jnp.where((mine < count)[None, :], gathered, jnp.float32(0.0))


def all_sum(x, axes):
    for axis in axes:
        count = lax.axis_size(axis)
        step = 1
        while step < count:
            x = x + lax.ppermute(x, axis, [(i, i ^ step) for i in range(count)])
            step *= 2
    return x


def solution(mesh):
    placed = (
        P(("grp", "col"), "inc", "wide", None),
        P(("grp", "col")),
        P(("grp", "inc"), "wide", None),
        P(("grp", "inc"), "wide", None),
        P(("grp", "inc"), "wide", None),
        P(("grp", "inc"), "wide", None),
        P(("grp", "inc"), "wide", None),
        P("grp", None),
        P(),
        P(),
        P(),
        P(),
    )
    return jax.shard_map(
        body,
        mesh=mesh,
        in_specs=placed,
        out_specs=P(("grp", "col"), ("wide", "inc")),
        check_vma=False,
    )
```

```python
import functools
import numpy as np
import jax
import jax.numpy as jnp
from jax import lax
from jax.experimental import pallas as pl
from jax.experimental.pallas import tpu as pltpu
from jax.sharding import PartitionSpec as P

NB = 512
NA = 256
NZ = 64
KBLOW = 128
Z_BLOCK = 8


def cosine_table(count):
    freq = jnp.arange(count, dtype=jnp.int32)[:, None]
    cell = jnp.arange(count, dtype=jnp.int32)[None, :]
    phase = (2 * cell + 1) * freq % (4 * count)
    angle = jnp.pi * phase.astype(jnp.float32) / (2.0 * count)
    first = jnp.where(freq == 0, jnp.sqrt(jnp.float32(0.5)), jnp.float32(1.0))
    return jnp.cos(angle) * jnp.sqrt(jnp.float32(2.0 / count)) * first


def cosine_constant(count):
    freq = np.arange(count)[:, None]
    cell = np.arange(count)[None, :]
    table = np.cos(np.pi * ((2 * cell + 1) * freq % (4 * count)) / (2.0 * count)) * np.sqrt(2.0 / count)
    table[0] *= np.sqrt(0.5)
    return table.astype(np.float32)


def slot_targets(owner, owners, capacity):
    onehot = (owner[:, None] == jnp.arange(owners, dtype=jnp.int32)[None, :]).astype(jnp.int32)
    before = jnp.cumsum(onehot, axis=0) - onehot
    slot = jnp.sum(before * onehot, axis=1)
    return owner * capacity + slot


def split_bf16(x):
    hi = x.astype(jnp.bfloat16)
    return hi, (x - hi.astype(jnp.float32)).astype(jnp.bfloat16)


def step_kernel(load_ref, vals_ref, lo_ref, up_ref, rl_ref, ri_ref, pf_ref, ml_ref, mi_ref, tb_ref, out_ref):
    columns = vals_ref.shape[0]
    zb, na, nb = rl_ref.shape
    kb = tb_ref.shape[1]
    rows = zb * na
    rl = rl_ref[...].reshape(rows, nb)
    ri = ri_ref[...].reshape(rows, nb)
    pf = pf_ref[...].reshape(rows, nb)
    mb = ml_ref[...].reshape(rows, nb) != 0
    ma = mi_ref[...].reshape(rows, nb) != 0
    col = lax.broadcasted_iota(jnp.int32, (rows, nb), 1)
    arow = lax.broadcasted_iota(jnp.int32, (zb, na, nb), 1).reshape(rows, nb)
    next_b = mb & (col != nb - 1)
    prev_b = jnp.logical_not(mb) & (col != 0)
    top = arow == na - 1
    bottom = arow == 0
    th, tl = split_bf16(tb_ref[...])
    pf_hi, pf_lo = split_bf16(pf)
    price = jnp.dot(pf_lo, th, preferred_element_type=jnp.float32)
    price = price + jnp.dot(pf_hi, tl, preferred_element_type=jnp.float32)
    price = price + jnp.dot(pf_hi, th, preferred_element_type=jnp.float32)

    def per_column(c, carry):
        v = vals_ref[c].reshape(rows, nb).astype(jnp.float32)
        lo = jnp.broadcast_to(lo_ref[c][:, None, :], (zb, na, nb)).reshape(rows, nb)
        up = jnp.broadcast_to(up_ref[c][:, None, :], (zb, na, nb)).reshape(rows, nb)
        side_b = jnp.where(next_b, pltpu.roll(v, nb - 1, 1), jnp.where(prev_b, pltpu.roll(v, 1, 1), v))
        above = jnp.where(top, up, pltpu.roll(v, rows - 1, 0))
        below = jnp.where(bottom, lo, pltpu.roll(v, 1, 0))
        side_a = jnp.where(ma, above, below)
        explicit = v + rl * (side_b - v) + ri * (side_a - v)
        hi, low = split_bf16(explicit)
        acc = jnp.dot(low, th, preferred_element_type=jnp.float32)
        acc = acc + jnp.dot(hi, tl, preferred_element_type=jnp.float32)
        acc = acc + jnp.dot(hi, th, preferred_element_type=jnp.float32)
        out_ref[c] = (acc + load_ref[c] * price).reshape(zb, na, kb)
        return carry

    lax.fori_loop(0, columns, per_column, 0)


def liquid_step(load, vals, lower, upper, rl, ri, pf, ml, mi, tb):
    columns, nz, na, nb = vals.shape
    kb = tb.shape[1]
    zb = min(Z_BLOCK, nz)
    field = pl.BlockSpec((zb, na, nb), lambda j: (j, 0, 0))
    edge = pl.BlockSpec((columns, zb, nb), lambda j: (0, j, 0))
    table = pl.BlockSpec((nb, kb), lambda j: (0, 0))
    return pl.pallas_call(
        step_kernel,
        grid=(nz // zb,),
        in_specs=[
            pl.BlockSpec(memory_space=pltpu.SMEM),
            pl.BlockSpec((columns, zb, na, nb), lambda j: (0, j, 0, 0)),
            edge,
            edge,
            field,
            field,
            field,
            field,
            field,
            table,
        ],
        out_specs=pl.BlockSpec((columns, zb, na, kb), lambda j: (0, j, 0, 0)),
        out_shape=jax.ShapeDtypeStruct((columns, nz, na, kb), jnp.float32),
        compiler_params=pltpu.CompilerParams(vmem_limit_bytes=56 * 1024 * 1024),
    )(load, vals, lower, upper, rl, ri, pf, ml, mi, tb)


def illiquid_kernel(kb_ref, ka_ref, ca_ref, t_ref, rim_ref, out_ref, spectrum):
    j = pl.program_id(0)
    block, na_loc, lanes = t_ref.shape
    ch, cl = split_bf16(ca_ref[...])
    row = lax.broadcasted_iota(jnp.int32, (na_loc, lanes), 0)
    for k in range(block):
        rim = rim_ref[k]
        t = t_ref[k] + jnp.where(row == 0, rim[0:1], 0.0)
        th, tl = split_bf16(t + jnp.where(row == na_loc - 1, rim[1:2], 0.0))
        acc = jnp.dot(cl, th, preferred_element_type=jnp.float32)
        acc = acc + jnp.dot(ch, tl, preferred_element_type=jnp.float32)
        spectrum[j * block + k] = acc + jnp.dot(ch, th, preferred_element_type=jnp.float32)

    @pl.when(j == pl.num_programs(0) - 1)
    def _():
        def pick(i, carry):
            out_ref[pl.ds(i, 1), :] = spectrum[kb_ref[i], pl.ds(ka_ref[i], 1), :]
            return carry

        lax.fori_loop(0, out_ref.shape[0], pick, 0, unroll=8)


def illiquid_pick(ca, t, rim, kb_index, ka_index):
    kb, na_loc, lanes = t.shape
    na = ca.shape[0]
    count = kb_index.shape[0]
    block = 8
    return pl.pallas_call(
        illiquid_kernel,
        grid_spec=pltpu.PrefetchScalarGridSpec(
            num_scalar_prefetch=2,
            grid=(kb // block,),
            in_specs=[
                pl.BlockSpec((na, na_loc), lambda j, *_: (0, 0)),
                pl.BlockSpec((block, na_loc, lanes), lambda j, *_: (j, 0, 0)),
                pl.BlockSpec((block, 2, lanes), lambda j, *_: (j, 0, 0)),
            ],
            out_specs=pl.BlockSpec((count, lanes), lambda j, *_: (0, 0)),
            scratch_shapes=[pltpu.VMEM((kb, na, lanes), jnp.float32)],
        ),
        out_shape=jax.ShapeDtypeStruct((count, lanes), jnp.float32),
        compiler_params=pltpu.CompilerParams(vmem_limit_bytes=60 * 1024 * 1024),
    )(kb_index, ka_index, ca, t, rim)


def edges(values, axis, dim):
    count = lax.axis_size(axis)
    pos = lax.axis_index(axis)
    ends = count - 1
    head = lax.index_in_dim(values, 0, axis=dim, keepdims=False)
    tail = lax.index_in_dim(values, values.shape[dim] - 1, axis=dim, keepdims=False)
    below = lax.ppermute(tail, axis, [(i, (i + 1) % count) for i in range(ends)])
    above = lax.ppermute(head, axis, [((i + 1) % count, i) for i in range(ends)])
    lower = jnp.where(pos == 0, head, below).astype(jnp.float32)
    upper = jnp.where(pos == ends, tail, above).astype(jnp.float32)
    return lower, upper


def body(
    values_in,
    shock_load,
    price_field,
    rate_liquid,
    rate_illiquid,
    mask_liquid,
    mask_illiquid,
    jump_inverse,
    coef_liquid,
    coef_illiquid,
    coef_income,
    owner,
):
    high = lax.Precision.HIGH
    columns, nz_loc, na_loc, _ = values_in.shape
    wide_pos = lax.axis_index("wide")
    inc_pos = lax.axis_index("inc")
    head = values_in[:, :, 0, :].astype(jnp.float32)
    tail = values_in[:, :, na_loc - 1, :].astype(jnp.float32)
    lower, upper = edges(values_in, "wide", 2)
    table_b = cosine_constant(NB)[:KBLOW]
    liquid_part = liquid_step(
        shock_load, values_in, head, tail, rate_liquid, rate_illiquid, price_field,
        mask_liquid, mask_illiquid, jnp.asarray(table_b.T),
    )
    rim = jnp.stack(
        [
            jnp.where(mask_illiquid[:, 0, :] == 0, rate_illiquid[:, 0, :] * (lower - head), 0.0),
            jnp.where(mask_illiquid[:, na_loc - 1, :] != 0, rate_illiquid[:, na_loc - 1, :] * (upper - tail), 0.0),
        ],
        axis=2,
    )
    rim = jnp.einsum("kb,czeb->czek", jnp.asarray(table_b), rim, precision=high)
    rim = jnp.transpose(rim, (3, 2, 0, 1)).reshape(KBLOW, 2, columns * nz_loc)
    liquid_part = jnp.transpose(liquid_part, (3, 2, 0, 1)).reshape(KBLOW, na_loc, columns * nz_loc)
    table_a = lax.dynamic_slice_in_dim(jnp.asarray(cosine_constant(NA)), wide_pos * na_loc, na_loc, axis=1)
    picked = illiquid_pick(
        table_a, liquid_part, rim, jnp.clip(coef_liquid, 0, KBLOW - 1), jnp.clip(coef_illiquid, 0, NA - 1)
    )
    folded = jnp.dot(jnp.asarray(cosine_constant(NZ)), jump_inverse, precision=lax.Precision.HIGHEST)
    folded = lax.dynamic_slice_in_dim(folded, inc_pos * nz_loc, nz_loc, axis=1)
    pick_z = (coef_income[:, None] == jnp.arange(NZ, dtype=jnp.int32)[None, :]).astype(jnp.float32)
    weight = jnp.dot(pick_z, folded, precision=lax.Precision.HIGHEST)
    partial = jnp.sum(picked.reshape(-1, columns, nz_loc) * weight[:, None, :], axis=2)
    kept = all_sum(partial.T, ("inc", "wide"))
    owners = lax.axis_size(("wide", "inc"))
    count = owner.shape[0]
    capacity = 2 * count // owners
    me = lax.axis_index(("wide", "inc"))
    seen = jnp.cumsum((owner == me).astype(jnp.int32))
    slots = jnp.arange(1, capacity + 1, dtype=jnp.int32)
    mine = jnp.sum((seen[None, :] < slots[:, None]).astype(jnp.int32), axis=1)
    gathered = jnp.take(kept, jnp.minimum(mine, count - 1), axis=1)
    return jnp.where((mine < count)[None, :], gathered, jnp.float32(0.0))


def all_sum(x, axes):
    for axis in axes:
        count = lax.axis_size(axis)
        step = 1
        while step < count:
            x = x + lax.ppermute(x, axis, [(i, i ^ step) for i in range(count)])
            step *= 2
    return x


def solution(mesh):
    placed = (
        P(("grp", "col"), "inc", "wide", None),
        P(("grp", "col")),
        P(("grp", "inc"), "wide", None),
        P(("grp", "inc"), "wide", None),
        P(("grp", "inc"), "wide", None),
        P(("grp", "inc"), "wide", None),
        P(("grp", "inc"), "wide", None),
        P("grp", None),
        P(),
        P(),
        P(),
        P(),
    )
    return jax.shard_map(
        body,
        mesh=mesh,
        in_specs=placed,
        out_specs=P(("grp", "col"), ("wide", "inc")),
        check_vma=False,
    )
```

```python
import functools
import numpy as np
import jax
import jax.numpy as jnp
from jax import lax
from jax.experimental import pallas as pl
from jax.experimental.pallas import tpu as pltpu
from jax.sharding import PartitionSpec as P

NB = 512
NA = 256
NZ = 64
KBLOW = 128
Z_BLOCK = 8


def cosine_table(count):
    freq = jnp.arange(count, dtype=jnp.int32)[:, None]
    cell = jnp.arange(count, dtype=jnp.int32)[None, :]
    phase = (2 * cell + 1) * freq % (4 * count)
    angle = jnp.pi * phase.astype(jnp.float32) / (2.0 * count)
    first = jnp.where(freq == 0, jnp.sqrt(jnp.float32(0.5)), jnp.float32(1.0))
    return jnp.cos(angle) * jnp.sqrt(jnp.float32(2.0 / count)) * first


def cosine_constant(count):
    freq = np.arange(count)[:, None]
    cell = np.arange(count)[None, :]
    table = np.cos(np.pi * ((2 * cell + 1) * freq % (4 * count)) / (2.0 * count)) * np.sqrt(2.0 / count)
    table[0] *= np.sqrt(0.5)
    return table.astype(np.float32)


def slot_targets(owner, owners, capacity):
    onehot = (owner[:, None] == jnp.arange(owners, dtype=jnp.int32)[None, :]).astype(jnp.int32)
    before = jnp.cumsum(onehot, axis=0) - onehot
    slot = jnp.sum(before * onehot, axis=1)
    return owner * capacity + slot


def split_bf16(x):
    hi = x.astype(jnp.bfloat16)
    return hi, (x - hi.astype(jnp.float32)).astype(jnp.bfloat16)


def step_kernel(load_ref, vals_ref, lo_ref, up_ref, rl_ref, ri_ref, pf_ref, ml_ref, mi_ref, tb_ref, out_ref):
    columns = vals_ref.shape[0]
    zb, na, nb = rl_ref.shape
    kb = tb_ref.shape[1]
    rows = zb * na
    rl = rl_ref[...].reshape(rows, nb)
    ri = ri_ref[...].reshape(rows, nb)
    pf = pf_ref[...].reshape(rows, nb)
    mb = ml_ref[...].reshape(rows, nb) != 0
    ma = mi_ref[...].reshape(rows, nb) != 0
    col = lax.broadcasted_iota(jnp.int32, (rows, nb), 1)
    arow = lax.broadcasted_iota(jnp.int32, (zb, na, nb), 1).reshape(rows, nb)
    next_b = mb & (col != nb - 1)
    prev_b = jnp.logical_not(mb) & (col != 0)
    top = arow == na - 1
    bottom = arow == 0
    th, tl = split_bf16(tb_ref[...])
    pf_hi, pf_lo = split_bf16(pf)
    price = jnp.dot(pf_lo, th, preferred_element_type=jnp.float32)
    price = price + jnp.dot(pf_hi, tl, preferred_element_type=jnp.float32)
    price = price + jnp.dot(pf_hi, th, preferred_element_type=jnp.float32)

    def per_column(c, carry):
        v = vals_ref[c].reshape(rows, nb).astype(jnp.float32)
        lo = jnp.broadcast_to(lo_ref[c][:, None, :], (zb, na, nb)).reshape(rows, nb)
        up = jnp.broadcast_to(up_ref[c][:, None, :], (zb, na, nb)).reshape(rows, nb)
        side_b = jnp.where(next_b, pltpu.roll(v, nb - 1, 1), jnp.where(prev_b, pltpu.roll(v, 1, 1), v))
        above = jnp.where(top, up, pltpu.roll(v, rows - 1, 0))
        below = jnp.where(bottom, lo, pltpu.roll(v, 1, 0))
        side_a = jnp.where(ma, above, below)
        explicit = v + rl * (side_b - v) + ri * (side_a - v)
        hi, low = split_bf16(explicit)
        acc = jnp.dot(low, th, preferred_element_type=jnp.float32)
        acc = acc + jnp.dot(hi, tl, preferred_element_type=jnp.float32)
        acc = acc + jnp.dot(hi, th, preferred_element_type=jnp.float32)
        out_ref[c] = (acc + load_ref[c] * price).reshape(zb, na, kb)
        return carry

    lax.fori_loop(0, columns, per_column, 0)


def liquid_step(load, vals, lower, upper, rl, ri, pf, ml, mi, tb):
    columns, nz, na, nb = vals.shape
    kb = tb.shape[1]
    zb = min(Z_BLOCK, nz)
    field = pl.BlockSpec((zb, na, nb), lambda j: (j, 0, 0))
    edge = pl.BlockSpec((columns, zb, nb), lambda j: (0, j, 0))
    table = pl.BlockSpec((nb, kb), lambda j: (0, 0))
    return pl.pallas_call(
        step_kernel,
        grid=(nz // zb,),
        in_specs=[
            pl.BlockSpec(memory_space=pltpu.SMEM),
            pl.BlockSpec((columns, zb, na, nb), lambda j: (0, j, 0, 0)),
            edge,
            edge,
            field,
            field,
            field,
            field,
            field,
            table,
        ],
        out_specs=pl.BlockSpec((columns, zb, na, kb), lambda j: (0, j, 0, 0)),
        out_shape=jax.ShapeDtypeStruct((columns, nz, na, kb), jnp.float32),
        compiler_params=pltpu.CompilerParams(vmem_limit_bytes=56 * 1024 * 1024),
    )(load, vals, lower, upper, rl, ri, pf, ml, mi, tb)


def illiquid_kernel(kb_ref, ka_ref, ca_ref, t_ref, rim_ref, w_ref, group_ref, out_ref, spectrum, picked):
    j = pl.program_id(0)
    block, na_loc, lanes = t_ref.shape
    ch, cl = split_bf16(ca_ref[...])
    row = lax.broadcasted_iota(jnp.int32, (na_loc, lanes), 0)
    for k in range(block):
        rim = rim_ref[k]
        t = t_ref[k] + jnp.where(row == 0, rim[0:1], 0.0)
        th, tl = split_bf16(t + jnp.where(row == na_loc - 1, rim[1:2], 0.0))
        acc = jnp.dot(cl, th, preferred_element_type=jnp.float32)
        acc = acc + jnp.dot(ch, tl, preferred_element_type=jnp.float32)
        spectrum[j * block + k] = acc + jnp.dot(ch, th, preferred_element_type=jnp.float32)

    @pl.when(j == pl.num_programs(0) - 1)
    def _():
        def pick(i, carry):
            picked[pl.ds(i, 1), :] = spectrum[kb_ref[i], pl.ds(ka_ref[i], 1), :]
            return carry

        lax.fori_loop(0, picked.shape[0], pick, 0, unroll=8)
        rest = picked[...] * w_ref[...]
        group = group_ref[...]
        total = None
        for _ in range(3):
            part = rest.astype(jnp.bfloat16)
            rest = rest - part.astype(jnp.float32)
            term = lax.dot_general(group, part, (((1,), (1,)), ((), ())), preferred_element_type=jnp.float32)
            total = term if total is None else total + term
        out_ref[...] = total


def illiquid_pick(ca, t, rim, weight, group, kb_index, ka_index):
    kb, na_loc, lanes = t.shape
    na = ca.shape[0]
    count = kb_index.shape[0]
    block = 8
    return pl.pallas_call(
        illiquid_kernel,
        grid_spec=pltpu.PrefetchScalarGridSpec(
            num_scalar_prefetch=2,
            grid=(kb // block,),
            in_specs=[
                pl.BlockSpec((na, na_loc), lambda j, *_: (0, 0)),
                pl.BlockSpec((block, na_loc, lanes), lambda j, *_: (j, 0, 0)),
                pl.BlockSpec((block, 2, lanes), lambda j, *_: (j, 0, 0)),
                pl.BlockSpec((count, lanes), lambda j, *_: (0, 0)),
                pl.BlockSpec(group.shape, lambda j, *_: (0, 0)),
            ],
            out_specs=pl.BlockSpec((group.shape[0], count), lambda j, *_: (0, 0)),
            scratch_shapes=[pltpu.VMEM((kb, na, lanes), jnp.float32), pltpu.VMEM((count, lanes), jnp.float32)],
        ),
        out_shape=jax.ShapeDtypeStruct((group.shape[0], count), jnp.float32),
        compiler_params=pltpu.CompilerParams(vmem_limit_bytes=60 * 1024 * 1024),
    )(kb_index, ka_index, ca, t, rim, weight, group)


def edges(values, axis, dim):
    count = lax.axis_size(axis)
    pos = lax.axis_index(axis)
    ends = count - 1
    head = lax.index_in_dim(values, 0, axis=dim, keepdims=False)
    tail = lax.index_in_dim(values, values.shape[dim] - 1, axis=dim, keepdims=False)
    below = lax.ppermute(tail, axis, [(i, (i + 1) % count) for i in range(ends)])
    above = lax.ppermute(head, axis, [((i + 1) % count, i) for i in range(ends)])
    lower = jnp.where(pos == 0, head, below).astype(jnp.float32)
    upper = jnp.where(pos == ends, tail, above).astype(jnp.float32)
    return lower, upper


def body(
    values_in,
    shock_load,
    price_field,
    rate_liquid,
    rate_illiquid,
    mask_liquid,
    mask_illiquid,
    jump_inverse,
    coef_liquid,
    coef_illiquid,
    coef_income,
    owner,
):
    high = lax.Precision.HIGH
    columns, nz_loc, na_loc, _ = values_in.shape
    wide_pos = lax.axis_index("wide")
    inc_pos = lax.axis_index("inc")
    head = values_in[:, :, 0, :].astype(jnp.float32)
    tail = values_in[:, :, na_loc - 1, :].astype(jnp.float32)
    lower, upper = edges(values_in, "wide", 2)
    table_b = cosine_constant(NB)[:KBLOW]
    liquid_part = liquid_step(
        shock_load, values_in, head, tail, rate_liquid, rate_illiquid, price_field,
        mask_liquid, mask_illiquid, jnp.asarray(table_b.T),
    )
    rim = jnp.stack(
        [
            jnp.where(mask_illiquid[:, 0, :] == 0, rate_illiquid[:, 0, :] * (lower - head), 0.0),
            jnp.where(mask_illiquid[:, na_loc - 1, :] != 0, rate_illiquid[:, na_loc - 1, :] * (upper - tail), 0.0),
        ],
        axis=2,
    )
    rim = jnp.einsum("kb,czeb->czek", jnp.asarray(table_b), rim, precision=high)
    rim = jnp.transpose(rim, (3, 2, 0, 1)).reshape(KBLOW, 2, columns * nz_loc)
    liquid_part = jnp.transpose(liquid_part, (3, 2, 0, 1)).reshape(KBLOW, na_loc, columns * nz_loc)
    table_a = lax.dynamic_slice_in_dim(jnp.asarray(cosine_constant(NA)), wide_pos * na_loc, na_loc, axis=1)
    folded = jnp.dot(jnp.asarray(cosine_constant(NZ)), jump_inverse, precision=lax.Precision.HIGHEST)
    folded = lax.dynamic_slice_in_dim(folded, inc_pos * nz_loc, nz_loc, axis=1)
    pick_z = (coef_income[:, None] == jnp.arange(NZ, dtype=jnp.int32)[None, :]).astype(jnp.float32)
    weight = jnp.dot(pick_z, jnp.tile(folded, (1, columns)), precision=lax.Precision.HIGHEST)
    lanes = columns * nz_loc
    group = (jnp.arange(lanes)[None, :] // nz_loc == jnp.arange(columns)[:, None]).astype(jnp.bfloat16)
    partial = illiquid_pick(
        table_a, liquid_part, rim, weight, group,
        jnp.clip(coef_liquid, 0, KBLOW - 1), jnp.clip(coef_illiquid, 0, NA - 1),
    )
    kept = all_sum(partial, ("inc", "wide"))
    owners = lax.axis_size(("wide", "inc"))
    count = owner.shape[0]
    capacity = 2 * count // owners
    me = lax.axis_index(("wide", "inc"))
    seen = jnp.cumsum((owner == me).astype(jnp.int32))
    slots = jnp.arange(1, capacity + 1, dtype=jnp.int32)
    mine = jnp.sum((seen[None, :] < slots[:, None]).astype(jnp.int32), axis=1)
    gathered = jnp.take(kept, jnp.minimum(mine, count - 1), axis=1)
    return jnp.where((mine < count)[None, :], gathered, jnp.float32(0.0))


def all_sum(x, axes):
    for axis in axes:
        count = lax.axis_size(axis)
        step = 1
        while step < count:
            x = x + lax.ppermute(x, axis, [(i, i ^ step) for i in range(count)])
            step *= 2
    return x


def solution(mesh):
    placed = (
        P(("grp", "col"), "inc", "wide", None),
        P(("grp", "col")),
        P(("grp", "inc"), "wide", None),
        P(("grp", "inc"), "wide", None),
        P(("grp", "inc"), "wide", None),
        P(("grp", "inc"), "wide", None),
        P(("grp", "inc"), "wide", None),
        P("grp", None),
        P(),
        P(),
        P(),
        P(),
    )
    return jax.shard_map(
        body,
        mesh=mesh,
        in_specs=placed,
        out_specs=P(("grp", "col"), ("wide", "inc")),
        check_vma=False,
    )
```

```python
import functools
import ml_dtypes
import numpy as np
import jax
import jax.numpy as jnp
from jax import lax
from jax.experimental import pallas as pl
from jax.experimental.pallas import tpu as pltpu
from jax.sharding import PartitionSpec as P

NB = 512
NA = 256
NZ = 64
KBLOW = 128
Z_BLOCK = 8


def cosine_table(count):
    freq = jnp.arange(count, dtype=jnp.int32)[:, None]
    cell = jnp.arange(count, dtype=jnp.int32)[None, :]
    phase = (2 * cell + 1) * freq % (4 * count)
    angle = jnp.pi * phase.astype(jnp.float32) / (2.0 * count)
    first = jnp.where(freq == 0, jnp.sqrt(jnp.float32(0.5)), jnp.float32(1.0))
    return jnp.cos(angle) * jnp.sqrt(jnp.float32(2.0 / count)) * first


def cosine_constant(count):
    freq = np.arange(count)[:, None]
    cell = np.arange(count)[None, :]
    table = np.cos(np.pi * ((2 * cell + 1) * freq % (4 * count)) / (2.0 * count)) * np.sqrt(2.0 / count)
    table[0] *= np.sqrt(0.5)
    return table.astype(np.float32)


def stacked_constant(count):
    table = cosine_constant(count)
    high = table.astype(ml_dtypes.bfloat16)
    low = (table - high.astype(np.float32)).astype(ml_dtypes.bfloat16)
    return np.stack([low, high, high], axis=1)


def slot_targets(owner, owners, capacity):
    onehot = (owner[:, None] == jnp.arange(owners, dtype=jnp.int32)[None, :]).astype(jnp.int32)
    before = jnp.cumsum(onehot, axis=0) - onehot
    slot = jnp.sum(before * onehot, axis=1)
    return owner * capacity + slot


def split_bf16(x):
    hi = x.astype(jnp.bfloat16)
    return hi, (x - hi.astype(jnp.float32)).astype(jnp.bfloat16)


def step_kernel(load_ref, vals_ref, lo_ref, up_ref, rl_ref, ri_ref, pf_ref, ml_ref, mi_ref, tb_ref, out_ref):
    columns = vals_ref.shape[0]
    zb, na, nb = rl_ref.shape
    kb = tb_ref.shape[1]
    rows = zb * na
    rl = rl_ref[...].reshape(rows, nb)
    ri = ri_ref[...].reshape(rows, nb)
    pf = pf_ref[...].reshape(rows, nb)
    mb = ml_ref[...].reshape(rows, nb) != 0
    ma = mi_ref[...].reshape(rows, nb) != 0
    col = lax.broadcasted_iota(jnp.int32, (rows, nb), 1)
    arow = lax.broadcasted_iota(jnp.int32, (zb, na, nb), 1).reshape(rows, nb)
    next_b = mb & (col != nb - 1)
    prev_b = jnp.logical_not(mb) & (col != 0)
    top = arow == na - 1
    bottom = arow == 0
    th, tl = split_bf16(tb_ref[...])
    pf_hi, pf_lo = split_bf16(pf)
    price = jnp.dot(pf_lo, th, preferred_element_type=jnp.float32)
    price = price + jnp.dot(pf_hi, tl, preferred_element_type=jnp.float32)
    price = price + jnp.dot(pf_hi, th, preferred_element_type=jnp.float32)

    def per_column(c, carry):
        v = vals_ref[c].reshape(rows, nb).astype(jnp.float32)
        lo = jnp.broadcast_to(lo_ref[c][:, None, :], (zb, na, nb)).reshape(rows, nb)
        up = jnp.broadcast_to(up_ref[c][:, None, :], (zb, na, nb)).reshape(rows, nb)
        side_b = jnp.where(next_b, pltpu.roll(v, nb - 1, 1), jnp.where(prev_b, pltpu.roll(v, 1, 1), v))
        above = jnp.where(top, up, pltpu.roll(v, rows - 1, 0))
        below = jnp.where(bottom, lo, pltpu.roll(v, 1, 0))
        side_a = jnp.where(ma, above, below)
        explicit = v + rl * (side_b - v) + ri * (side_a - v)
        hi, low = split_bf16(explicit)
        acc = jnp.dot(low, th, preferred_element_type=jnp.float32)
        acc = acc + jnp.dot(hi, tl, preferred_element_type=jnp.float32)
        acc = acc + jnp.dot(hi, th, preferred_element_type=jnp.float32)
        out_ref[c] = (acc + load_ref[c] * price).reshape(zb, na, kb)
        return carry

    lax.fori_loop(0, columns, per_column, 0)


def liquid_step(load, vals, lower, upper, rl, ri, pf, ml, mi, tb):
    columns, nz, na, nb = vals.shape
    kb = tb.shape[1]
    zb = min(Z_BLOCK, nz)
    field = pl.BlockSpec((zb, na, nb), lambda j: (j, 0, 0))
    edge = pl.BlockSpec((columns, zb, nb), lambda j: (0, j, 0))
    table = pl.BlockSpec((nb, kb), lambda j: (0, 0))
    return pl.pallas_call(
        step_kernel,
        grid=(nz // zb,),
        in_specs=[
            pl.BlockSpec(memory_space=pltpu.SMEM),
            pl.BlockSpec((columns, zb, na, nb), lambda j: (0, j, 0, 0)),
            edge,
            edge,
            field,
            field,
            field,
            field,
            field,
            table,
        ],
        out_specs=pl.BlockSpec((columns, zb, na, kb), lambda j: (0, j, 0, 0)),
        out_shape=jax.ShapeDtypeStruct((columns, nz, na, kb), jnp.float32),
        compiler_params=pltpu.CompilerParams(vmem_limit_bytes=56 * 1024 * 1024),
    )(load, vals, lower, upper, rl, ri, pf, ml, mi, tb)


def illiquid_kernel(kb_ref, ka_ref, ca_ref, t_ref, rim_ref, w_ref, group_ref, out_ref, spectrum, picked):
    j = pl.program_id(0)
    block, na_loc, lanes = t_ref.shape
    stacked = ca_ref[...]
    row = lax.broadcasted_iota(jnp.int32, (na_loc, lanes), 0)
    for k in range(block):
        rim = rim_ref[k]
        t = t_ref[k] + jnp.where(row == 0, rim[0:1], 0.0)
        th, tl = split_bf16(t + jnp.where(row == na_loc - 1, rim[1:2], 0.0))
        rhs = jnp.concatenate([th, th, tl], axis=0)
        spectrum[j * block + k] = jnp.dot(stacked, rhs, preferred_element_type=jnp.float32)

    @pl.when(j == pl.num_programs(0) - 1)
    def _():
        def pick(i, carry):
            picked[pl.ds(i, 1), :] = spectrum[kb_ref[i], pl.ds(ka_ref[i], 1), :]
            return carry

        lax.fori_loop(0, picked.shape[0], pick, 0, unroll=8)
        rest = picked[...] * w_ref[...]
        group = group_ref[...]
        total = None
        for _ in range(3):
            part = rest.astype(jnp.bfloat16)
            rest = rest - part.astype(jnp.float32)
            term = lax.dot_general(group, part, (((1,), (1,)), ((), ())), preferred_element_type=jnp.float32)
            total = term if total is None else total + term
        out_ref[...] = total


def illiquid_pick(ca, t, rim, weight, group, kb_index, ka_index):
    kb, na_loc, lanes = t.shape
    na, depth = ca.shape
    count = kb_index.shape[0]
    block = 8
    return pl.pallas_call(
        illiquid_kernel,
        grid_spec=pltpu.PrefetchScalarGridSpec(
            num_scalar_prefetch=2,
            grid=(kb // block,),
            in_specs=[
                pl.BlockSpec((na, depth), lambda j, *_: (0, 0)),
                pl.BlockSpec((block, na_loc, lanes), lambda j, *_: (j, 0, 0)),
                pl.BlockSpec((block, 2, lanes), lambda j, *_: (j, 0, 0)),
                pl.BlockSpec((count, lanes), lambda j, *_: (0, 0)),
                pl.BlockSpec(group.shape, lambda j, *_: (0, 0)),
            ],
            out_specs=pl.BlockSpec((group.shape[0], count), lambda j, *_: (0, 0)),
            scratch_shapes=[pltpu.VMEM((kb, na, lanes), jnp.float32), pltpu.VMEM((count, lanes), jnp.float32)],
        ),
        out_shape=jax.ShapeDtypeStruct((group.shape[0], count), jnp.float32),
        compiler_params=pltpu.CompilerParams(vmem_limit_bytes=60 * 1024 * 1024),
    )(kb_index, ka_index, ca, t, rim, weight, group)


def edges(values, axis, dim):
    count = lax.axis_size(axis)
    pos = lax.axis_index(axis)
    ends = count - 1
    head = lax.index_in_dim(values, 0, axis=dim, keepdims=False)
    tail = lax.index_in_dim(values, values.shape[dim] - 1, axis=dim, keepdims=False)
    below = lax.ppermute(tail, axis, [(i, (i + 1) % count) for i in range(ends)])
    above = lax.ppermute(head, axis, [((i + 1) % count, i) for i in range(ends)])
    lower = jnp.where(pos == 0, head, below).astype(jnp.float32)
    upper = jnp.where(pos == ends, tail, above).astype(jnp.float32)
    return lower, upper


def body(
    values_in,
    shock_load,
    price_field,
    rate_liquid,
    rate_illiquid,
    mask_liquid,
    mask_illiquid,
    jump_inverse,
    coef_liquid,
    coef_illiquid,
    coef_income,
    owner,
):
    high = lax.Precision.HIGH
    columns, nz_loc, na_loc, _ = values_in.shape
    wide_pos = lax.axis_index("wide")
    inc_pos = lax.axis_index("inc")
    head = values_in[:, :, 0, :].astype(jnp.float32)
    tail = values_in[:, :, na_loc - 1, :].astype(jnp.float32)
    lower, upper = edges(values_in, "wide", 2)
    table_b = cosine_constant(NB)[:KBLOW]
    liquid_part = liquid_step(
        shock_load, values_in, head, tail, rate_liquid, rate_illiquid, price_field,
        mask_liquid, mask_illiquid, jnp.asarray(table_b.T),
    )
    rim = jnp.stack(
        [
            jnp.where(mask_illiquid[:, 0, :] == 0, rate_illiquid[:, 0, :] * (lower - head), 0.0),
            jnp.where(mask_illiquid[:, na_loc - 1, :] != 0, rate_illiquid[:, na_loc - 1, :] * (upper - tail), 0.0),
        ],
        axis=2,
    )
    rim = jnp.einsum("kb,czeb->czek", jnp.asarray(table_b), rim, precision=high)
    rim = jnp.transpose(rim, (3, 2, 0, 1)).reshape(KBLOW, 2, columns * nz_loc)
    liquid_part = jnp.transpose(liquid_part, (3, 2, 0, 1)).reshape(KBLOW, na_loc, columns * nz_loc)
    table_a = lax.dynamic_slice_in_dim(jnp.asarray(stacked_constant(NA)), wide_pos * na_loc, na_loc, axis=2)
    table_a = table_a.reshape(NA, 3 * na_loc)
    folded = jnp.dot(jnp.asarray(cosine_constant(NZ)), jump_inverse, precision=lax.Precision.HIGHEST)
    folded = lax.dynamic_slice_in_dim(folded, inc_pos * nz_loc, nz_loc, axis=1)
    pick_z = (coef_income[:, None] == jnp.arange(NZ, dtype=jnp.int32)[None, :]).astype(jnp.float32)
    weight = jnp.dot(pick_z, jnp.tile(folded, (1, columns)), precision=lax.Precision.HIGHEST)
    lanes = columns * nz_loc
    group = (jnp.arange(lanes)[None, :] // nz_loc == jnp.arange(columns)[:, None]).astype(jnp.bfloat16)
    partial = illiquid_pick(
        table_a, liquid_part, rim, weight, group,
        jnp.clip(coef_liquid, 0, KBLOW - 1), jnp.clip(coef_illiquid, 0, NA - 1),
    )
    kept = all_sum(partial, ("inc", "wide"))
    owners = lax.axis_size(("wide", "inc"))
    count = owner.shape[0]
    capacity = 2 * count // owners
    me = lax.axis_index(("wide", "inc"))
    seen = jnp.cumsum((owner == me).astype(jnp.int32))
    slots = jnp.arange(1, capacity + 1, dtype=jnp.int32)
    mine = jnp.sum((seen[None, :] < slots[:, None]).astype(jnp.int32), axis=1)
    gathered = jnp.take(kept, jnp.minimum(mine, count - 1), axis=1)
    return jnp.where((mine < count)[None, :], gathered, jnp.float32(0.0))


def all_sum(x, axes):
    for axis in axes:
        count = lax.axis_size(axis)
        step = 1
        while step < count:
            x = x + lax.ppermute(x, axis, [(i, i ^ step) for i in range(count)])
            step *= 2
    return x


def solution(mesh):
    placed = (
        P(("grp", "col"), "inc", "wide", None),
        P(("grp", "col")),
        P(("grp", "inc"), "wide", None),
        P(("grp", "inc"), "wide", None),
        P(("grp", "inc"), "wide", None),
        P(("grp", "inc"), "wide", None),
        P(("grp", "inc"), "wide", None),
        P("grp", None),
        P(),
        P(),
        P(),
        P(),
    )
    return jax.shard_map(
        body,
        mesh=mesh,
        in_specs=placed,
        out_specs=P(("grp", "col"), ("wide", "inc")),
        check_vma=False,
    )
```

```python
import functools
import ml_dtypes
import numpy as np
import jax
import jax.numpy as jnp
from jax import lax
from jax.experimental import pallas as pl
from jax.experimental.pallas import tpu as pltpu
from jax.sharding import PartitionSpec as P

NB = 512
NA = 256
NZ = 64
KBLOW = 128
Z_BLOCK = 8


def cosine_table(count):
    freq = jnp.arange(count, dtype=jnp.int32)[:, None]
    cell = jnp.arange(count, dtype=jnp.int32)[None, :]
    phase = (2 * cell + 1) * freq % (4 * count)
    angle = jnp.pi * phase.astype(jnp.float32) / (2.0 * count)
    first = jnp.where(freq == 0, jnp.sqrt(jnp.float32(0.5)), jnp.float32(1.0))
    return jnp.cos(angle) * jnp.sqrt(jnp.float32(2.0 / count)) * first


def cosine_constant(count):
    freq = np.arange(count)[:, None]
    cell = np.arange(count)[None, :]
    table = np.cos(np.pi * ((2 * cell + 1) * freq % (4 * count)) / (2.0 * count)) * np.sqrt(2.0 / count)
    table[0] *= np.sqrt(0.5)
    return table.astype(np.float32)


def stacked_constant(count):
    table = cosine_constant(count)
    high = table.astype(ml_dtypes.bfloat16)
    low = (table - high.astype(np.float32)).astype(ml_dtypes.bfloat16)
    return np.stack([low, high, high], axis=1)


def slot_targets(owner, owners, capacity):
    onehot = (owner[:, None] == jnp.arange(owners, dtype=jnp.int32)[None, :]).astype(jnp.int32)
    before = jnp.cumsum(onehot, axis=0) - onehot
    slot = jnp.sum(before * onehot, axis=1)
    return owner * capacity + slot


def split_bf16(x):
    hi = x.astype(jnp.bfloat16)
    return hi, (x - hi.astype(jnp.float32)).astype(jnp.bfloat16)


def step_kernel(load_ref, vals_ref, lo_ref, up_ref, rl_ref, ri_ref, pf_ref, ml_ref, mi_ref, tb_ref, out_ref):
    columns = vals_ref.shape[0]
    zb, na, nb = rl_ref.shape
    kb = tb_ref.shape[1]
    rows = zb * na
    rl = rl_ref[...].reshape(rows, nb)
    ri = ri_ref[...].reshape(rows, nb)
    pf = pf_ref[...].reshape(rows, nb)
    mb = ml_ref[...].reshape(rows, nb) != 0
    ma = mi_ref[...].reshape(rows, nb) != 0
    col = lax.broadcasted_iota(jnp.int32, (rows, nb), 1)
    arow = lax.broadcasted_iota(jnp.int32, (zb, na, nb), 1).reshape(rows, nb)
    next_b = mb & (col != nb - 1)
    prev_b = jnp.logical_not(mb) & (col != 0)
    top = arow == na - 1
    bottom = arow == 0
    th, tl = split_bf16(tb_ref[...])
    both = jnp.concatenate([th, tl], axis=1)

    def transform(x):
        hi, low = split_bf16(x)
        pair = jnp.dot(hi, both, preferred_element_type=jnp.float32)
        return jnp.dot(low, th, preferred_element_type=jnp.float32) + pair[:, kb:] + pair[:, :kb]

    price = transform(pf)

    def per_column(c, carry):
        v = vals_ref[c].reshape(rows, nb).astype(jnp.float32)
        lo = jnp.broadcast_to(lo_ref[c][:, None, :], (zb, na, nb)).reshape(rows, nb)
        up = jnp.broadcast_to(up_ref[c][:, None, :], (zb, na, nb)).reshape(rows, nb)
        side_b = jnp.where(next_b, pltpu.roll(v, nb - 1, 1), jnp.where(prev_b, pltpu.roll(v, 1, 1), v))
        above = jnp.where(top, up, pltpu.roll(v, rows - 1, 0))
        below = jnp.where(bottom, lo, pltpu.roll(v, 1, 0))
        side_a = jnp.where(ma, above, below)
        explicit = v + rl * (side_b - v) + ri * (side_a - v)
        out_ref[c] = (transform(explicit) + load_ref[c] * price).reshape(zb, na, kb)
        return carry

    lax.fori_loop(0, columns, per_column, 0)


def liquid_step(load, vals, lower, upper, rl, ri, pf, ml, mi, tb):
    columns, nz, na, nb = vals.shape
    kb = tb.shape[1]
    zb = min(Z_BLOCK, nz)
    field = pl.BlockSpec((zb, na, nb), lambda j: (j, 0, 0))
    edge = pl.BlockSpec((columns, zb, nb), lambda j: (0, j, 0))
    table = pl.BlockSpec((nb, kb), lambda j: (0, 0))
    return pl.pallas_call(
        step_kernel,
        grid=(nz // zb,),
        in_specs=[
            pl.BlockSpec(memory_space=pltpu.SMEM),
            pl.BlockSpec((columns, zb, na, nb), lambda j: (0, j, 0, 0)),
            edge,
            edge,
            field,
            field,
            field,
            field,
            field,
            table,
        ],
        out_specs=pl.BlockSpec((columns, zb, na, kb), lambda j: (0, j, 0, 0)),
        out_shape=jax.ShapeDtypeStruct((columns, nz, na, kb), jnp.float32),
        compiler_params=pltpu.CompilerParams(vmem_limit_bytes=56 * 1024 * 1024),
    )(load, vals, lower, upper, rl, ri, pf, ml, mi, tb)


def illiquid_kernel(kb_ref, ka_ref, ca_ref, t_ref, rim_ref, w_ref, group_ref, out_ref, spectrum, picked):
    j = pl.program_id(0)
    block, na_loc, lanes = t_ref.shape
    stacked = ca_ref[...]
    row = lax.broadcasted_iota(jnp.int32, (na_loc, lanes), 0)
    for k in range(block):
        rim = rim_ref[k]
        t = t_ref[k] + jnp.where(row == 0, rim[0:1], 0.0)
        th, tl = split_bf16(t + jnp.where(row == na_loc - 1, rim[1:2], 0.0))
        rhs = jnp.concatenate([th, th, tl], axis=0)
        spectrum[j * block + k] = jnp.dot(stacked, rhs, preferred_element_type=jnp.float32)

    @pl.when(j == pl.num_programs(0) - 1)
    def _():
        def pick(i, carry):
            picked[pl.ds(i, 1), :] = spectrum[kb_ref[i], pl.ds(ka_ref[i], 1), :]
            return carry

        lax.fori_loop(0, picked.shape[0], pick, 0, unroll=8)
        rest = picked[...] * w_ref[...]
        group = group_ref[...]
        total = None
        for _ in range(3):
            part = rest.astype(jnp.bfloat16)
            rest = rest - part.astype(jnp.float32)
            term = lax.dot_general(group, part, (((1,), (1,)), ((), ())), preferred_element_type=jnp.float32)
            total = term if total is None else total + term
        out_ref[...] = total


def illiquid_pick(ca, t, rim, weight, group, kb_index, ka_index):
    kb, na_loc, lanes = t.shape
    na, depth = ca.shape
    count = kb_index.shape[0]
    block = 8
    return pl.pallas_call(
        illiquid_kernel,
        grid_spec=pltpu.PrefetchScalarGridSpec(
            num_scalar_prefetch=2,
            grid=(kb // block,),
            in_specs=[
                pl.BlockSpec((na, depth), lambda j, *_: (0, 0)),
                pl.BlockSpec((block, na_loc, lanes), lambda j, *_: (j, 0, 0)),
                pl.BlockSpec((block, 2, lanes), lambda j, *_: (j, 0, 0)),
                pl.BlockSpec((count, lanes), lambda j, *_: (0, 0)),
                pl.BlockSpec(group.shape, lambda j, *_: (0, 0)),
            ],
            out_specs=pl.BlockSpec((group.shape[0], count), lambda j, *_: (0, 0)),
            scratch_shapes=[pltpu.VMEM((kb, na, lanes), jnp.float32), pltpu.VMEM((count, lanes), jnp.float32)],
        ),
        out_shape=jax.ShapeDtypeStruct((group.shape[0], count), jnp.float32),
        compiler_params=pltpu.CompilerParams(vmem_limit_bytes=60 * 1024 * 1024),
    )(kb_index, ka_index, ca, t, rim, weight, group)


def edges(values, axis, dim):
    count = lax.axis_size(axis)
    pos = lax.axis_index(axis)
    ends = count - 1
    head = lax.index_in_dim(values, 0, axis=dim, keepdims=False)
    tail = lax.index_in_dim(values, values.shape[dim] - 1, axis=dim, keepdims=False)
    below = lax.ppermute(tail, axis, [(i, (i + 1) % count) for i in range(ends)])
    above = lax.ppermute(head, axis, [((i + 1) % count, i) for i in range(ends)])
    lower = jnp.where(pos == 0, head, below).astype(jnp.float32)
    upper = jnp.where(pos == ends, tail, above).astype(jnp.float32)
    return lower, upper


def body(
    values_in,
    shock_load,
    price_field,
    rate_liquid,
    rate_illiquid,
    mask_liquid,
    mask_illiquid,
    jump_inverse,
    coef_liquid,
    coef_illiquid,
    coef_income,
    owner,
):
    high = lax.Precision.HIGH
    columns, nz_loc, na_loc, _ = values_in.shape
    wide_pos = lax.axis_index("wide")
    inc_pos = lax.axis_index("inc")
    head = values_in[:, :, 0, :].astype(jnp.float32)
    tail = values_in[:, :, na_loc - 1, :].astype(jnp.float32)
    lower, upper = edges(values_in, "wide", 2)
    table_b = cosine_constant(NB)[:KBLOW]
    liquid_part = liquid_step(
        shock_load, values_in, head, tail, rate_liquid, rate_illiquid, price_field,
        mask_liquid, mask_illiquid, jnp.asarray(table_b.T),
    )
    rim = jnp.stack(
        [
            jnp.where(mask_illiquid[:, 0, :] == 0, rate_illiquid[:, 0, :] * (lower - head), 0.0),
            jnp.where(mask_illiquid[:, na_loc - 1, :] != 0, rate_illiquid[:, na_loc - 1, :] * (upper - tail), 0.0),
        ],
        axis=2,
    )
    rim = jnp.einsum("kb,czeb->czek", jnp.asarray(table_b), rim, precision=high)
    rim = jnp.transpose(rim, (3, 2, 0, 1)).reshape(KBLOW, 2, columns * nz_loc)
    liquid_part = jnp.transpose(liquid_part, (3, 2, 0, 1)).reshape(KBLOW, na_loc, columns * nz_loc)
    table_a = lax.dynamic_slice_in_dim(jnp.asarray(stacked_constant(NA)), wide_pos * na_loc, na_loc, axis=2)
    table_a = table_a.reshape(NA, 3 * na_loc)
    folded = jnp.dot(jnp.asarray(cosine_constant(NZ)), jump_inverse, precision=lax.Precision.HIGHEST)
    folded = lax.dynamic_slice_in_dim(folded, inc_pos * nz_loc, nz_loc, axis=1)
    pick_z = (coef_income[:, None] == jnp.arange(NZ, dtype=jnp.int32)[None, :]).astype(jnp.float32)
    weight = jnp.dot(pick_z, jnp.tile(folded, (1, columns)), precision=lax.Precision.HIGHEST)
    lanes = columns * nz_loc
    group = (jnp.arange(lanes)[None, :] // nz_loc == jnp.arange(columns)[:, None]).astype(jnp.bfloat16)
    partial = illiquid_pick(
        table_a, liquid_part, rim, weight, group,
        jnp.clip(coef_liquid, 0, KBLOW - 1), jnp.clip(coef_illiquid, 0, NA - 1),
    )
    kept = all_sum(partial, ("inc", "wide"))
    owners = lax.axis_size(("wide", "inc"))
    count = owner.shape[0]
    capacity = 2 * count // owners
    me = lax.axis_index(("wide", "inc"))
    seen = jnp.cumsum((owner == me).astype(jnp.int32))
    slots = jnp.arange(1, capacity + 1, dtype=jnp.int32)
    mine = jnp.sum((seen[None, :] < slots[:, None]).astype(jnp.int32), axis=1)
    gathered = jnp.take(kept, jnp.minimum(mine, count - 1), axis=1)
    return jnp.where((mine < count)[None, :], gathered, jnp.float32(0.0))


def all_sum(x, axes):
    for axis in axes:
        count = lax.axis_size(axis)
        step = 1
        while step < count:
            x = x + lax.ppermute(x, axis, [(i, i ^ step) for i in range(count)])
            step *= 2
    return x


def solution(mesh):
    placed = (
        P(("grp", "col"), "inc", "wide", None),
        P(("grp", "col")),
        P(("grp", "inc"), "wide", None),
        P(("grp", "inc"), "wide", None),
        P(("grp", "inc"), "wide", None),
        P(("grp", "inc"), "wide", None),
        P(("grp", "inc"), "wide", None),
        P("grp", None),
        P(),
        P(),
        P(),
        P(),
    )
    return jax.shard_map(
        body,
        mesh=mesh,
        in_specs=placed,
        out_specs=P(("grp", "col"), ("wide", "inc")),
        check_vma=False,
    )
```

```python
import functools
import ml_dtypes
import numpy as np
import jax
import jax.numpy as jnp
from jax import lax
from jax.experimental import pallas as pl
from jax.experimental.pallas import tpu as pltpu
from jax.sharding import PartitionSpec as P

NB = 512
NA = 256
NZ = 64
KBLOW = 128
Z_BLOCK = 8


def cosine_table(count):
    freq = jnp.arange(count, dtype=jnp.int32)[:, None]
    cell = jnp.arange(count, dtype=jnp.int32)[None, :]
    phase = (2 * cell + 1) * freq % (4 * count)
    angle = jnp.pi * phase.astype(jnp.float32) / (2.0 * count)
    first = jnp.where(freq == 0, jnp.sqrt(jnp.float32(0.5)), jnp.float32(1.0))
    return jnp.cos(angle) * jnp.sqrt(jnp.float32(2.0 / count)) * first


def cosine_constant(count):
    freq = np.arange(count)[:, None]
    cell = np.arange(count)[None, :]
    table = np.cos(np.pi * ((2 * cell + 1) * freq % (4 * count)) / (2.0 * count)) * np.sqrt(2.0 / count)
    table[0] *= np.sqrt(0.5)
    return table.astype(np.float32)


def stacked_constant(count):
    table = cosine_constant(count)
    high = table.astype(ml_dtypes.bfloat16)
    low = (table - high.astype(np.float32)).astype(ml_dtypes.bfloat16)
    return np.stack([low, high, high], axis=1)


def slot_targets(owner, owners, capacity):
    onehot = (owner[:, None] == jnp.arange(owners, dtype=jnp.int32)[None, :]).astype(jnp.int32)
    before = jnp.cumsum(onehot, axis=0) - onehot
    slot = jnp.sum(before * onehot, axis=1)
    return owner * capacity + slot


def split_bf16(x):
    hi = x.astype(jnp.bfloat16)
    return hi, (x - hi.astype(jnp.float32)).astype(jnp.bfloat16)


def step_kernel(load_ref, vals_ref, lo_ref, up_ref, rl_ref, ri_ref, pf_ref, ml_ref, mi_ref, tb_ref, out_ref):
    columns = vals_ref.shape[0]
    zb, na, nb = rl_ref.shape
    kb = tb_ref.shape[1]
    rows = zb * na
    rl = rl_ref[...].reshape(rows, nb)
    ri = ri_ref[...].reshape(rows, nb)
    pf = pf_ref[...].reshape(rows, nb)
    mb = ml_ref[...].reshape(rows, nb) != 0
    ma = mi_ref[...].reshape(rows, nb) != 0
    col = lax.broadcasted_iota(jnp.int32, (rows, nb), 1)
    arow = lax.broadcasted_iota(jnp.int32, (zb, na, nb), 1).reshape(rows, nb)
    next_b = mb & (col != nb - 1)
    prev_b = jnp.logical_not(mb) & (col != 0)
    top = arow == na - 1
    bottom = arow == 0
    th, tl = split_bf16(tb_ref[...])
    both = jnp.concatenate([th, tl], axis=1)

    def transform(x):
        hi, low = split_bf16(x)
        pair = jnp.dot(hi, both, preferred_element_type=jnp.float32)
        return jnp.dot(low, th, preferred_element_type=jnp.float32) + pair[:, kb:] + pair[:, :kb]

    price = transform(pf)

    def per_column(c, carry):
        v = vals_ref[c].reshape(rows, nb).astype(jnp.float32)
        lo = jnp.broadcast_to(lo_ref[c][:, None, :], (zb, na, nb)).reshape(rows, nb)
        up = jnp.broadcast_to(up_ref[c][:, None, :], (zb, na, nb)).reshape(rows, nb)
        side_b = jnp.where(next_b, pltpu.roll(v, nb - 1, 1), jnp.where(prev_b, pltpu.roll(v, 1, 1), v))
        above = jnp.where(top, up, pltpu.roll(v, rows - 1, 0))
        below = jnp.where(bottom, lo, pltpu.roll(v, 1, 0))
        side_a = jnp.where(ma, above, below)
        explicit = v + rl * (side_b - v) + ri * (side_a - v)
        out_ref[c] = (transform(explicit) + load_ref[c] * price).reshape(zb, na, kb)
        return carry

    lax.fori_loop(0, columns, per_column, 0)


def liquid_step(load, vals, lower, upper, rl, ri, pf, ml, mi, tb):
    columns, nz, na, nb = vals.shape
    kb = tb.shape[1]
    zb = min(Z_BLOCK, nz)
    field = pl.BlockSpec((zb, na, nb), lambda j: (j, 0, 0))
    edge = pl.BlockSpec((columns, zb, nb), lambda j: (0, j, 0))
    table = pl.BlockSpec((nb, kb), lambda j: (0, 0))
    return pl.pallas_call(
        step_kernel,
        grid=(nz // zb,),
        in_specs=[
            pl.BlockSpec(memory_space=pltpu.SMEM),
            pl.BlockSpec((columns, zb, na, nb), lambda j: (0, j, 0, 0)),
            edge,
            edge,
            field,
            field,
            field,
            field,
            field,
            table,
        ],
        out_specs=pl.BlockSpec((columns, zb, na, kb), lambda j: (0, j, 0, 0)),
        out_shape=jax.ShapeDtypeStruct((columns, nz, na, kb), jnp.float32),
        compiler_params=pltpu.CompilerParams(vmem_limit_bytes=56 * 1024 * 1024),
    )(load, vals, lower, upper, rl, ri, pf, ml, mi, tb)


def illiquid_kernel(row_ref, ca_ref, t_ref, rim_ref, w_ref, group_ref, out_ref, spectrum, picked):
    j = pl.program_id(0)
    block, na_loc, lanes = t_ref.shape
    stacked = ca_ref[...]
    row = lax.broadcasted_iota(jnp.int32, (na_loc, lanes), 0)
    for k in range(block):
        rim = rim_ref[k]
        t = t_ref[k] + jnp.where(row == 0, rim[0:1], 0.0)
        th, tl = split_bf16(t + jnp.where(row == na_loc - 1, rim[1:2], 0.0))
        rhs = jnp.concatenate([th, th, tl], axis=0)
        start = pl.multiple_of((j * block + k) * stacked.shape[0], stacked.shape[0])
        spectrum[pl.ds(start, stacked.shape[0]), :] = jnp.dot(stacked, rhs, preferred_element_type=jnp.float32)

    @pl.when(j == pl.num_programs(0) - 1)
    def _():
        def pick(i, carry):
            picked[pl.ds(i, 1), :] = spectrum[pl.ds(row_ref[i], 1), :]
            return carry

        lax.fori_loop(0, picked.shape[0], pick, 0, unroll=8)
        rest = picked[...] * w_ref[...]
        group = group_ref[...]
        total = None
        for _ in range(3):
            part = rest.astype(jnp.bfloat16)
            rest = rest - part.astype(jnp.float32)
            term = lax.dot_general(group, part, (((1,), (1,)), ((), ())), preferred_element_type=jnp.float32)
            total = term if total is None else total + term
        out_ref[...] = total


def illiquid_pick(ca, t, rim, weight, group, row_index):
    kb, na_loc, lanes = t.shape
    na, depth = ca.shape
    count = row_index.shape[0]
    block = 8
    return pl.pallas_call(
        illiquid_kernel,
        grid_spec=pltpu.PrefetchScalarGridSpec(
            num_scalar_prefetch=1,
            grid=(kb // block,),
            in_specs=[
                pl.BlockSpec((na, depth), lambda j, *_: (0, 0)),
                pl.BlockSpec((block, na_loc, lanes), lambda j, *_: (j, 0, 0)),
                pl.BlockSpec((block, 2, lanes), lambda j, *_: (j, 0, 0)),
                pl.BlockSpec((count, lanes), lambda j, *_: (0, 0)),
                pl.BlockSpec(group.shape, lambda j, *_: (0, 0)),
            ],
            out_specs=pl.BlockSpec((group.shape[0], count), lambda j, *_: (0, 0)),
            scratch_shapes=[pltpu.VMEM((kb * na, lanes), jnp.float32), pltpu.VMEM((count, lanes), jnp.float32)],
        ),
        out_shape=jax.ShapeDtypeStruct((group.shape[0], count), jnp.float32),
        compiler_params=pltpu.CompilerParams(vmem_limit_bytes=60 * 1024 * 1024),
    )(row_index, ca, t, rim, weight, group)


def edges(values, axis, dim):
    count = lax.axis_size(axis)
    pos = lax.axis_index(axis)
    ends = count - 1
    head = lax.index_in_dim(values, 0, axis=dim, keepdims=False)
    tail = lax.index_in_dim(values, values.shape[dim] - 1, axis=dim, keepdims=False)
    below = lax.ppermute(tail, axis, [(i, (i + 1) % count) for i in range(ends)])
    above = lax.ppermute(head, axis, [((i + 1) % count, i) for i in range(ends)])
    lower = jnp.where(pos == 0, head, below).astype(jnp.float32)
    upper = jnp.where(pos == ends, tail, above).astype(jnp.float32)
    return lower, upper


def body(
    values_in,
    shock_load,
    price_field,
    rate_liquid,
    rate_illiquid,
    mask_liquid,
    mask_illiquid,
    jump_inverse,
    coef_liquid,
    coef_illiquid,
    coef_income,
    owner,
):
    high = lax.Precision.HIGH
    columns, nz_loc, na_loc, _ = values_in.shape
    wide_pos = lax.axis_index("wide")
    inc_pos = lax.axis_index("inc")
    head = values_in[:, :, 0, :].astype(jnp.float32)
    tail = values_in[:, :, na_loc - 1, :].astype(jnp.float32)
    lower, upper = edges(values_in, "wide", 2)
    table_b = cosine_constant(NB)[:KBLOW]
    liquid_part = liquid_step(
        shock_load, values_in, head, tail, rate_liquid, rate_illiquid, price_field,
        mask_liquid, mask_illiquid, jnp.asarray(table_b.T),
    )
    rim = jnp.stack(
        [
            jnp.where(mask_illiquid[:, 0, :] == 0, rate_illiquid[:, 0, :] * (lower - head), 0.0),
            jnp.where(mask_illiquid[:, na_loc - 1, :] != 0, rate_illiquid[:, na_loc - 1, :] * (upper - tail), 0.0),
        ],
        axis=2,
    )
    rim = jnp.einsum("kb,czeb->czek", jnp.asarray(table_b), rim, precision=high)
    rim = jnp.transpose(rim, (3, 2, 0, 1)).reshape(KBLOW, 2, columns * nz_loc)
    liquid_part = jnp.transpose(liquid_part, (3, 2, 0, 1)).reshape(KBLOW, na_loc, columns * nz_loc)
    table_a = lax.dynamic_slice_in_dim(jnp.asarray(stacked_constant(NA)), wide_pos * na_loc, na_loc, axis=2)
    table_a = table_a.reshape(NA, 3 * na_loc)
    folded = jnp.dot(jnp.asarray(cosine_constant(NZ)), jump_inverse, precision=lax.Precision.HIGHEST)
    folded = lax.dynamic_slice_in_dim(folded, inc_pos * nz_loc, nz_loc, axis=1)
    pick_z = (coef_income[:, None] == jnp.arange(NZ, dtype=jnp.int32)[None, :]).astype(jnp.float32)
    weight = jnp.dot(pick_z, jnp.tile(folded, (1, columns)), precision=lax.Precision.HIGHEST)
    lanes = columns * nz_loc
    group = (jnp.arange(lanes)[None, :] // nz_loc == jnp.arange(columns)[:, None]).astype(jnp.bfloat16)
    partial = illiquid_pick(
        table_a, liquid_part, rim, weight, group,
        jnp.clip(coef_liquid, 0, KBLOW - 1) * NA + jnp.clip(coef_illiquid, 0, NA - 1),
    )
    kept = all_sum(partial, ("inc", "wide"))
    owners = lax.axis_size(("wide", "inc"))
    count = owner.shape[0]
    capacity = 2 * count // owners
    me = lax.axis_index(("wide", "inc"))
    seen = jnp.cumsum((owner == me).astype(jnp.int32))
    slots = jnp.arange(1, capacity + 1, dtype=jnp.int32)
    mine = jnp.sum((seen[None, :] < slots[:, None]).astype(jnp.int32), axis=1)
    gathered = jnp.take(kept, jnp.minimum(mine, count - 1), axis=1)
    return jnp.where((mine < count)[None, :], gathered, jnp.float32(0.0))


def all_sum(x, axes):
    for axis in axes:
        count = lax.axis_size(axis)
        step = 1
        while step < count:
            x = x + lax.ppermute(x, axis, [(i, i ^ step) for i in range(count)])
            step *= 2
    return x


def solution(mesh):
    placed = (
        P(("grp", "col"), "inc", "wide", None),
        P(("grp", "col")),
        P(("grp", "inc"), "wide", None),
        P(("grp", "inc"), "wide", None),
        P(("grp", "inc"), "wide", None),
        P(("grp", "inc"), "wide", None),
        P(("grp", "inc"), "wide", None),
        P("grp", None),
        P(),
        P(),
        P(),
        P(),
    )
    return jax.shard_map(
        body,
        mesh=mesh,
        in_specs=placed,
        out_specs=P(("grp", "col"), ("wide", "inc")),
        check_vma=False,
    )
```

```python
import functools
import ml_dtypes
import numpy as np
import jax
import jax.numpy as jnp
from jax import lax
from jax.experimental import pallas as pl
from jax.experimental.pallas import tpu as pltpu
from jax.sharding import PartitionSpec as P

NB = 512
NA = 256
NZ = 64
KBLOW = 128
Z_BLOCK = 8


def cosine_table(count):
    freq = jnp.arange(count, dtype=jnp.int32)[:, None]
    cell = jnp.arange(count, dtype=jnp.int32)[None, :]
    phase = (2 * cell + 1) * freq % (4 * count)
    angle = jnp.pi * phase.astype(jnp.float32) / (2.0 * count)
    first = jnp.where(freq == 0, jnp.sqrt(jnp.float32(0.5)), jnp.float32(1.0))
    return jnp.cos(angle) * jnp.sqrt(jnp.float32(2.0 / count)) * first


def cosine_constant(count):
    freq = np.arange(count)[:, None]
    cell = np.arange(count)[None, :]
    table = np.cos(np.pi * ((2 * cell + 1) * freq % (4 * count)) / (2.0 * count)) * np.sqrt(2.0 / count)
    table[0] *= np.sqrt(0.5)
    return table.astype(np.float32)


def stacked_constant(count):
    table = cosine_constant(count)
    high = table.astype(ml_dtypes.bfloat16)
    low = (table - high.astype(np.float32)).astype(ml_dtypes.bfloat16)
    return np.stack([low, high, high], axis=1)


def slot_targets(owner, owners, capacity):
    onehot = (owner[:, None] == jnp.arange(owners, dtype=jnp.int32)[None, :]).astype(jnp.int32)
    before = jnp.cumsum(onehot, axis=0) - onehot
    slot = jnp.sum(before * onehot, axis=1)
    return owner * capacity + slot


def split_bf16(x):
    hi = x.astype(jnp.bfloat16)
    return hi, (x - hi.astype(jnp.float32)).astype(jnp.bfloat16)


def step_kernel(load_ref, vals_ref, rl_ref, ri_ref, pf_ref, ml_ref, mi_ref, tb_ref, out_ref):
    columns = vals_ref.shape[0]
    zb, na, nb = rl_ref.shape
    kb = tb_ref.shape[1]
    rows = zb * na
    rl = rl_ref[...].reshape(rows, nb)
    ri = ri_ref[...].reshape(rows, nb)
    pf = pf_ref[...].reshape(rows, nb)
    mb = ml_ref[...].reshape(rows, nb) != 0
    ma = mi_ref[...].reshape(rows, nb) != 0
    col = lax.broadcasted_iota(jnp.int32, (rows, nb), 1)
    arow = lax.broadcasted_iota(jnp.int32, (zb, na, nb), 1).reshape(rows, nb)
    next_b = mb & (col != nb - 1)
    prev_b = jnp.logical_not(mb) & (col != 0)
    next_a = ma & (arow != na - 1)
    prev_a = jnp.logical_not(ma) & (arow != 0)
    th, tl = split_bf16(tb_ref[...])
    both = jnp.concatenate([th, tl], axis=1)

    def transform(x):
        hi, low = split_bf16(x)
        pair = jnp.dot(hi, both, preferred_element_type=jnp.float32)
        return jnp.dot(low, th, preferred_element_type=jnp.float32) + pair[:, kb:] + pair[:, :kb]

    price = transform(pf)

    def per_column(c, carry):
        v = vals_ref[c].reshape(rows, nb).astype(jnp.float32)
        side_b = jnp.where(next_b, pltpu.roll(v, nb - 1, 1), jnp.where(prev_b, pltpu.roll(v, 1, 1), v))
        side_a = jnp.where(next_a, pltpu.roll(v, rows - 1, 0), jnp.where(prev_a, pltpu.roll(v, 1, 0), v))
        explicit = v + rl * (side_b - v) + ri * (side_a - v)
        out_ref[c] = (transform(explicit) + load_ref[c] * price).reshape(zb, na, kb)
        return carry

    lax.fori_loop(0, columns, per_column, 0)


def liquid_step(load, vals, rl, ri, pf, ml, mi, tb):
    columns, nz, na, nb = vals.shape
    kb = tb.shape[1]
    zb = min(Z_BLOCK, nz)
    field = pl.BlockSpec((zb, na, nb), lambda j: (j, 0, 0))
    table = pl.BlockSpec((nb, kb), lambda j: (0, 0))
    return pl.pallas_call(
        step_kernel,
        grid=(nz // zb,),
        in_specs=[
            pl.BlockSpec(memory_space=pltpu.SMEM),
            pl.BlockSpec((columns, zb, na, nb), lambda j: (0, j, 0, 0)),
            field,
            field,
            field,
            field,
            field,
            table,
        ],
        out_specs=pl.BlockSpec((columns, zb, na, kb), lambda j: (0, j, 0, 0)),
        out_shape=jax.ShapeDtypeStruct((columns, nz, na, kb), jnp.float32),
        compiler_params=pltpu.CompilerParams(vmem_limit_bytes=56 * 1024 * 1024),
    )(load, vals, rl, ri, pf, ml, mi, tb)


def illiquid_kernel(row_ref, ca_ref, t_ref, rim_ref, w_ref, group_ref, out_ref, spectrum, picked):
    j = pl.program_id(0)
    block, na_loc, lanes = t_ref.shape
    stacked = ca_ref[...]
    row = lax.broadcasted_iota(jnp.int32, (na_loc, lanes), 0)
    for k in range(block):
        rim = rim_ref[k]
        t = t_ref[k] + jnp.where(row == 0, rim[0:1], 0.0)
        th, tl = split_bf16(t + jnp.where(row == na_loc - 1, rim[1:2], 0.0))
        rhs = jnp.concatenate([th, th, tl], axis=0)
        start = pl.multiple_of((j * block + k) * stacked.shape[0], stacked.shape[0])
        spectrum[pl.ds(start, stacked.shape[0]), :] = jnp.dot(stacked, rhs, preferred_element_type=jnp.float32)

    @pl.when(j == pl.num_programs(0) - 1)
    def _():
        def pick(i, carry):
            picked[pl.ds(i, 1), :] = spectrum[pl.ds(row_ref[i], 1), :]
            return carry

        lax.fori_loop(0, picked.shape[0], pick, 0, unroll=8)
        rest = picked[...] * w_ref[...]
        group = group_ref[...]
        total = None
        for _ in range(3):
            part = rest.astype(jnp.bfloat16)
            rest = rest - part.astype(jnp.float32)
            term = lax.dot_general(group, part, (((1,), (1,)), ((), ())), preferred_element_type=jnp.float32)
            total = term if total is None else total + term
        out_ref[...] = total


def illiquid_pick(ca, t, rim, weight, group, row_index):
    kb, na_loc, lanes = t.shape
    na, depth = ca.shape
    count = row_index.shape[0]
    block = 8
    return pl.pallas_call(
        illiquid_kernel,
        grid_spec=pltpu.PrefetchScalarGridSpec(
            num_scalar_prefetch=1,
            grid=(kb // block,),
            in_specs=[
                pl.BlockSpec((na, depth), lambda j, *_: (0, 0)),
                pl.BlockSpec((block, na_loc, lanes), lambda j, *_: (j, 0, 0)),
                pl.BlockSpec((block, 2, lanes), lambda j, *_: (j, 0, 0)),
                pl.BlockSpec((count, lanes), lambda j, *_: (0, 0)),
                pl.BlockSpec(group.shape, lambda j, *_: (0, 0)),
            ],
            out_specs=pl.BlockSpec((group.shape[0], count), lambda j, *_: (0, 0)),
            scratch_shapes=[pltpu.VMEM((kb * na, lanes), jnp.float32), pltpu.VMEM((count, lanes), jnp.float32)],
        ),
        out_shape=jax.ShapeDtypeStruct((group.shape[0], count), jnp.float32),
        compiler_params=pltpu.CompilerParams(vmem_limit_bytes=60 * 1024 * 1024),
    )(row_index, ca, t, rim, weight, group)


def edges(values, axis, dim):
    count = lax.axis_size(axis)
    pos = lax.axis_index(axis)
    ends = count - 1
    head = lax.index_in_dim(values, 0, axis=dim, keepdims=False)
    tail = lax.index_in_dim(values, values.shape[dim] - 1, axis=dim, keepdims=False)
    below = lax.ppermute(tail, axis, [(i, (i + 1) % count) for i in range(ends)])
    above = lax.ppermute(head, axis, [((i + 1) % count, i) for i in range(ends)])
    lower = jnp.where(pos == 0, head, below).astype(jnp.float32)
    upper = jnp.where(pos == ends, tail, above).astype(jnp.float32)
    return lower, upper


def body(
    values_in,
    shock_load,
    price_field,
    rate_liquid,
    rate_illiquid,
    mask_liquid,
    mask_illiquid,
    jump_inverse,
    coef_liquid,
    coef_illiquid,
    coef_income,
    owner,
):
    high = lax.Precision.HIGH
    columns, nz_loc, na_loc, _ = values_in.shape
    wide_pos = lax.axis_index("wide")
    inc_pos = lax.axis_index("inc")
    head = values_in[:, :, 0, :].astype(jnp.float32)
    tail = values_in[:, :, na_loc - 1, :].astype(jnp.float32)
    lower, upper = edges(values_in, "wide", 2)
    table_b = cosine_constant(NB)[:KBLOW]
    liquid_part = liquid_step(
        shock_load, values_in, rate_liquid, rate_illiquid, price_field,
        mask_liquid, mask_illiquid, jnp.asarray(table_b.T),
    )
    rim = jnp.stack(
        [
            jnp.where(mask_illiquid[:, 0, :] == 0, rate_illiquid[:, 0, :] * (lower - head), 0.0),
            jnp.where(mask_illiquid[:, na_loc - 1, :] != 0, rate_illiquid[:, na_loc - 1, :] * (upper - tail), 0.0),
        ],
        axis=2,
    )
    rim = jnp.einsum("kb,czeb->czek", jnp.asarray(table_b), rim, precision=high)
    rim = jnp.transpose(rim, (3, 2, 0, 1)).reshape(KBLOW, 2, columns * nz_loc)
    liquid_part = jnp.transpose(liquid_part, (3, 2, 0, 1)).reshape(KBLOW, na_loc, columns * nz_loc)
    table_a = lax.dynamic_slice_in_dim(jnp.asarray(stacked_constant(NA)), wide_pos * na_loc, na_loc, axis=2)
    table_a = table_a.reshape(NA, 3 * na_loc)
    folded = jnp.dot(jnp.asarray(cosine_constant(NZ)), jump_inverse, precision=lax.Precision.HIGHEST)
    folded = lax.dynamic_slice_in_dim(folded, inc_pos * nz_loc, nz_loc, axis=1)
    pick_z = (coef_income[:, None] == jnp.arange(NZ, dtype=jnp.int32)[None, :]).astype(jnp.float32)
    weight = jnp.dot(pick_z, jnp.tile(folded, (1, columns)), precision=lax.Precision.HIGHEST)
    lanes = columns * nz_loc
    group = (jnp.arange(lanes)[None, :] // nz_loc == jnp.arange(columns)[:, None]).astype(jnp.bfloat16)
    partial = illiquid_pick(
        table_a, liquid_part, rim, weight, group,
        jnp.clip(coef_liquid, 0, KBLOW - 1) * NA + jnp.clip(coef_illiquid, 0, NA - 1),
    )
    kept = all_sum(partial, ("inc", "wide"))
    owners = lax.axis_size(("wide", "inc"))
    count = owner.shape[0]
    capacity = 2 * count // owners
    me = lax.axis_index(("wide", "inc"))
    seen = jnp.cumsum((owner == me).astype(jnp.int32))
    slots = jnp.arange(1, capacity + 1, dtype=jnp.int32)
    mine = jnp.sum((seen[None, :] < slots[:, None]).astype(jnp.int32), axis=1)
    gathered = jnp.take(kept, jnp.minimum(mine, count - 1), axis=1)
    return jnp.where((mine < count)[None, :], gathered, jnp.float32(0.0))


def all_sum(x, axes):
    for axis in axes:
        count = lax.axis_size(axis)
        step = 1
        while step < count:
            x = x + lax.ppermute(x, axis, [(i, i ^ step) for i in range(count)])
            step *= 2
    return x


def solution(mesh):
    placed = (
        P(("grp", "col"), "inc", "wide", None),
        P(("grp", "col")),
        P(("grp", "inc"), "wide", None),
        P(("grp", "inc"), "wide", None),
        P(("grp", "inc"), "wide", None),
        P(("grp", "inc"), "wide", None),
        P(("grp", "inc"), "wide", None),
        P("grp", None),
        P(),
        P(),
        P(),
        P(),
    )
    return jax.shard_map(
        body,
        mesh=mesh,
        in_specs=placed,
        out_specs=P(("grp", "col"), ("wide", "inc")),
        check_vma=False,
    )
```

```python
import functools
import ml_dtypes
import numpy as np
import jax
import jax.numpy as jnp
from jax import lax
from jax.experimental import pallas as pl
from jax.experimental.pallas import tpu as pltpu
from jax.sharding import PartitionSpec as P

NB = 512
NA = 256
NZ = 64
KBLOW = 128
Z_BLOCK = 8


def cosine_table(count):
    freq = jnp.arange(count, dtype=jnp.int32)[:, None]
    cell = jnp.arange(count, dtype=jnp.int32)[None, :]
    phase = (2 * cell + 1) * freq % (4 * count)
    angle = jnp.pi * phase.astype(jnp.float32) / (2.0 * count)
    first = jnp.where(freq == 0, jnp.sqrt(jnp.float32(0.5)), jnp.float32(1.0))
    return jnp.cos(angle) * jnp.sqrt(jnp.float32(2.0 / count)) * first


def cosine_constant(count):
    freq = np.arange(count)[:, None]
    cell = np.arange(count)[None, :]
    table = np.cos(np.pi * ((2 * cell + 1) * freq % (4 * count)) / (2.0 * count)) * np.sqrt(2.0 / count)
    table[0] *= np.sqrt(0.5)
    return table.astype(np.float32)


def stacked_constant(count):
    table = cosine_constant(count)
    high = table.astype(ml_dtypes.bfloat16)
    low = (table - high.astype(np.float32)).astype(ml_dtypes.bfloat16)
    return np.stack([low, high, high], axis=1)


def slot_targets(owner, owners, capacity):
    onehot = (owner[:, None] == jnp.arange(owners, dtype=jnp.int32)[None, :]).astype(jnp.int32)
    before = jnp.cumsum(onehot, axis=0) - onehot
    slot = jnp.sum(before * onehot, axis=1)
    return owner * capacity + slot


def split_bf16(x):
    hi = x.astype(jnp.bfloat16)
    return hi, (x - hi.astype(jnp.float32)).astype(jnp.bfloat16)


def step_kernel(load_ref, vals_ref, lo_ref, up_ref, rl_ref, ri_ref, pf_ref, ml_ref, mi_ref, tb_ref, out_ref):
    columns = vals_ref.shape[0]
    zb, na, nb = rl_ref.shape
    kb = tb_ref.shape[1]
    rows = zb * na
    rl = rl_ref[...].reshape(rows, nb)
    ri = ri_ref[...].reshape(rows, nb)
    pf = pf_ref[...].reshape(rows, nb)
    mb = ml_ref[...].reshape(rows, nb) != 0
    ma = mi_ref[...].reshape(rows, nb) != 0
    col = lax.broadcasted_iota(jnp.int32, (rows, nb), 1)
    arow = lax.broadcasted_iota(jnp.int32, (zb, na, nb), 1).reshape(rows, nb)
    next_b = mb & (col != nb - 1)
    prev_b = jnp.logical_not(mb) & (col != 0)
    top = arow == na - 1
    bottom = arow == 0
    th, tl = split_bf16(tb_ref[...])
    both = jnp.concatenate([th, tl], axis=1)

    def transform(x):
        hi, low = split_bf16(x)
        pair = jnp.dot(hi, both, preferred_element_type=jnp.float32)
        return jnp.dot(low, th, preferred_element_type=jnp.float32) + pair[:, kb:] + pair[:, :kb]

    price = transform(pf)

    def per_column(c, carry):
        v = vals_ref[c].reshape(rows, nb).astype(jnp.float32)
        lo = jnp.broadcast_to(lo_ref[c][:, None, :], (zb, na, nb)).reshape(rows, nb)
        up = jnp.broadcast_to(up_ref[c][:, None, :], (zb, na, nb)).reshape(rows, nb)
        side_b = jnp.where(next_b, pltpu.roll(v, nb - 1, 1), jnp.where(prev_b, pltpu.roll(v, 1, 1), v))
        above = jnp.where(top, up, pltpu.roll(v, rows - 1, 0))
        below = jnp.where(bottom, lo, pltpu.roll(v, 1, 0))
        side_a = jnp.where(ma, above, below)
        explicit = v + rl * (side_b - v) + ri * (side_a - v)
        out_ref[c] = (transform(explicit) + load_ref[c] * price).reshape(zb, na, kb)
        return carry

    lax.fori_loop(0, columns, per_column, 0)


def liquid_step(load, vals, lower, upper, rl, ri, pf, ml, mi, tb):
    columns, nz, na, nb = vals.shape
    kb = tb.shape[1]
    zb = min(Z_BLOCK, nz)
    field = pl.BlockSpec((zb, na, nb), lambda j: (j, 0, 0))
    edge = pl.BlockSpec((columns, zb, nb), lambda j: (0, j, 0))
    table = pl.BlockSpec((nb, kb), lambda j: (0, 0))
    return pl.pallas_call(
        step_kernel,
        grid=(nz // zb,),
        in_specs=[
            pl.BlockSpec(memory_space=pltpu.SMEM),
            pl.BlockSpec((columns, zb, na, nb), lambda j: (0, j, 0, 0)),
            edge,
            edge,
            field,
            field,
            field,
            field,
            field,
            table,
        ],
        out_specs=pl.BlockSpec((columns, zb, na, kb), lambda j: (0, j, 0, 0)),
        out_shape=jax.ShapeDtypeStruct((columns, nz, na, kb), jnp.float32),
        compiler_params=pltpu.CompilerParams(vmem_limit_bytes=56 * 1024 * 1024),
    )(load, vals, lower, upper, rl, ri, pf, ml, mi, tb)


def illiquid_kernel(row_ref, ca_ref, t_ref, rim_ref, w_ref, group_ref, out_ref, spectrum, picked):
    j = pl.program_id(0)
    block, na_loc, lanes = t_ref.shape
    stacked = ca_ref[...]
    row = lax.broadcasted_iota(jnp.int32, (na_loc, lanes), 0)
    for k in range(block):
        rim = rim_ref[k]
        t = t_ref[k] + jnp.where(row == 0, rim[0:1], 0.0)
        th, tl = split_bf16(t + jnp.where(row == na_loc - 1, rim[1:2], 0.0))
        rhs = jnp.concatenate([th, th, tl], axis=0)
        start = pl.multiple_of((j * block + k) * stacked.shape[0], stacked.shape[0])
        spectrum[pl.ds(start, stacked.shape[0]), :] = jnp.dot(stacked, rhs, preferred_element_type=jnp.float32)

    @pl.when(j == pl.num_programs(0) - 1)
    def _():
        def pick(i, carry):
            picked[pl.ds(i, 1), :] = spectrum[pl.ds(row_ref[i], 1), :]
            return carry

        lax.fori_loop(0, picked.shape[0], pick, 0, unroll=32)
        rest = picked[...] * w_ref[...]
        group = group_ref[...]
        total = None
        for _ in range(3):
            part = rest.astype(jnp.bfloat16)
            rest = rest - part.astype(jnp.float32)
            term = lax.dot_general(group, part, (((1,), (1,)), ((), ())), preferred_element_type=jnp.float32)
            total = term if total is None else total + term
        out_ref[...] = total


def illiquid_pick(ca, t, rim, weight, group, row_index):
    kb, na_loc, lanes = t.shape
    na, depth = ca.shape
    count = row_index.shape[0]
    block = 8
    return pl.pallas_call(
        illiquid_kernel,
        grid_spec=pltpu.PrefetchScalarGridSpec(
            num_scalar_prefetch=1,
            grid=(kb // block,),
            in_specs=[
                pl.BlockSpec((na, depth), lambda j, *_: (0, 0)),
                pl.BlockSpec((block, na_loc, lanes), lambda j, *_: (j, 0, 0)),
                pl.BlockSpec((block, 2, lanes), lambda j, *_: (j, 0, 0)),
                pl.BlockSpec((count, lanes), lambda j, *_: (0, 0)),
                pl.BlockSpec(group.shape, lambda j, *_: (0, 0)),
            ],
            out_specs=pl.BlockSpec((group.shape[0], count), lambda j, *_: (0, 0)),
            scratch_shapes=[pltpu.VMEM((kb * na, lanes), jnp.float32), pltpu.VMEM((count, lanes), jnp.float32)],
        ),
        out_shape=jax.ShapeDtypeStruct((group.shape[0], count), jnp.float32),
        compiler_params=pltpu.CompilerParams(vmem_limit_bytes=60 * 1024 * 1024),
    )(row_index, ca, t, rim, weight, group)


def edges(values, axis, dim):
    count = lax.axis_size(axis)
    pos = lax.axis_index(axis)
    ends = count - 1
    head = lax.index_in_dim(values, 0, axis=dim, keepdims=False)
    tail = lax.index_in_dim(values, values.shape[dim] - 1, axis=dim, keepdims=False)
    below = lax.ppermute(tail, axis, [(i, (i + 1) % count) for i in range(ends)])
    above = lax.ppermute(head, axis, [((i + 1) % count, i) for i in range(ends)])
    lower = jnp.where(pos == 0, head, below).astype(jnp.float32)
    upper = jnp.where(pos == ends, tail, above).astype(jnp.float32)
    return lower, upper


def body(
    values_in,
    shock_load,
    price_field,
    rate_liquid,
    rate_illiquid,
    mask_liquid,
    mask_illiquid,
    jump_inverse,
    coef_liquid,
    coef_illiquid,
    coef_income,
    owner,
):
    high = lax.Precision.HIGH
    columns, nz_loc, na_loc, _ = values_in.shape
    wide_pos = lax.axis_index("wide")
    inc_pos = lax.axis_index("inc")
    head = values_in[:, :, 0, :].astype(jnp.float32)
    tail = values_in[:, :, na_loc - 1, :].astype(jnp.float32)
    lower, upper = edges(values_in, "wide", 2)
    table_b = cosine_constant(NB)[:KBLOW]
    liquid_part = liquid_step(
        shock_load, values_in, head, tail, rate_liquid, rate_illiquid, price_field,
        mask_liquid, mask_illiquid, jnp.asarray(table_b.T),
    )
    rim = jnp.stack(
        [
            jnp.where(mask_illiquid[:, 0, :] == 0, rate_illiquid[:, 0, :] * (lower - head), 0.0),
            jnp.where(mask_illiquid[:, na_loc - 1, :] != 0, rate_illiquid[:, na_loc - 1, :] * (upper - tail), 0.0),
        ],
        axis=2,
    )
    rim = jnp.einsum("kb,czeb->czek", jnp.asarray(table_b), rim, precision=high)
    rim = jnp.transpose(rim, (3, 2, 0, 1)).reshape(KBLOW, 2, columns * nz_loc)
    liquid_part = jnp.transpose(liquid_part, (3, 2, 0, 1)).reshape(KBLOW, na_loc, columns * nz_loc)
    table_a = lax.dynamic_slice_in_dim(jnp.asarray(stacked_constant(NA)), wide_pos * na_loc, na_loc, axis=2)
    table_a = table_a.reshape(NA, 3 * na_loc)
    folded = jnp.dot(jnp.asarray(cosine_constant(NZ)), jump_inverse, precision=lax.Precision.HIGHEST)
    folded = lax.dynamic_slice_in_dim(folded, inc_pos * nz_loc, nz_loc, axis=1)
    pick_z = (coef_income[:, None] == jnp.arange(NZ, dtype=jnp.int32)[None, :]).astype(jnp.float32)
    weight = jnp.dot(pick_z, jnp.tile(folded, (1, columns)), precision=lax.Precision.HIGHEST)
    lanes = columns * nz_loc
    group = (jnp.arange(lanes)[None, :] // nz_loc == jnp.arange(columns)[:, None]).astype(jnp.bfloat16)
    partial = illiquid_pick(
        table_a, liquid_part, rim, weight, group,
        jnp.clip(coef_liquid, 0, KBLOW - 1) * NA + jnp.clip(coef_illiquid, 0, NA - 1),
    )
    kept = all_sum(partial, ("inc", "wide"))
    owners = lax.axis_size(("wide", "inc"))
    count = owner.shape[0]
    capacity = 2 * count // owners
    me = lax.axis_index(("wide", "inc"))
    seen = jnp.cumsum((owner == me).astype(jnp.int32))
    slots = jnp.arange(1, capacity + 1, dtype=jnp.int32)
    mine = jnp.sum((seen[None, :] < slots[:, None]).astype(jnp.int32), axis=1)
    gathered = jnp.take(kept, jnp.minimum(mine, count - 1), axis=1)
    return jnp.where((mine < count)[None, :], gathered, jnp.float32(0.0))


def all_sum(x, axes):
    for axis in axes:
        count = lax.axis_size(axis)
        step = 1
        while step < count:
            x = x + lax.ppermute(x, axis, [(i, i ^ step) for i in range(count)])
            step *= 2
    return x


def solution(mesh):
    placed = (
        P(("grp", "col"), "inc", "wide", None),
        P(("grp", "col")),
        P(("grp", "inc"), "wide", None),
        P(("grp", "inc"), "wide", None),
        P(("grp", "inc"), "wide", None),
        P(("grp", "inc"), "wide", None),
        P(("grp", "inc"), "wide", None),
        P("grp", None),
        P(),
        P(),
        P(),
        P(),
    )
    return jax.shard_map(
        body,
        mesh=mesh,
        in_specs=placed,
        out_specs=P(("grp", "col"), ("wide", "inc")),
        check_vma=False,
    )
```

```python
import functools
import ml_dtypes
import numpy as np
import jax
import jax.numpy as jnp
from jax import lax
from jax.experimental import pallas as pl
from jax.experimental.pallas import tpu as pltpu
from jax.sharding import PartitionSpec as P

NB = 512
NA = 256
NZ = 64
KBLOW = 128
Z_BLOCK = 8


def cosine_table(count):
    freq = jnp.arange(count, dtype=jnp.int32)[:, None]
    cell = jnp.arange(count, dtype=jnp.int32)[None, :]
    phase = (2 * cell + 1) * freq % (4 * count)
    angle = jnp.pi * phase.astype(jnp.float32) / (2.0 * count)
    first = jnp.where(freq == 0, jnp.sqrt(jnp.float32(0.5)), jnp.float32(1.0))
    return jnp.cos(angle) * jnp.sqrt(jnp.float32(2.0 / count)) * first


def cosine_constant(count):
    freq = np.arange(count)[:, None]
    cell = np.arange(count)[None, :]
    table = np.cos(np.pi * ((2 * cell + 1) * freq % (4 * count)) / (2.0 * count)) * np.sqrt(2.0 / count)
    table[0] *= np.sqrt(0.5)
    return table.astype(np.float32)


def stacked_constant(count):
    table = cosine_constant(count)
    high = table.astype(ml_dtypes.bfloat16)
    low = (table - high.astype(np.float32)).astype(ml_dtypes.bfloat16)
    return np.stack([low, high, high], axis=1)


def slot_targets(owner, owners, capacity):
    onehot = (owner[:, None] == jnp.arange(owners, dtype=jnp.int32)[None, :]).astype(jnp.int32)
    before = jnp.cumsum(onehot, axis=0) - onehot
    slot = jnp.sum(before * onehot, axis=1)
    return owner * capacity + slot


def split_bf16(x):
    hi = x.astype(jnp.bfloat16)
    return hi, (x - hi.astype(jnp.float32)).astype(jnp.bfloat16)


def step_kernel(load_ref, vals_ref, lo_ref, up_ref, rl_ref, ri_ref, pf_ref, ml_ref, mi_ref, tb_ref, out_ref):
    columns = vals_ref.shape[0]
    zb, na, nb = rl_ref.shape
    kb = tb_ref.shape[1]
    rows = zb * na
    rl = rl_ref[...].reshape(rows, nb)
    ri = ri_ref[...].reshape(rows, nb)
    pf = pf_ref[...].reshape(rows, nb)
    mb = ml_ref[...].reshape(rows, nb) != 0
    ma = mi_ref[...].reshape(rows, nb) != 0
    col = lax.broadcasted_iota(jnp.int32, (rows, nb), 1)
    arow = lax.broadcasted_iota(jnp.int32, (zb, na, nb), 1).reshape(rows, nb)
    next_b = mb & (col != nb - 1)
    prev_b = jnp.logical_not(mb) & (col != 0)
    top = arow == na - 1
    bottom = arow == 0
    th, tl = split_bf16(tb_ref[...])
    both = jnp.concatenate(
        [jnp.concatenate([th, tl], axis=1), jnp.concatenate([th, jnp.zeros_like(tl)], axis=1)], axis=0
    )

    def transform(x):
        hi, low = split_bf16(x)
        pair = jnp.dot(jnp.concatenate([hi, low], axis=1), both, preferred_element_type=jnp.float32)
        return pair[:, kb:] + pair[:, :kb]

    price = transform(pf)

    def per_column(c, carry):
        v = vals_ref[c].reshape(rows, nb).astype(jnp.float32)
        lo = jnp.broadcast_to(lo_ref[c][:, None, :], (zb, na, nb)).reshape(rows, nb)
        up = jnp.broadcast_to(up_ref[c][:, None, :], (zb, na, nb)).reshape(rows, nb)
        side_b = jnp.where(next_b, pltpu.roll(v, nb - 1, 1), jnp.where(prev_b, pltpu.roll(v, 1, 1), v))
        above = jnp.where(top, up, pltpu.roll(v, rows - 1, 0))
        below = jnp.where(bottom, lo, pltpu.roll(v, 1, 0))
        side_a = jnp.where(ma, above, below)
        explicit = v + rl * (side_b - v) + ri * (side_a - v)
        out_ref[c] = (transform(explicit) + load_ref[c] * price).reshape(zb, na, kb)
        return carry

    lax.fori_loop(0, columns, per_column, 0)


def liquid_step(load, vals, lower, upper, rl, ri, pf, ml, mi, tb):
    columns, nz, na, nb = vals.shape
    kb = tb.shape[1]
    zb = min(Z_BLOCK, nz)
    field = pl.BlockSpec((zb, na, nb), lambda j: (j, 0, 0))
    edge = pl.BlockSpec((columns, zb, nb), lambda j: (0, j, 0))
    table = pl.BlockSpec((nb, kb), lambda j: (0, 0))
    return pl.pallas_call(
        step_kernel,
        grid=(nz // zb,),
        in_specs=[
            pl.BlockSpec(memory_space=pltpu.SMEM),
            pl.BlockSpec((columns, zb, na, nb), lambda j: (0, j, 0, 0)),
            edge,
            edge,
            field,
            field,
            field,
            field,
            field,
            table,
        ],
        out_specs=pl.BlockSpec((columns, zb, na, kb), lambda j: (0, j, 0, 0)),
        out_shape=jax.ShapeDtypeStruct((columns, nz, na, kb), jnp.float32),
        compiler_params=pltpu.CompilerParams(vmem_limit_bytes=56 * 1024 * 1024),
    )(load, vals, lower, upper, rl, ri, pf, ml, mi, tb)


def illiquid_kernel(row_ref, ca_ref, t_ref, rim_ref, w_ref, group_ref, out_ref, spectrum, picked):
    j = pl.program_id(0)
    block, na_loc, lanes = t_ref.shape
    stacked = ca_ref[...]
    row = lax.broadcasted_iota(jnp.int32, (na_loc, lanes), 0)
    for k in range(block):
        rim = rim_ref[k]
        t = t_ref[k] + jnp.where(row == 0, rim[0:1], 0.0)
        th, tl = split_bf16(t + jnp.where(row == na_loc - 1, rim[1:2], 0.0))
        rhs = jnp.concatenate([th, th, tl], axis=0)
        start = pl.multiple_of((j * block + k) * stacked.shape[0], stacked.shape[0])
        spectrum[pl.ds(start, stacked.shape[0]), :] = jnp.dot(stacked, rhs, preferred_element_type=jnp.float32)

    @pl.when(j == pl.num_programs(0) - 1)
    def _():
        def pick(i, carry):
            picked[pl.ds(i, 1), :] = spectrum[pl.ds(row_ref[i], 1), :]
            return carry

        lax.fori_loop(0, picked.shape[0], pick, 0, unroll=32)
        rest = picked[...] * w_ref[...]
        group = group_ref[...]
        total = None
        for _ in range(3):
            part = rest.astype(jnp.bfloat16)
            rest = rest - part.astype(jnp.float32)
            term = lax.dot_general(group, part, (((1,), (1,)), ((), ())), preferred_element_type=jnp.float32)
            total = term if total is None else total + term
        out_ref[...] = total


def illiquid_pick(ca, t, rim, weight, group, row_index):
    kb, na_loc, lanes = t.shape
    na, depth = ca.shape
    count = row_index.shape[0]
    block = 8
    return pl.pallas_call(
        illiquid_kernel,
        grid_spec=pltpu.PrefetchScalarGridSpec(
            num_scalar_prefetch=1,
            grid=(kb // block,),
            in_specs=[
                pl.BlockSpec((na, depth), lambda j, *_: (0, 0)),
                pl.BlockSpec((block, na_loc, lanes), lambda j, *_: (j, 0, 0)),
                pl.BlockSpec((block, 2, lanes), lambda j, *_: (j, 0, 0)),
                pl.BlockSpec((count, lanes), lambda j, *_: (0, 0)),
                pl.BlockSpec(group.shape, lambda j, *_: (0, 0)),
            ],
            out_specs=pl.BlockSpec((group.shape[0], count), lambda j, *_: (0, 0)),
            scratch_shapes=[pltpu.VMEM((kb * na, lanes), jnp.float32), pltpu.VMEM((count, lanes), jnp.float32)],
        ),
        out_shape=jax.ShapeDtypeStruct((group.shape[0], count), jnp.float32),
        compiler_params=pltpu.CompilerParams(vmem_limit_bytes=60 * 1024 * 1024),
    )(row_index, ca, t, rim, weight, group)


def edges(values, axis, dim):
    count = lax.axis_size(axis)
    pos = lax.axis_index(axis)
    ends = count - 1
    head = lax.index_in_dim(values, 0, axis=dim, keepdims=False)
    tail = lax.index_in_dim(values, values.shape[dim] - 1, axis=dim, keepdims=False)
    below = lax.ppermute(tail, axis, [(i, (i + 1) % count) for i in range(ends)])
    above = lax.ppermute(head, axis, [((i + 1) % count, i) for i in range(ends)])
    lower = jnp.where(pos == 0, head, below).astype(jnp.float32)
    upper = jnp.where(pos == ends, tail, above).astype(jnp.float32)
    return lower, upper


def body(
    values_in,
    shock_load,
    price_field,
    rate_liquid,
    rate_illiquid,
    mask_liquid,
    mask_illiquid,
    jump_inverse,
    coef_liquid,
    coef_illiquid,
    coef_income,
    owner,
):
    high = lax.Precision.HIGH
    columns, nz_loc, na_loc, _ = values_in.shape
    wide_pos = lax.axis_index("wide")
    inc_pos = lax.axis_index("inc")
    head = values_in[:, :, 0, :].astype(jnp.float32)
    tail = values_in[:, :, na_loc - 1, :].astype(jnp.float32)
    lower, upper = edges(values_in, "wide", 2)
    table_b = cosine_constant(NB)[:KBLOW]
    liquid_part = liquid_step(
        shock_load, values_in, head, tail, rate_liquid, rate_illiquid, price_field,
        mask_liquid, mask_illiquid, jnp.asarray(table_b.T),
    )
    rim = jnp.stack(
        [
            jnp.where(mask_illiquid[:, 0, :] == 0, rate_illiquid[:, 0, :] * (lower - head), 0.0),
            jnp.where(mask_illiquid[:, na_loc - 1, :] != 0, rate_illiquid[:, na_loc - 1, :] * (upper - tail), 0.0),
        ],
        axis=2,
    )
    rim = jnp.einsum("kb,czeb->czek", jnp.asarray(table_b), rim, precision=high)
    rim = jnp.transpose(rim, (3, 2, 0, 1)).reshape(KBLOW, 2, columns * nz_loc)
    liquid_part = jnp.transpose(liquid_part, (3, 2, 0, 1)).reshape(KBLOW, na_loc, columns * nz_loc)
    table_a = lax.dynamic_slice_in_dim(jnp.asarray(stacked_constant(NA)), wide_pos * na_loc, na_loc, axis=2)
    table_a = table_a.reshape(NA, 3 * na_loc)
    folded = jnp.dot(jnp.asarray(cosine_constant(NZ)), jump_inverse, precision=lax.Precision.HIGHEST)
    folded = lax.dynamic_slice_in_dim(folded, inc_pos * nz_loc, nz_loc, axis=1)
    pick_z = (coef_income[:, None] == jnp.arange(NZ, dtype=jnp.int32)[None, :]).astype(jnp.float32)
    weight = jnp.dot(pick_z, jnp.tile(folded, (1, columns)), precision=lax.Precision.HIGHEST)
    lanes = columns * nz_loc
    group = (jnp.arange(lanes)[None, :] // nz_loc == jnp.arange(columns)[:, None]).astype(jnp.bfloat16)
    partial = illiquid_pick(
        table_a, liquid_part, rim, weight, group,
        jnp.clip(coef_liquid, 0, KBLOW - 1) * NA + jnp.clip(coef_illiquid, 0, NA - 1),
    )
    kept = all_sum(partial, ("inc", "wide"))
    owners = lax.axis_size(("wide", "inc"))
    count = owner.shape[0]
    capacity = 2 * count // owners
    me = lax.axis_index(("wide", "inc"))
    seen = jnp.cumsum((owner == me).astype(jnp.int32))
    slots = jnp.arange(1, capacity + 1, dtype=jnp.int32)
    mine = jnp.sum((seen[None, :] < slots[:, None]).astype(jnp.int32), axis=1)
    gathered = jnp.take(kept, jnp.minimum(mine, count - 1), axis=1)
    return jnp.where((mine < count)[None, :], gathered, jnp.float32(0.0))


def all_sum(x, axes):
    for axis in axes:
        count = lax.axis_size(axis)
        step = 1
        while step < count:
            x = x + lax.ppermute(x, axis, [(i, i ^ step) for i in range(count)])
            step *= 2
    return x


def solution(mesh):
    placed = (
        P(("grp", "col"), "inc", "wide", None),
        P(("grp", "col")),
        P(("grp", "inc"), "wide", None),
        P(("grp", "inc"), "wide", None),
        P(("grp", "inc"), "wide", None),
        P(("grp", "inc"), "wide", None),
        P(("grp", "inc"), "wide", None),
        P("grp", None),
        P(),
        P(),
        P(),
        P(),
    )
    return jax.shard_map(
        body,
        mesh=mesh,
        in_specs=placed,
        out_specs=P(("grp", "col"), ("wide", "inc")),
        check_vma=False,
    )
```

```python
import functools
import ml_dtypes
import numpy as np
import jax
import jax.numpy as jnp
from jax import lax
from jax.experimental import pallas as pl
from jax.experimental.pallas import tpu as pltpu
from jax.sharding import PartitionSpec as P

NB = 512
NA = 256
NZ = 64
KBLOW = 128
Z_BLOCK = 8


def cosine_table(count):
    freq = jnp.arange(count, dtype=jnp.int32)[:, None]
    cell = jnp.arange(count, dtype=jnp.int32)[None, :]
    phase = (2 * cell + 1) * freq % (4 * count)
    angle = jnp.pi * phase.astype(jnp.float32) / (2.0 * count)
    first = jnp.where(freq == 0, jnp.sqrt(jnp.float32(0.5)), jnp.float32(1.0))
    return jnp.cos(angle) * jnp.sqrt(jnp.float32(2.0 / count)) * first


def cosine_constant(count):
    freq = np.arange(count)[:, None]
    cell = np.arange(count)[None, :]
    table = np.cos(np.pi * ((2 * cell + 1) * freq % (4 * count)) / (2.0 * count)) * np.sqrt(2.0 / count)
    table[0] *= np.sqrt(0.5)
    return table.astype(np.float32)


def stacked_constant(count):
    table = cosine_constant(count)
    high = table.astype(ml_dtypes.bfloat16)
    low = (table - high.astype(np.float32)).astype(ml_dtypes.bfloat16)
    return np.stack([low, high, high], axis=1)


def slot_targets(owner, owners, capacity):
    onehot = (owner[:, None] == jnp.arange(owners, dtype=jnp.int32)[None, :]).astype(jnp.int32)
    before = jnp.cumsum(onehot, axis=0) - onehot
    slot = jnp.sum(before * onehot, axis=1)
    return owner * capacity + slot


def split_bf16(x):
    hi = x.astype(jnp.bfloat16)
    return hi, (x - hi.astype(jnp.float32)).astype(jnp.bfloat16)


def step_kernel(load_ref, vals_ref, lo_ref, up_ref, rl_ref, ri_ref, pf_ref, ml_ref, mi_ref, tb_ref, out_ref):
    columns = vals_ref.shape[0]
    zb, na, nb = rl_ref.shape
    kb = tb_ref.shape[1]
    rows = zb * na
    rl = rl_ref[...].reshape(rows, nb)
    ri = ri_ref[...].reshape(rows, nb)
    pf = pf_ref[...].reshape(rows, nb)
    mb = ml_ref[...].reshape(rows, nb) != 0
    ma = mi_ref[...].reshape(rows, nb) != 0
    col = lax.broadcasted_iota(jnp.int32, (rows, nb), 1)
    arow = lax.broadcasted_iota(jnp.int32, (zb, na, nb), 1).reshape(rows, nb)
    next_b = mb & (col != nb - 1)
    prev_b = jnp.logical_not(mb) & (col != 0)
    top = arow == na - 1
    bottom = arow == 0
    th, tl = split_bf16(tb_ref[...])
    both = jnp.concatenate([th, tl], axis=1)

    def transform(x):
        hi, low = split_bf16(x)
        pair = jnp.dot(hi, both, preferred_element_type=jnp.float32)
        return jnp.dot(low, th, preferred_element_type=jnp.float32) + pair[:, kb:] + pair[:, :kb]

    price = transform(pf)

    def per_column(c, carry):
        v = vals_ref[c].reshape(rows, nb).astype(jnp.float32)
        lo = jnp.broadcast_to(lo_ref[c][:, None, :], (zb, na, nb)).reshape(rows, nb)
        up = jnp.broadcast_to(up_ref[c][:, None, :], (zb, na, nb)).reshape(rows, nb)
        side_b = jnp.where(next_b, pltpu.roll(v, nb - 1, 1), jnp.where(prev_b, pltpu.roll(v, 1, 1), v))
        above = jnp.where(top, up, pltpu.roll(v, rows - 1, 0))
        below = jnp.where(bottom, lo, pltpu.roll(v, 1, 0))
        side_a = jnp.where(ma, above, below)
        explicit = v + rl * (side_b - v) + ri * (side_a - v)
        out_ref[c] = (transform(explicit) + load_ref[c] * price).reshape(zb, na, kb)
        return carry

    lax.fori_loop(0, columns, per_column, 0)


def liquid_step(load, vals, lower, upper, rl, ri, pf, ml, mi, tb):
    columns, nz, na, nb = vals.shape
    kb = tb.shape[1]
    zb = min(Z_BLOCK, nz)
    field = pl.BlockSpec((zb, na, nb), lambda j: (j, 0, 0))
    edge = pl.BlockSpec((columns, zb, nb), lambda j: (0, j, 0))
    table = pl.BlockSpec((nb, kb), lambda j: (0, 0))
    return pl.pallas_call(
        step_kernel,
        grid=(nz // zb,),
        in_specs=[
            pl.BlockSpec(memory_space=pltpu.SMEM),
            pl.BlockSpec((columns, zb, na, nb), lambda j: (0, j, 0, 0)),
            edge,
            edge,
            field,
            field,
            field,
            field,
            field,
            table,
        ],
        out_specs=pl.BlockSpec((columns, zb, na, kb), lambda j: (0, j, 0, 0)),
        out_shape=jax.ShapeDtypeStruct((columns, nz, na, kb), jnp.float32),
        compiler_params=pltpu.CompilerParams(vmem_limit_bytes=56 * 1024 * 1024),
    )(load, vals, lower, upper, rl, ri, pf, ml, mi, tb)


def illiquid_kernel(row_ref, ca_ref, t_ref, rim_ref, w_ref, group_ref, out_ref, spectrum, picked):
    j = pl.program_id(0)
    block, na_loc, lanes = t_ref.shape
    stacked = ca_ref[...]
    row = lax.broadcasted_iota(jnp.int32, (na_loc, lanes), 0)
    for k in range(block):
        rim = rim_ref[k]
        t = t_ref[k] + jnp.where(row == 0, rim[0:1], 0.0)
        th, tl = split_bf16(t + jnp.where(row == na_loc - 1, rim[1:2], 0.0))
        rhs = jnp.concatenate([th, th, tl], axis=0)
        start = pl.multiple_of((j * block + k) * stacked.shape[0], stacked.shape[0])
        spectrum[pl.ds(start, stacked.shape[0]), :] = jnp.dot(stacked, rhs, preferred_element_type=jnp.float32)

    @pl.when(j == pl.num_programs(0) - 1)
    def _():
        def pick(i, carry):
            picked[pl.ds(i, 1), :] = spectrum[pl.ds(row_ref[i], 1), :]
            return carry

        lax.fori_loop(0, picked.shape[0], pick, 0, unroll=32)
        rest = picked[...] * w_ref[...]
        group = group_ref[...]
        total = None
        for _ in range(3):
            part = rest.astype(jnp.bfloat16)
            rest = rest - part.astype(jnp.float32)
            term = lax.dot_general(group, part, (((1,), (1,)), ((), ())), preferred_element_type=jnp.float32)
            total = term if total is None else total + term
        out_ref[...] = total


def illiquid_pick(ca, t, rim, weight, group, row_index):
    kb, na_loc, lanes = t.shape
    na, depth = ca.shape
    count = row_index.shape[0]
    block = 16
    return pl.pallas_call(
        illiquid_kernel,
        grid_spec=pltpu.PrefetchScalarGridSpec(
            num_scalar_prefetch=1,
            grid=(kb // block,),
            in_specs=[
                pl.BlockSpec((na, depth), lambda j, *_: (0, 0)),
                pl.BlockSpec((block, na_loc, lanes), lambda j, *_: (j, 0, 0)),
                pl.BlockSpec((block, 2, lanes), lambda j, *_: (j, 0, 0)),
                pl.BlockSpec((count, lanes), lambda j, *_: (0, 0)),
                pl.BlockSpec(group.shape, lambda j, *_: (0, 0)),
            ],
            out_specs=pl.BlockSpec((group.shape[0], count), lambda j, *_: (0, 0)),
            scratch_shapes=[pltpu.VMEM((kb * na, lanes), jnp.float32), pltpu.VMEM((count, lanes), jnp.float32)],
        ),
        out_shape=jax.ShapeDtypeStruct((group.shape[0], count), jnp.float32),
        compiler_params=pltpu.CompilerParams(vmem_limit_bytes=60 * 1024 * 1024),
    )(row_index, ca, t, rim, weight, group)


def edges(values, axis, dim):
    count = lax.axis_size(axis)
    pos = lax.axis_index(axis)
    ends = count - 1
    head = lax.index_in_dim(values, 0, axis=dim, keepdims=False)
    tail = lax.index_in_dim(values, values.shape[dim] - 1, axis=dim, keepdims=False)
    below = lax.ppermute(tail, axis, [(i, (i + 1) % count) for i in range(ends)])
    above = lax.ppermute(head, axis, [((i + 1) % count, i) for i in range(ends)])
    lower = jnp.where(pos == 0, head, below).astype(jnp.float32)
    upper = jnp.where(pos == ends, tail, above).astype(jnp.float32)
    return lower, upper


def body(
    values_in,
    shock_load,
    price_field,
    rate_liquid,
    rate_illiquid,
    mask_liquid,
    mask_illiquid,
    jump_inverse,
    coef_liquid,
    coef_illiquid,
    coef_income,
    owner,
):
    high = lax.Precision.HIGH
    columns, nz_loc, na_loc, _ = values_in.shape
    wide_pos = lax.axis_index("wide")
    inc_pos = lax.axis_index("inc")
    head = values_in[:, :, 0, :].astype(jnp.float32)
    tail = values_in[:, :, na_loc - 1, :].astype(jnp.float32)
    lower, upper = edges(values_in, "wide", 2)
    table_b = cosine_constant(NB)[:KBLOW]
    liquid_part = liquid_step(
        shock_load, values_in, head, tail, rate_liquid, rate_illiquid, price_field,
        mask_liquid, mask_illiquid, jnp.asarray(table_b.T),
    )
    rim = jnp.stack(
        [
            jnp.where(mask_illiquid[:, 0, :] == 0, rate_illiquid[:, 0, :] * (lower - head), 0.0),
            jnp.where(mask_illiquid[:, na_loc - 1, :] != 0, rate_illiquid[:, na_loc - 1, :] * (upper - tail), 0.0),
        ],
        axis=2,
    )
    rim = jnp.einsum("kb,czeb->czek", jnp.asarray(table_b), rim, precision=high)
    rim = jnp.transpose(rim, (3, 2, 0, 1)).reshape(KBLOW, 2, columns * nz_loc)
    liquid_part = jnp.transpose(liquid_part, (3, 2, 0, 1)).reshape(KBLOW, na_loc, columns * nz_loc)
    table_a = lax.dynamic_slice_in_dim(jnp.asarray(stacked_constant(NA)), wide_pos * na_loc, na_loc, axis=2)
    table_a = table_a.reshape(NA, 3 * na_loc)
    folded = jnp.dot(jnp.asarray(cosine_constant(NZ)), jump_inverse, precision=lax.Precision.HIGHEST)
    folded = lax.dynamic_slice_in_dim(folded, inc_pos * nz_loc, nz_loc, axis=1)
    pick_z = (coef_income[:, None] == jnp.arange(NZ, dtype=jnp.int32)[None, :]).astype(jnp.float32)
    weight = jnp.dot(pick_z, jnp.tile(folded, (1, columns)), precision=lax.Precision.HIGHEST)
    lanes = columns * nz_loc
    group = (jnp.arange(lanes)[None, :] // nz_loc == jnp.arange(columns)[:, None]).astype(jnp.bfloat16)
    partial = illiquid_pick(
        table_a, liquid_part, rim, weight, group,
        jnp.clip(coef_liquid, 0, KBLOW - 1) * NA + jnp.clip(coef_illiquid, 0, NA - 1),
    )
    kept = all_sum(partial, ("inc", "wide"))
    owners = lax.axis_size(("wide", "inc"))
    count = owner.shape[0]
    capacity = 2 * count // owners
    me = lax.axis_index(("wide", "inc"))
    seen = jnp.cumsum((owner == me).astype(jnp.int32))
    slots = jnp.arange(1, capacity + 1, dtype=jnp.int32)
    mine = jnp.sum((seen[None, :] < slots[:, None]).astype(jnp.int32), axis=1)
    gathered = jnp.take(kept, jnp.minimum(mine, count - 1), axis=1)
    return jnp.where((mine < count)[None, :], gathered, jnp.float32(0.0))


def all_sum(x, axes):
    for axis in axes:
        count = lax.axis_size(axis)
        step = 1
        while step < count:
            x = x + lax.ppermute(x, axis, [(i, i ^ step) for i in range(count)])
            step *= 2
    return x


def solution(mesh):
    placed = (
        P(("grp", "col"), "inc", "wide", None),
        P(("grp", "col")),
        P(("grp", "inc"), "wide", None),
        P(("grp", "inc"), "wide", None),
        P(("grp", "inc"), "wide", None),
        P(("grp", "inc"), "wide", None),
        P(("grp", "inc"), "wide", None),
        P("grp", None),
        P(),
        P(),
        P(),
        P(),
    )
    return jax.shard_map(
        body,
        mesh=mesh,
        in_specs=placed,
        out_specs=P(("grp", "col"), ("wide", "inc")),
        check_vma=False,
    )
```

```python
import functools
import ml_dtypes
import numpy as np
import jax
import jax.numpy as jnp
from jax import lax
from jax.experimental import pallas as pl
from jax.experimental.pallas import tpu as pltpu
from jax.sharding import PartitionSpec as P

NB = 512
NA = 256
NZ = 64
KBLOW = 128
Z_BLOCK = 8


def cosine_table(count):
    freq = jnp.arange(count, dtype=jnp.int32)[:, None]
    cell = jnp.arange(count, dtype=jnp.int32)[None, :]
    phase = (2 * cell + 1) * freq % (4 * count)
    angle = jnp.pi * phase.astype(jnp.float32) / (2.0 * count)
    first = jnp.where(freq == 0, jnp.sqrt(jnp.float32(0.5)), jnp.float32(1.0))
    return jnp.cos(angle) * jnp.sqrt(jnp.float32(2.0 / count)) * first


def cosine_constant(count):
    freq = np.arange(count)[:, None]
    cell = np.arange(count)[None, :]
    table = np.cos(np.pi * ((2 * cell + 1) * freq % (4 * count)) / (2.0 * count)) * np.sqrt(2.0 / count)
    table[0] *= np.sqrt(0.5)
    return table.astype(np.float32)


def stacked_constant(count):
    table = cosine_constant(count)
    high = table.astype(ml_dtypes.bfloat16)
    low = (table - high.astype(np.float32)).astype(ml_dtypes.bfloat16)
    return np.stack([low, high, high], axis=1)


def slot_targets(owner, owners, capacity):
    onehot = (owner[:, None] == jnp.arange(owners, dtype=jnp.int32)[None, :]).astype(jnp.int32)
    before = jnp.cumsum(onehot, axis=0) - onehot
    slot = jnp.sum(before * onehot, axis=1)
    return owner * capacity + slot


def split_bf16(x):
    hi = x.astype(jnp.bfloat16)
    return hi, (x - hi.astype(jnp.float32)).astype(jnp.bfloat16)


def step_kernel(load_ref, vals_ref, lo_ref, up_ref, rl_ref, ri_ref, pf_ref, ml_ref, mi_ref, tb_ref, out_ref):
    columns = vals_ref.shape[0]
    zb, na, nb = rl_ref.shape
    kb = tb_ref.shape[1]
    rows = zb * na
    rl = rl_ref[...].reshape(rows, nb)
    ri = ri_ref[...].reshape(rows, nb)
    pf = pf_ref[...].reshape(rows, nb)
    mb = ml_ref[...].reshape(rows, nb) != 0
    ma = mi_ref[...].reshape(rows, nb) != 0
    col = lax.broadcasted_iota(jnp.int32, (rows, nb), 1)
    arow = lax.broadcasted_iota(jnp.int32, (zb, na, nb), 1).reshape(rows, nb)
    next_b = mb & (col != nb - 1)
    prev_b = jnp.logical_not(mb) & (col != 0)
    top = arow == na - 1
    bottom = arow == 0
    th, tl = split_bf16(tb_ref[...])
    both = jnp.concatenate([th, tl], axis=1)

    def transform(x):
        hi, low = split_bf16(x)
        pair = jnp.dot(hi, both, preferred_element_type=jnp.float32)
        return jnp.dot(low, th, preferred_element_type=jnp.float32) + pair[:, kb:] + pair[:, :kb]

    price = transform(pf)

    def per_column(c, carry):
        v = vals_ref[c].reshape(rows, nb).astype(jnp.float32)
        lo = jnp.broadcast_to(lo_ref[c][:, None, :], (zb, na, nb)).reshape(rows, nb)
        up = jnp.broadcast_to(up_ref[c][:, None, :], (zb, na, nb)).reshape(rows, nb)
        side_b = jnp.where(next_b, pltpu.roll(v, nb - 1, 1), jnp.where(prev_b, pltpu.roll(v, 1, 1), v))
        above = jnp.where(top, up, pltpu.roll(v, rows - 1, 0))
        below = jnp.where(bottom, lo, pltpu.roll(v, 1, 0))
        side_a = jnp.where(ma, above, below)
        explicit = v + rl * (side_b - v) + ri * (side_a - v)
        out_ref[c] = (transform(explicit) + load_ref[c] * price).reshape(zb, na, kb)
        return carry

    lax.fori_loop(0, columns, per_column, 0)


def liquid_step(load, vals, lower, upper, rl, ri, pf, ml, mi, tb):
    columns, nz, na, nb = vals.shape
    kb = tb.shape[1]
    zb = min(Z_BLOCK, nz)
    field = pl.BlockSpec((zb, na, nb), lambda j: (j, 0, 0))
    edge = pl.BlockSpec((columns, zb, nb), lambda j: (0, j, 0))
    table = pl.BlockSpec((nb, kb), lambda j: (0, 0))
    return pl.pallas_call(
        step_kernel,
        grid=(nz // zb,),
        in_specs=[
            pl.BlockSpec(memory_space=pltpu.SMEM),
            pl.BlockSpec((columns, zb, na, nb), lambda j: (0, j, 0, 0)),
            edge,
            edge,
            field,
            field,
            field,
            field,
            field,
            table,
        ],
        out_specs=pl.BlockSpec((columns, zb, na, kb), lambda j: (0, j, 0, 0)),
        out_shape=jax.ShapeDtypeStruct((columns, nz, na, kb), jnp.float32),
        compiler_params=pltpu.CompilerParams(vmem_limit_bytes=56 * 1024 * 1024),
    )(load, vals, lower, upper, rl, ri, pf, ml, mi, tb)


def illiquid_kernel(row_ref, ca_ref, t_ref, rim_ref, w_ref, group_ref, out_ref, spectrum, picked):
    j = pl.program_id(0)
    block, na_loc, lanes = t_ref.shape
    stacked = ca_ref[...]
    row = lax.broadcasted_iota(jnp.int32, (na_loc, lanes), 0)
    for k in range(block):
        rim = rim_ref[k]
        t = t_ref[k] + jnp.where(row == 0, rim[0:1], 0.0)
        th, tl = split_bf16(t + jnp.where(row == na_loc - 1, rim[1:2], 0.0))
        rhs = jnp.concatenate([th, th, tl], axis=0)
        start = pl.multiple_of((j * block + k) * stacked.shape[0], stacked.shape[0])
        spectrum[pl.ds(start, stacked.shape[0]), :] = jnp.dot(stacked, rhs, preferred_element_type=jnp.float32)

    @pl.when(j == pl.num_programs(0) - 1)
    def _():
        def pick(i, carry):
            picked[pl.ds(i, 1), :] = spectrum[pl.ds(row_ref[i], 1), :]
            return carry

        lax.fori_loop(0, picked.shape[0], pick, 0, unroll=32)
        rest = picked[...] * w_ref[...]
        group = group_ref[...]
        total = None
        for _ in range(3):
            part = rest.astype(jnp.bfloat16)
            rest = rest - part.astype(jnp.float32)
            term = lax.dot_general(group, part, (((1,), (1,)), ((), ())), preferred_element_type=jnp.float32)
            total = term if total is None else total + term
        out_ref[...] = total


def illiquid_pick(ca, t, rim, weight, group, row_index):
    kb, na_loc, lanes = t.shape
    na, depth = ca.shape
    count = row_index.shape[0]
    block = 32
    return pl.pallas_call(
        illiquid_kernel,
        grid_spec=pltpu.PrefetchScalarGridSpec(
            num_scalar_prefetch=1,
            grid=(kb // block,),
            in_specs=[
                pl.BlockSpec((na, depth), lambda j, *_: (0, 0)),
                pl.BlockSpec((block, na_loc, lanes), lambda j, *_: (j, 0, 0)),
                pl.BlockSpec((block, 2, lanes), lambda j, *_: (j, 0, 0)),
                pl.BlockSpec((count, lanes), lambda j, *_: (0, 0)),
                pl.BlockSpec(group.shape, lambda j, *_: (0, 0)),
            ],
            out_specs=pl.BlockSpec((group.shape[0], count), lambda j, *_: (0, 0)),
            scratch_shapes=[pltpu.VMEM((kb * na, lanes), jnp.float32), pltpu.VMEM((count, lanes), jnp.float32)],
        ),
        out_shape=jax.ShapeDtypeStruct((group.shape[0], count), jnp.float32),
        compiler_params=pltpu.CompilerParams(vmem_limit_bytes=60 * 1024 * 1024),
    )(row_index, ca, t, rim, weight, group)


def edges(values, axis, dim):
    count = lax.axis_size(axis)
    pos = lax.axis_index(axis)
    ends = count - 1
    head = lax.index_in_dim(values, 0, axis=dim, keepdims=False)
    tail = lax.index_in_dim(values, values.shape[dim] - 1, axis=dim, keepdims=False)
    below = lax.ppermute(tail, axis, [(i, (i + 1) % count) for i in range(ends)])
    above = lax.ppermute(head, axis, [((i + 1) % count, i) for i in range(ends)])
    lower = jnp.where(pos == 0, head, below).astype(jnp.float32)
    upper = jnp.where(pos == ends, tail, above).astype(jnp.float32)
    return lower, upper


def body(
    values_in,
    shock_load,
    price_field,
    rate_liquid,
    rate_illiquid,
    mask_liquid,
    mask_illiquid,
    jump_inverse,
    coef_liquid,
    coef_illiquid,
    coef_income,
    owner,
):
    high = lax.Precision.HIGH
    columns, nz_loc, na_loc, _ = values_in.shape
    wide_pos = lax.axis_index("wide")
    inc_pos = lax.axis_index("inc")
    head = values_in[:, :, 0, :].astype(jnp.float32)
    tail = values_in[:, :, na_loc - 1, :].astype(jnp.float32)
    lower, upper = edges(values_in, "wide", 2)
    table_b = cosine_constant(NB)[:KBLOW]
    liquid_part = liquid_step(
        shock_load, values_in, head, tail, rate_liquid, rate_illiquid, price_field,
        mask_liquid, mask_illiquid, jnp.asarray(table_b.T),
    )
    rim = jnp.stack(
        [
            jnp.where(mask_illiquid[:, 0, :] == 0, rate_illiquid[:, 0, :] * (lower - head), 0.0),
            jnp.where(mask_illiquid[:, na_loc - 1, :] != 0, rate_illiquid[:, na_loc - 1, :] * (upper - tail), 0.0),
        ],
        axis=2,
    )
    rim = jnp.einsum("kb,czeb->czek", jnp.asarray(table_b), rim, precision=high)
    rim = jnp.transpose(rim, (3, 2, 0, 1)).reshape(KBLOW, 2, columns * nz_loc)
    liquid_part = jnp.transpose(liquid_part, (3, 2, 0, 1)).reshape(KBLOW, na_loc, columns * nz_loc)
    table_a = lax.dynamic_slice_in_dim(jnp.asarray(stacked_constant(NA)), wide_pos * na_loc, na_loc, axis=2)
    table_a = table_a.reshape(NA, 3 * na_loc)
    folded = jnp.dot(jnp.asarray(cosine_constant(NZ)), jump_inverse, precision=lax.Precision.HIGHEST)
    folded = lax.dynamic_slice_in_dim(folded, inc_pos * nz_loc, nz_loc, axis=1)
    pick_z = (coef_income[:, None] == jnp.arange(NZ, dtype=jnp.int32)[None, :]).astype(jnp.float32)
    weight = jnp.dot(pick_z, jnp.tile(folded, (1, columns)), precision=lax.Precision.HIGHEST)
    lanes = columns * nz_loc
    group = (jnp.arange(lanes)[None, :] // nz_loc == jnp.arange(columns)[:, None]).astype(jnp.bfloat16)
    partial = illiquid_pick(
        table_a, liquid_part, rim, weight, group,
        jnp.clip(coef_liquid, 0, KBLOW - 1) * NA + jnp.clip(coef_illiquid, 0, NA - 1),
    )
    kept = all_sum(partial, ("inc", "wide"))
    owners = lax.axis_size(("wide", "inc"))
    count = owner.shape[0]
    capacity = 2 * count // owners
    me = lax.axis_index(("wide", "inc"))
    seen = jnp.cumsum((owner == me).astype(jnp.int32))
    slots = jnp.arange(1, capacity + 1, dtype=jnp.int32)
    mine = jnp.sum((seen[None, :] < slots[:, None]).astype(jnp.int32), axis=1)
    gathered = jnp.take(kept, jnp.minimum(mine, count - 1), axis=1)
    return jnp.where((mine < count)[None, :], gathered, jnp.float32(0.0))


def all_sum(x, axes):
    for axis in axes:
        count = lax.axis_size(axis)
        step = 1
        while step < count:
            x = x + lax.ppermute(x, axis, [(i, i ^ step) for i in range(count)])
            step *= 2
    return x


def solution(mesh):
    placed = (
        P(("grp", "col"), "inc", "wide", None),
        P(("grp", "col")),
        P(("grp", "inc"), "wide", None),
        P(("grp", "inc"), "wide", None),
        P(("grp", "inc"), "wide", None),
        P(("grp", "inc"), "wide", None),
        P(("grp", "inc"), "wide", None),
        P("grp", None),
        P(),
        P(),
        P(),
        P(),
    )
    return jax.shard_map(
        body,
        mesh=mesh,
        in_specs=placed,
        out_specs=P(("grp", "col"), ("wide", "inc")),
        check_vma=False,
    )
```

```python
import functools
import ml_dtypes
import numpy as np
import jax
import jax.numpy as jnp
from jax import lax
from jax.experimental import pallas as pl
from jax.experimental.pallas import tpu as pltpu
from jax.sharding import PartitionSpec as P

NB = 512
NA = 256
NZ = 64
KBLOW = 128
Z_BLOCK = 8


def cosine_table(count):
    freq = jnp.arange(count, dtype=jnp.int32)[:, None]
    cell = jnp.arange(count, dtype=jnp.int32)[None, :]
    phase = (2 * cell + 1) * freq % (4 * count)
    angle = jnp.pi * phase.astype(jnp.float32) / (2.0 * count)
    first = jnp.where(freq == 0, jnp.sqrt(jnp.float32(0.5)), jnp.float32(1.0))
    return jnp.cos(angle) * jnp.sqrt(jnp.float32(2.0 / count)) * first


def cosine_constant(count):
    freq = np.arange(count)[:, None]
    cell = np.arange(count)[None, :]
    table = np.cos(np.pi * ((2 * cell + 1) * freq % (4 * count)) / (2.0 * count)) * np.sqrt(2.0 / count)
    table[0] *= np.sqrt(0.5)
    return table.astype(np.float32)


def stacked_constant(count):
    table = cosine_constant(count)
    high = table.astype(ml_dtypes.bfloat16)
    low = (table - high.astype(np.float32)).astype(ml_dtypes.bfloat16)
    return np.stack([low, high, high], axis=1)


def slot_targets(owner, owners, capacity):
    onehot = (owner[:, None] == jnp.arange(owners, dtype=jnp.int32)[None, :]).astype(jnp.int32)
    before = jnp.cumsum(onehot, axis=0) - onehot
    slot = jnp.sum(before * onehot, axis=1)
    return owner * capacity + slot


def split_bf16(x):
    hi = x.astype(jnp.bfloat16)
    return hi, (x - hi.astype(jnp.float32)).astype(jnp.bfloat16)


def step_kernel(load_ref, vals_ref, lo_ref, up_ref, rl_ref, ri_ref, pf_ref, ml_ref, mi_ref, tb_ref, out_ref):
    columns = vals_ref.shape[0]
    zb, na, nb = rl_ref.shape
    kb = tb_ref.shape[1]
    rows = zb * na
    rl = rl_ref[...].reshape(rows, nb)
    ri = ri_ref[...].reshape(rows, nb)
    pf = pf_ref[...].reshape(rows, nb)
    mb = ml_ref[...].reshape(rows, nb) != 0
    ma = mi_ref[...].reshape(rows, nb) != 0
    col = lax.broadcasted_iota(jnp.int32, (rows, nb), 1)
    arow = lax.broadcasted_iota(jnp.int32, (zb, na, nb), 1).reshape(rows, nb)
    next_b = mb & (col != nb - 1)
    prev_b = jnp.logical_not(mb) & (col != 0)
    top = arow == na - 1
    bottom = arow == 0
    th, tl = split_bf16(tb_ref[...])
    both = jnp.concatenate([th, tl], axis=1)

    def transform(x):
        hi, low = split_bf16(x)
        pair = jnp.dot(hi, both, preferred_element_type=jnp.float32)
        return jnp.dot(low, th, preferred_element_type=jnp.float32) + pair[:, kb:] + pair[:, :kb]

    price = transform(pf)

    def per_column(c, carry):
        v = vals_ref[c].reshape(rows, nb).astype(jnp.float32)
        lo = jnp.broadcast_to(lo_ref[c][:, None, :], (zb, na, nb)).reshape(rows, nb)
        up = jnp.broadcast_to(up_ref[c][:, None, :], (zb, na, nb)).reshape(rows, nb)
        side_b = jnp.where(next_b, pltpu.roll(v, nb - 1, 1), jnp.where(prev_b, pltpu.roll(v, 1, 1), v))
        above = jnp.where(top, up, pltpu.roll(v, rows - 1, 0))
        below = jnp.where(bottom, lo, pltpu.roll(v, 1, 0))
        side_a = jnp.where(ma, above, below)
        explicit = v + rl * (side_b - v) + ri * (side_a - v)
        out_ref[c] = (transform(explicit) + load_ref[c] * price).reshape(zb, na, kb)
        return carry

    lax.fori_loop(0, columns, per_column, 0)


def liquid_step(load, vals, lower, upper, rl, ri, pf, ml, mi, tb):
    columns, nz, na, nb = vals.shape
    kb = tb.shape[1]
    zb = min(Z_BLOCK, nz)
    field = pl.BlockSpec((zb, na, nb), lambda j: (j, 0, 0))
    edge = pl.BlockSpec((columns, zb, nb), lambda j: (0, j, 0))
    table = pl.BlockSpec((nb, kb), lambda j: (0, 0))
    return pl.pallas_call(
        step_kernel,
        grid=(nz // zb,),
        in_specs=[
            pl.BlockSpec(memory_space=pltpu.SMEM),
            pl.BlockSpec((columns, zb, na, nb), lambda j: (0, j, 0, 0)),
            edge,
            edge,
            field,
            field,
            field,
            field,
            field,
            table,
        ],
        out_specs=pl.BlockSpec((columns, zb, na, kb), lambda j: (0, j, 0, 0)),
        out_shape=jax.ShapeDtypeStruct((columns, nz, na, kb), jnp.float32),
        compiler_params=pltpu.CompilerParams(vmem_limit_bytes=56 * 1024 * 1024),
    )(load, vals, lower, upper, rl, ri, pf, ml, mi, tb)


def illiquid_kernel(row_ref, ca_ref, t_ref, rim_ref, w_ref, group_ref, out_ref, spectrum, picked):
    j = pl.program_id(0)
    block, na_loc, lanes = t_ref.shape
    stacked = ca_ref[...]
    row = lax.broadcasted_iota(jnp.int32, (na_loc, lanes), 0)
    for k in range(block):
        rim = rim_ref[k]
        t = t_ref[k] + jnp.where(row == 0, rim[0:1], 0.0)
        th, tl = split_bf16(t + jnp.where(row == na_loc - 1, rim[1:2], 0.0))
        rhs = jnp.concatenate([th, th, tl], axis=0)
        start = pl.multiple_of((j * block + k) * stacked.shape[0], stacked.shape[0])
        spectrum[pl.ds(start, stacked.shape[0]), :] = jnp.dot(stacked, rhs, preferred_element_type=jnp.float32)

    @pl.when(j == pl.num_programs(0) - 1)
    def _():
        def pick(i, carry):
            picked[pl.ds(i, 1), :] = spectrum[pl.ds(row_ref[i], 1), :]
            return carry

        lax.fori_loop(0, picked.shape[0], pick, 0, unroll=32)
        rest = picked[...] * w_ref[...]
        group = group_ref[...]
        total = None
        for _ in range(3):
            part = rest.astype(jnp.bfloat16)
            rest = rest - part.astype(jnp.float32)
            term = lax.dot_general(group, part, (((1,), (1,)), ((), ())), preferred_element_type=jnp.float32)
            total = term if total is None else total + term
        out_ref[...] = total


def illiquid_pick(ca, t, rim, weight, group, row_index):
    kb, na_loc, lanes = t.shape
    na, depth = ca.shape
    count = row_index.shape[0]
    block = 64
    return pl.pallas_call(
        illiquid_kernel,
        grid_spec=pltpu.PrefetchScalarGridSpec(
            num_scalar_prefetch=1,
            grid=(kb // block,),
            in_specs=[
                pl.BlockSpec((na, depth), lambda j, *_: (0, 0)),
                pl.BlockSpec((block, na_loc, lanes), lambda j, *_: (j, 0, 0)),
                pl.BlockSpec((block, 2, lanes), lambda j, *_: (j, 0, 0)),
                pl.BlockSpec((count, lanes), lambda j, *_: (0, 0)),
                pl.BlockSpec(group.shape, lambda j, *_: (0, 0)),
            ],
            out_specs=pl.BlockSpec((group.shape[0], count), lambda j, *_: (0, 0)),
            scratch_shapes=[pltpu.VMEM((kb * na, lanes), jnp.float32), pltpu.VMEM((count, lanes), jnp.float32)],
        ),
        out_shape=jax.ShapeDtypeStruct((group.shape[0], count), jnp.float32),
        compiler_params=pltpu.CompilerParams(vmem_limit_bytes=60 * 1024 * 1024),
    )(row_index, ca, t, rim, weight, group)


def edges(values, axis, dim):
    count = lax.axis_size(axis)
    pos = lax.axis_index(axis)
    ends = count - 1
    head = lax.index_in_dim(values, 0, axis=dim, keepdims=False)
    tail = lax.index_in_dim(values, values.shape[dim] - 1, axis=dim, keepdims=False)
    below = lax.ppermute(tail, axis, [(i, (i + 1) % count) for i in range(ends)])
    above = lax.ppermute(head, axis, [((i + 1) % count, i) for i in range(ends)])
    lower = jnp.where(pos == 0, head, below).astype(jnp.float32)
    upper = jnp.where(pos == ends, tail, above).astype(jnp.float32)
    return lower, upper


def body(
    values_in,
    shock_load,
    price_field,
    rate_liquid,
    rate_illiquid,
    mask_liquid,
    mask_illiquid,
    jump_inverse,
    coef_liquid,
    coef_illiquid,
    coef_income,
    owner,
):
    high = lax.Precision.HIGH
    columns, nz_loc, na_loc, _ = values_in.shape
    wide_pos = lax.axis_index("wide")
    inc_pos = lax.axis_index("inc")
    head = values_in[:, :, 0, :].astype(jnp.float32)
    tail = values_in[:, :, na_loc - 1, :].astype(jnp.float32)
    lower, upper = edges(values_in, "wide", 2)
    table_b = cosine_constant(NB)[:KBLOW]
    liquid_part = liquid_step(
        shock_load, values_in, head, tail, rate_liquid, rate_illiquid, price_field,
        mask_liquid, mask_illiquid, jnp.asarray(table_b.T),
    )
    rim = jnp.stack(
        [
            jnp.where(mask_illiquid[:, 0, :] == 0, rate_illiquid[:, 0, :] * (lower - head), 0.0),
            jnp.where(mask_illiquid[:, na_loc - 1, :] != 0, rate_illiquid[:, na_loc - 1, :] * (upper - tail), 0.0),
        ],
        axis=2,
    )
    rim = jnp.einsum("kb,czeb->czek", jnp.asarray(table_b), rim, precision=high)
    rim = jnp.transpose(rim, (3, 2, 0, 1)).reshape(KBLOW, 2, columns * nz_loc)
    liquid_part = jnp.transpose(liquid_part, (3, 2, 0, 1)).reshape(KBLOW, na_loc, columns * nz_loc)
    table_a = lax.dynamic_slice_in_dim(jnp.asarray(stacked_constant(NA)), wide_pos * na_loc, na_loc, axis=2)
    table_a = table_a.reshape(NA, 3 * na_loc)
    folded = jnp.dot(jnp.asarray(cosine_constant(NZ)), jump_inverse, precision=lax.Precision.HIGHEST)
    folded = lax.dynamic_slice_in_dim(folded, inc_pos * nz_loc, nz_loc, axis=1)
    pick_z = (coef_income[:, None] == jnp.arange(NZ, dtype=jnp.int32)[None, :]).astype(jnp.float32)
    weight = jnp.dot(pick_z, jnp.tile(folded, (1, columns)), precision=lax.Precision.HIGHEST)
    lanes = columns * nz_loc
    group = (jnp.arange(lanes)[None, :] // nz_loc == jnp.arange(columns)[:, None]).astype(jnp.bfloat16)
    partial = illiquid_pick(
        table_a, liquid_part, rim, weight, group,
        jnp.clip(coef_liquid, 0, KBLOW - 1) * NA + jnp.clip(coef_illiquid, 0, NA - 1),
    )
    kept = all_sum(partial, ("inc", "wide"))
    owners = lax.axis_size(("wide", "inc"))
    count = owner.shape[0]
    capacity = 2 * count // owners
    me = lax.axis_index(("wide", "inc"))
    seen = jnp.cumsum((owner == me).astype(jnp.int32))
    slots = jnp.arange(1, capacity + 1, dtype=jnp.int32)
    mine = jnp.sum((seen[None, :] < slots[:, None]).astype(jnp.int32), axis=1)
    gathered = jnp.take(kept, jnp.minimum(mine, count - 1), axis=1)
    return jnp.where((mine < count)[None, :], gathered, jnp.float32(0.0))


def all_sum(x, axes):
    for axis in axes:
        count = lax.axis_size(axis)
        step = 1
        while step < count:
            x = x + lax.ppermute(x, axis, [(i, i ^ step) for i in range(count)])
            step *= 2
    return x


def solution(mesh):
    placed = (
        P(("grp", "col"), "inc", "wide", None),
        P(("grp", "col")),
        P(("grp", "inc"), "wide", None),
        P(("grp", "inc"), "wide", None),
        P(("grp", "inc"), "wide", None),
        P(("grp", "inc"), "wide", None),
        P(("grp", "inc"), "wide", None),
        P("grp", None),
        P(),
        P(),
        P(),
        P(),
    )
    return jax.shard_map(
        body,
        mesh=mesh,
        in_specs=placed,
        out_specs=P(("grp", "col"), ("wide", "inc")),
        check_vma=False,
    )
```

```python
import functools
import ml_dtypes
import numpy as np
import jax
import jax.numpy as jnp
from jax import lax
from jax.experimental import pallas as pl
from jax.experimental.pallas import tpu as pltpu
from jax.sharding import PartitionSpec as P

NB = 512
NA = 256
NZ = 64
KBLOW = 128
Z_BLOCK = 8


def cosine_table(count):
    freq = jnp.arange(count, dtype=jnp.int32)[:, None]
    cell = jnp.arange(count, dtype=jnp.int32)[None, :]
    phase = (2 * cell + 1) * freq % (4 * count)
    angle = jnp.pi * phase.astype(jnp.float32) / (2.0 * count)
    first = jnp.where(freq == 0, jnp.sqrt(jnp.float32(0.5)), jnp.float32(1.0))
    return jnp.cos(angle) * jnp.sqrt(jnp.float32(2.0 / count)) * first


def cosine_constant(count):
    freq = np.arange(count)[:, None]
    cell = np.arange(count)[None, :]
    table = np.cos(np.pi * ((2 * cell + 1) * freq % (4 * count)) / (2.0 * count)) * np.sqrt(2.0 / count)
    table[0] *= np.sqrt(0.5)
    return table.astype(np.float32)


def stacked_constant(count):
    table = cosine_constant(count)
    high = table.astype(ml_dtypes.bfloat16)
    low = (table - high.astype(np.float32)).astype(ml_dtypes.bfloat16)
    return np.stack([low, high, high], axis=1)


def slot_targets(owner, owners, capacity):
    onehot = (owner[:, None] == jnp.arange(owners, dtype=jnp.int32)[None, :]).astype(jnp.int32)
    before = jnp.cumsum(onehot, axis=0) - onehot
    slot = jnp.sum(before * onehot, axis=1)
    return owner * capacity + slot


def split_bf16(x):
    hi = x.astype(jnp.bfloat16)
    return hi, (x - hi.astype(jnp.float32)).astype(jnp.bfloat16)


def step_kernel(load_ref, vals_ref, lo_ref, up_ref, rl_ref, ri_ref, pf_ref, ml_ref, mi_ref, tb_ref, out_ref):
    columns = vals_ref.shape[0]
    zb, na, nb = rl_ref.shape
    kb = tb_ref.shape[1]
    rows = zb * na
    rl = rl_ref[...].reshape(rows, nb)
    ri = ri_ref[...].reshape(rows, nb)
    pf = pf_ref[...].reshape(rows, nb)
    mb = ml_ref[...].reshape(rows, nb) != 0
    ma = mi_ref[...].reshape(rows, nb) != 0
    col = lax.broadcasted_iota(jnp.int32, (rows, nb), 1)
    arow = lax.broadcasted_iota(jnp.int32, (zb, na, nb), 1).reshape(rows, nb)
    next_b = mb & (col != nb - 1)
    prev_b = jnp.logical_not(mb) & (col != 0)
    top = arow == na - 1
    bottom = arow == 0
    th, tl = split_bf16(tb_ref[...])
    both = jnp.concatenate([th, tl], axis=1)

    def transform(x):
        hi, low = split_bf16(x)
        pair = jnp.dot(hi, both, preferred_element_type=jnp.float32)
        return jnp.dot(low, th, preferred_element_type=jnp.float32) + pair[:, kb:] + pair[:, :kb]

    price = transform(pf)

    def per_column(c, carry):
        v = vals_ref[c].reshape(rows, nb).astype(jnp.float32)
        lo = jnp.broadcast_to(lo_ref[c][:, None, :], (zb, na, nb)).reshape(rows, nb)
        up = jnp.broadcast_to(up_ref[c][:, None, :], (zb, na, nb)).reshape(rows, nb)
        side_b = jnp.where(next_b, pltpu.roll(v, nb - 1, 1), jnp.where(prev_b, pltpu.roll(v, 1, 1), v))
        above = jnp.where(top, up, pltpu.roll(v, rows - 1, 0))
        below = jnp.where(bottom, lo, pltpu.roll(v, 1, 0))
        side_a = jnp.where(ma, above, below)
        explicit = v + rl * (side_b - v) + ri * (side_a - v)
        out_ref[c] = (transform(explicit) + load_ref[c] * price).reshape(zb, na, kb)
        return carry

    lax.fori_loop(0, columns, per_column, 0)


def liquid_step(load, vals, lower, upper, rl, ri, pf, ml, mi, tb):
    columns, nz, na, nb = vals.shape
    kb = tb.shape[1]
    zb = min(Z_BLOCK, nz)
    field = pl.BlockSpec((zb, na, nb), lambda j: (j, 0, 0))
    edge = pl.BlockSpec((columns, zb, nb), lambda j: (0, j, 0))
    table = pl.BlockSpec((nb, kb), lambda j: (0, 0))
    return pl.pallas_call(
        step_kernel,
        grid=(nz // zb,),
        in_specs=[
            pl.BlockSpec(memory_space=pltpu.SMEM),
            pl.BlockSpec((columns, zb, na, nb), lambda j: (0, j, 0, 0)),
            edge,
            edge,
            field,
            field,
            field,
            field,
            field,
            table,
        ],
        out_specs=pl.BlockSpec((columns, zb, na, kb), lambda j: (0, j, 0, 0)),
        out_shape=jax.ShapeDtypeStruct((columns, nz, na, kb), jnp.float32),
        compiler_params=pltpu.CompilerParams(vmem_limit_bytes=56 * 1024 * 1024),
    )(load, vals, lower, upper, rl, ri, pf, ml, mi, tb)


def illiquid_kernel(row_ref, ca_ref, t_ref, rim_ref, w_ref, group_ref, out_ref, spectrum, picked):
    j = pl.program_id(0)
    block, na_loc, lanes = t_ref.shape
    stacked = ca_ref[...]
    row = lax.broadcasted_iota(jnp.int32, (na_loc, lanes), 0)
    for k in range(block):
        rim = rim_ref[k]
        t = t_ref[k] + jnp.where(row == 0, rim[0:1], 0.0)
        th, tl = split_bf16(t + jnp.where(row == na_loc - 1, rim[1:2], 0.0))
        rhs = jnp.concatenate([th, th, tl], axis=0)
        start = pl.multiple_of((j * block + k) * stacked.shape[0], stacked.shape[0])
        spectrum[pl.ds(start, stacked.shape[0]), :] = jnp.dot(stacked, rhs, preferred_element_type=jnp.float32)

    @pl.when(j == pl.num_programs(0) - 1)
    def _():
        def pick(i, carry):
            picked[pl.ds(i, 1), :] = spectrum[pl.ds(row_ref[i], 1), :]
            return carry

        lax.fori_loop(0, picked.shape[0], pick, 0, unroll=64)
        rest = picked[...] * w_ref[...]
        group = group_ref[...]
        total = None
        for _ in range(3):
            part = rest.astype(jnp.bfloat16)
            rest = rest - part.astype(jnp.float32)
            term = lax.dot_general(group, part, (((1,), (1,)), ((), ())), preferred_element_type=jnp.float32)
            total = term if total is None else total + term
        out_ref[...] = total


def illiquid_pick(ca, t, rim, weight, group, row_index):
    kb, na_loc, lanes = t.shape
    na, depth = ca.shape
    count = row_index.shape[0]
    block = 32
    return pl.pallas_call(
        illiquid_kernel,
        grid_spec=pltpu.PrefetchScalarGridSpec(
            num_scalar_prefetch=1,
            grid=(kb // block,),
            in_specs=[
                pl.BlockSpec((na, depth), lambda j, *_: (0, 0)),
                pl.BlockSpec((block, na_loc, lanes), lambda j, *_: (j, 0, 0)),
                pl.BlockSpec((block, 2, lanes), lambda j, *_: (j, 0, 0)),
                pl.BlockSpec((count, lanes), lambda j, *_: (0, 0)),
                pl.BlockSpec(group.shape, lambda j, *_: (0, 0)),
            ],
            out_specs=pl.BlockSpec((group.shape[0], count), lambda j, *_: (0, 0)),
            scratch_shapes=[pltpu.VMEM((kb * na, lanes), jnp.float32), pltpu.VMEM((count, lanes), jnp.float32)],
        ),
        out_shape=jax.ShapeDtypeStruct((group.shape[0], count), jnp.float32),
        compiler_params=pltpu.CompilerParams(vmem_limit_bytes=60 * 1024 * 1024),
    )(row_index, ca, t, rim, weight, group)


def edges(values, axis, dim):
    count = lax.axis_size(axis)
    pos = lax.axis_index(axis)
    ends = count - 1
    head = lax.index_in_dim(values, 0, axis=dim, keepdims=False)
    tail = lax.index_in_dim(values, values.shape[dim] - 1, axis=dim, keepdims=False)
    below = lax.ppermute(tail, axis, [(i, (i + 1) % count) for i in range(ends)])
    above = lax.ppermute(head, axis, [((i + 1) % count, i) for i in range(ends)])
    lower = jnp.where(pos == 0, head, below).astype(jnp.float32)
    upper = jnp.where(pos == ends, tail, above).astype(jnp.float32)
    return lower, upper


def body(
    values_in,
    shock_load,
    price_field,
    rate_liquid,
    rate_illiquid,
    mask_liquid,
    mask_illiquid,
    jump_inverse,
    coef_liquid,
    coef_illiquid,
    coef_income,
    owner,
):
    high = lax.Precision.HIGH
    columns, nz_loc, na_loc, _ = values_in.shape
    wide_pos = lax.axis_index("wide")
    inc_pos = lax.axis_index("inc")
    head = values_in[:, :, 0, :].astype(jnp.float32)
    tail = values_in[:, :, na_loc - 1, :].astype(jnp.float32)
    lower, upper = edges(values_in, "wide", 2)
    table_b = cosine_constant(NB)[:KBLOW]
    liquid_part = liquid_step(
        shock_load, values_in, head, tail, rate_liquid, rate_illiquid, price_field,
        mask_liquid, mask_illiquid, jnp.asarray(table_b.T),
    )
    rim = jnp.stack(
        [
            jnp.where(mask_illiquid[:, 0, :] == 0, rate_illiquid[:, 0, :] * (lower - head), 0.0),
            jnp.where(mask_illiquid[:, na_loc - 1, :] != 0, rate_illiquid[:, na_loc - 1, :] * (upper - tail), 0.0),
        ],
        axis=2,
    )
    rim = jnp.einsum("kb,czeb->czek", jnp.asarray(table_b), rim, precision=high)
    rim = jnp.transpose(rim, (3, 2, 0, 1)).reshape(KBLOW, 2, columns * nz_loc)
    liquid_part = jnp.transpose(liquid_part, (3, 2, 0, 1)).reshape(KBLOW, na_loc, columns * nz_loc)
    table_a = lax.dynamic_slice_in_dim(jnp.asarray(stacked_constant(NA)), wide_pos * na_loc, na_loc, axis=2)
    table_a = table_a.reshape(NA, 3 * na_loc)
    folded = jnp.dot(jnp.asarray(cosine_constant(NZ)), jump_inverse, precision=lax.Precision.HIGHEST)
    folded = lax.dynamic_slice_in_dim(folded, inc_pos * nz_loc, nz_loc, axis=1)
    pick_z = (coef_income[:, None] == jnp.arange(NZ, dtype=jnp.int32)[None, :]).astype(jnp.float32)
    weight = jnp.dot(pick_z, jnp.tile(folded, (1, columns)), precision=lax.Precision.HIGHEST)
    lanes = columns * nz_loc
    group = (jnp.arange(lanes)[None, :] // nz_loc == jnp.arange(columns)[:, None]).astype(jnp.bfloat16)
    partial = illiquid_pick(
        table_a, liquid_part, rim, weight, group,
        jnp.clip(coef_liquid, 0, KBLOW - 1) * NA + jnp.clip(coef_illiquid, 0, NA - 1),
    )
    kept = all_sum(partial, ("inc", "wide"))
    owners = lax.axis_size(("wide", "inc"))
    count = owner.shape[0]
    capacity = 2 * count // owners
    me = lax.axis_index(("wide", "inc"))
    seen = jnp.cumsum((owner == me).astype(jnp.int32))
    slots = jnp.arange(1, capacity + 1, dtype=jnp.int32)
    mine = jnp.sum((seen[None, :] < slots[:, None]).astype(jnp.int32), axis=1)
    gathered = jnp.take(kept, jnp.minimum(mine, count - 1), axis=1)
    return jnp.where((mine < count)[None, :], gathered, jnp.float32(0.0))


def all_sum(x, axes):
    for axis in axes:
        count = lax.axis_size(axis)
        step = 1
        while step < count:
            x = x + lax.ppermute(x, axis, [(i, i ^ step) for i in range(count)])
            step *= 2
    return x


def solution(mesh):
    placed = (
        P(("grp", "col"), "inc", "wide", None),
        P(("grp", "col")),
        P(("grp", "inc"), "wide", None),
        P(("grp", "inc"), "wide", None),
        P(("grp", "inc"), "wide", None),
        P(("grp", "inc"), "wide", None),
        P(("grp", "inc"), "wide", None),
        P("grp", None),
        P(),
        P(),
        P(),
        P(),
    )
    return jax.shard_map(
        body,
        mesh=mesh,
        in_specs=placed,
        out_specs=P(("grp", "col"), ("wide", "inc")),
        check_vma=False,
    )
```

```python
import functools
import ml_dtypes
import numpy as np
import jax
import jax.numpy as jnp
from jax import lax
from jax.experimental import pallas as pl
from jax.experimental.pallas import tpu as pltpu
from jax.sharding import PartitionSpec as P

NB = 512
NA = 256
NZ = 64
KBLOW = 128
Z_BLOCK = 8


def cosine_table(count):
    freq = jnp.arange(count, dtype=jnp.int32)[:, None]
    cell = jnp.arange(count, dtype=jnp.int32)[None, :]
    phase = (2 * cell + 1) * freq % (4 * count)
    angle = jnp.pi * phase.astype(jnp.float32) / (2.0 * count)
    first = jnp.where(freq == 0, jnp.sqrt(jnp.float32(0.5)), jnp.float32(1.0))
    return jnp.cos(angle) * jnp.sqrt(jnp.float32(2.0 / count)) * first


def cosine_constant(count):
    freq = np.arange(count)[:, None]
    cell = np.arange(count)[None, :]
    table = np.cos(np.pi * ((2 * cell + 1) * freq % (4 * count)) / (2.0 * count)) * np.sqrt(2.0 / count)
    table[0] *= np.sqrt(0.5)
    return table.astype(np.float32)


def stacked_constant(count):
    table = cosine_constant(count)
    high = table.astype(ml_dtypes.bfloat16)
    low = (table - high.astype(np.float32)).astype(ml_dtypes.bfloat16)
    return np.stack([low, high, high], axis=1)


def slot_targets(owner, owners, capacity):
    onehot = (owner[:, None] == jnp.arange(owners, dtype=jnp.int32)[None, :]).astype(jnp.int32)
    before = jnp.cumsum(onehot, axis=0) - onehot
    slot = jnp.sum(before * onehot, axis=1)
    return owner * capacity + slot


def split_bf16(x):
    hi = x.astype(jnp.bfloat16)
    return hi, (x - hi.astype(jnp.float32)).astype(jnp.bfloat16)


def step_kernel(load_ref, vals_ref, lo_ref, up_ref, rl_ref, ri_ref, pf_ref, ml_ref, mi_ref, tb_ref, out_ref):
    columns = vals_ref.shape[0]
    zb, na, nb = rl_ref.shape
    kb = tb_ref.shape[1]
    rows = zb * na
    rl = rl_ref[...].reshape(rows, nb)
    ri = ri_ref[...].reshape(rows, nb)
    pf = pf_ref[...].reshape(rows, nb)
    mb = ml_ref[...].reshape(rows, nb) != 0
    ma = mi_ref[...].reshape(rows, nb) != 0
    col = lax.broadcasted_iota(jnp.int32, (rows, nb), 1)
    arow = lax.broadcasted_iota(jnp.int32, (zb, na, nb), 1).reshape(rows, nb)
    next_b = mb & (col != nb - 1)
    prev_b = jnp.logical_not(mb) & (col != 0)
    top = arow == na - 1
    bottom = arow == 0
    th, tl = split_bf16(tb_ref[...])
    both = jnp.concatenate([th, tl], axis=1)

    def transform(x):
        hi, low = split_bf16(x)
        pair = jnp.dot(hi, both, preferred_element_type=jnp.float32)
        return jnp.dot(low, th, preferred_element_type=jnp.float32) + pair[:, kb:] + pair[:, :kb]

    price = transform(pf)

    def per_column(c, carry):
        v = vals_ref[c].reshape(rows, nb).astype(jnp.float32)
        lo = jnp.broadcast_to(lo_ref[c][:, None, :], (zb, na, nb)).reshape(rows, nb)
        up = jnp.broadcast_to(up_ref[c][:, None, :], (zb, na, nb)).reshape(rows, nb)
        side_b = jnp.where(next_b, pltpu.roll(v, nb - 1, 1), jnp.where(prev_b, pltpu.roll(v, 1, 1), v))
        above = jnp.where(top, up, pltpu.roll(v, rows - 1, 0))
        below = jnp.where(bottom, lo, pltpu.roll(v, 1, 0))
        side_a = jnp.where(ma, above, below)
        explicit = v + rl * (side_b - v) + ri * (side_a - v)
        out_ref[c] = (transform(explicit) + load_ref[c] * price).reshape(zb, na, kb)
        return carry

    lax.fori_loop(0, columns, per_column, 0)


def liquid_step(load, vals, lower, upper, rl, ri, pf, ml, mi, tb):
    columns, nz, na, nb = vals.shape
    kb = tb.shape[1]
    zb = min(Z_BLOCK, nz)
    field = pl.BlockSpec((zb, na, nb), lambda j: (j, 0, 0))
    edge = pl.BlockSpec((columns, zb, nb), lambda j: (0, j, 0))
    table = pl.BlockSpec((nb, kb), lambda j: (0, 0))
    return pl.pallas_call(
        step_kernel,
        grid=(nz // zb,),
        in_specs=[
            pl.BlockSpec(memory_space=pltpu.SMEM),
            pl.BlockSpec((columns, zb, na, nb), lambda j: (0, j, 0, 0)),
            edge,
            edge,
            field,
            field,
            field,
            field,
            field,
            table,
        ],
        out_specs=pl.BlockSpec((columns, zb, na, kb), lambda j: (0, j, 0, 0)),
        out_shape=jax.ShapeDtypeStruct((columns, nz, na, kb), jnp.float32),
        compiler_params=pltpu.CompilerParams(vmem_limit_bytes=56 * 1024 * 1024),
    )(load, vals, lower, upper, rl, ri, pf, ml, mi, tb)


def illiquid_kernel(row_ref, ca_ref, t_ref, rim_ref, w_ref, group_ref, out_ref, spectrum, picked):
    j = pl.program_id(0)
    block, na_loc, lanes = t_ref.shape
    stacked = ca_ref[...]
    row = lax.broadcasted_iota(jnp.int32, (na_loc, lanes), 0)
    for k in range(block):
        rim = rim_ref[k]
        t = t_ref[k] + jnp.where(row == 0, rim[0:1], 0.0)
        th, tl = split_bf16(t + jnp.where(row == na_loc - 1, rim[1:2], 0.0))
        rhs = jnp.concatenate([th, th, tl], axis=0)
        start = pl.multiple_of((j * block + k) * stacked.shape[0], stacked.shape[0])
        spectrum[pl.ds(start, stacked.shape[0]), :] = jnp.dot(stacked, rhs, preferred_element_type=jnp.float32)

    @pl.when(j == pl.num_programs(0) - 1)
    def _():
        def pick(i, carry):
            picked[pl.ds(i, 1), :] = spectrum[pl.ds(row_ref[i], 1), :]
            return carry

        lax.fori_loop(0, picked.shape[0], pick, 0, unroll=64)
        rest = picked[...] * w_ref[...]
        group = group_ref[...]
        total = None
        for _ in range(3):
            part = rest.astype(jnp.bfloat16)
            rest = rest - part.astype(jnp.float32)
            term = lax.dot_general(group, part, (((1,), (1,)), ((), ())), preferred_element_type=jnp.float32)
            total = term if total is None else total + term
        out_ref[...] = total


def illiquid_pick(ca, t, rim, weight, group, row_index):
    kb, na_loc, lanes = t.shape
    na, depth = ca.shape
    count = row_index.shape[0]
    block = 32
    return pl.pallas_call(
        illiquid_kernel,
        grid_spec=pltpu.PrefetchScalarGridSpec(
            num_scalar_prefetch=1,
            grid=(kb // block,),
            in_specs=[
                pl.BlockSpec((na, depth), lambda j, *_: (0, 0)),
                pl.BlockSpec((block, na_loc, lanes), lambda j, *_: (j, 0, 0)),
                pl.BlockSpec((block, 2, lanes), lambda j, *_: (j, 0, 0)),
                pl.BlockSpec((count, lanes), lambda j, *_: (0, 0)),
                pl.BlockSpec(group.shape, lambda j, *_: (0, 0)),
            ],
            out_specs=pl.BlockSpec((group.shape[0], count), lambda j, *_: (0, 0)),
            scratch_shapes=[pltpu.VMEM((kb * na, lanes), jnp.float32), pltpu.VMEM((count, lanes), jnp.float32)],
        ),
        out_shape=jax.ShapeDtypeStruct((group.shape[0], count), jnp.float32),
        compiler_params=pltpu.CompilerParams(vmem_limit_bytes=60 * 1024 * 1024),
    )(row_index, ca, t, rim, weight, group)


def edges(values, axis, dim):
    count = lax.axis_size(axis)
    pos = lax.axis_index(axis)
    ends = count - 1
    head = lax.index_in_dim(values, 0, axis=dim, keepdims=False)
    tail = lax.index_in_dim(values, values.shape[dim] - 1, axis=dim, keepdims=False)
    below = lax.ppermute(tail, axis, [(i, (i + 1) % count) for i in range(ends)])
    above = lax.ppermute(head, axis, [((i + 1) % count, i) for i in range(ends)])
    lower = jnp.where(pos == 0, head, below).astype(jnp.float32)
    upper = jnp.where(pos == ends, tail, above).astype(jnp.float32)
    return lower, upper


def body(
    values_in,
    shock_load,
    price_field,
    rate_liquid,
    rate_illiquid,
    mask_liquid,
    mask_illiquid,
    jump_inverse,
    coef_liquid,
    coef_illiquid,
    coef_income,
    owner,
):
    high = lax.Precision.HIGH
    columns, nz_loc, na_loc, _ = values_in.shape
    wide_pos = lax.axis_index("wide")
    inc_pos = lax.axis_index("inc")
    head = values_in[:, :, 0, :].astype(jnp.float32)
    tail = values_in[:, :, na_loc - 1, :].astype(jnp.float32)
    lower, upper = edges(values_in, "wide", 2)
    table_b = cosine_constant(NB)[:KBLOW]
    liquid_part = liquid_step(
        shock_load, values_in, head, tail, rate_liquid, rate_illiquid, price_field,
        mask_liquid, mask_illiquid, jnp.asarray(table_b.T),
    )
    rim = jnp.stack(
        [
            jnp.where(mask_illiquid[:, 0, :] == 0, rate_illiquid[:, 0, :] * (lower - head), 0.0),
            jnp.where(mask_illiquid[:, na_loc - 1, :] != 0, rate_illiquid[:, na_loc - 1, :] * (upper - tail), 0.0),
        ],
        axis=2,
    )
    rim = jnp.einsum("kb,czeb->czek", jnp.asarray(table_b), rim, precision=high)
    rim = jnp.transpose(rim, (3, 2, 0, 1)).reshape(KBLOW, 2, columns * nz_loc)
    liquid_part = jnp.transpose(liquid_part, (3, 2, 0, 1)).reshape(KBLOW, na_loc, columns * nz_loc)
    table_a = lax.dynamic_slice_in_dim(jnp.asarray(stacked_constant(NA)), wide_pos * na_loc, na_loc, axis=2)
    table_a = table_a.reshape(NA, 3 * na_loc)
    folded = jnp.dot(jnp.asarray(cosine_constant(NZ)), jump_inverse, precision=lax.Precision.HIGHEST)
    folded = lax.dynamic_slice_in_dim(folded, inc_pos * nz_loc, nz_loc, axis=1)
    pick_z = (coef_income[:, None] == jnp.arange(NZ, dtype=jnp.int32)[None, :]).astype(jnp.float32)
    weight = jnp.tile(jnp.dot(pick_z, folded, precision=lax.Precision.HIGHEST), (1, columns))
    lanes = columns * nz_loc
    group = (jnp.arange(lanes)[None, :] // nz_loc == jnp.arange(columns)[:, None]).astype(jnp.bfloat16)
    partial = illiquid_pick(
        table_a, liquid_part, rim, weight, group,
        jnp.clip(coef_liquid, 0, KBLOW - 1) * NA + jnp.clip(coef_illiquid, 0, NA - 1),
    )
    kept = all_sum(partial, ("inc", "wide"))
    owners = lax.axis_size(("wide", "inc"))
    count = owner.shape[0]
    capacity = 2 * count // owners
    me = lax.axis_index(("wide", "inc"))
    seen = jnp.cumsum((owner == me).astype(jnp.int32))
    slots = jnp.arange(1, capacity + 1, dtype=jnp.int32)
    mine = jnp.sum((seen[None, :] < slots[:, None]).astype(jnp.int32), axis=1)
    gathered = jnp.take(kept, jnp.minimum(mine, count - 1), axis=1)
    return jnp.where((mine < count)[None, :], gathered, jnp.float32(0.0))


def all_sum(x, axes):
    for axis in axes:
        count = lax.axis_size(axis)
        step = 1
        while step < count:
            x = x + lax.ppermute(x, axis, [(i, i ^ step) for i in range(count)])
            step *= 2
    return x


def solution(mesh):
    placed = (
        P(("grp", "col"), "inc", "wide", None),
        P(("grp", "col")),
        P(("grp", "inc"), "wide", None),
        P(("grp", "inc"), "wide", None),
        P(("grp", "inc"), "wide", None),
        P(("grp", "inc"), "wide", None),
        P(("grp", "inc"), "wide", None),
        P("grp", None),
        P(),
        P(),
        P(),
        P(),
    )
    return jax.shard_map(
        body,
        mesh=mesh,
        in_specs=placed,
        out_specs=P(("grp", "col"), ("wide", "inc")),
        check_vma=False,
    )
```
